32 devices in a mesh: beam: 8 (over z, y), cross: 4 (over x, core).
Axes of the slice: x: 2, y: 2, z: 4, core: 2. Of those that a mesh axis runs over, the one named last changes fastest.
Arguments:
- xenon_spin_polarization: float32 [64, 128, 128], P('beam', 'cross'), may hold values from 0 to 0.6
- heat_ratio: float32 [64, 128, 128], P('beam', 'cross'), may hold values from 1 to 1.12
- rubidium_polarization_old: float32 [64, 128, 128], P('beam', 'cross'), may hold values from 0.1 to 0.9
- earlier_spectral_power: bfloat16 [64, 64, 128, 128], P(None, 'beam', 'cross'), may hold values from 0 to 2
- entry_spectral_power: float32 [64, 128, 128], P(None, 'cross'), may hold values from 0.3 to 3
- spectral_attenuation_section: float32 [64], replicated, may hold values from 0.3 to 20
- flow_rate_forward: float32 [128, 128], P('cross'), may hold values from 0.3 to 1
- solid_pillar_flags: int32 [64, 128], P('beam', 'cross'), may hold values from 0 to 1, as said below
Outputs:
- spectral_power: bfloat16 [64, 64, 128, 128], P(None, 'beam', 'cross')
- xenon_next: float32 [64, 128, 128], P('beam', 'cross')
- temperature_next: float32 [64, 128, 128], P('beam', 'cross')
- rubidium_polarization_new: float32 [64, 128, 128], P('beam', 'cross')
The draws below stay inside these ranges and needn't reach their ends.
Inputs may be any that keep to these rules, and one draw needn't show every extreme that they name: `solid_pillar_flags`: constant on aligned tiles of 4 x 4 grid columns; at least one tile is glass.
All inputs are finite; a program needn't handle non-finite values.
Results may differ from the reference program's by a relative error of at most 0.001.
Values sent between devices are 32-bit elements; how exact they have to be, the bound alone decides.
No kernel may reach another device: no remote copies, remote signals or barrier semaphores. Data moves between devices by JAX's collectives and lax.ppermute only.
A program may use at most 128 MiB of HBM per device.

```python
import math
import jax
import jax.numpy as jnp
from jax import lax

L = 64
HEIGHT_SITES = 128
SUBSTEPS = 2
TILE = 4
LASER_AXIS_SITES = 64
TRANSVERSE_SITES = 128


def draw_solid_pillar_flags(key, part):
    tile_rows = LASER_AXIS_SITES // TILE
    tile_columns = TRANSVERSE_SITES // TILE
    tile_draw = jax.random.randint(jax.random.fold_in(key, 11), (tile_rows, tile_columns), 0, 16)
    chosen = jax.random.randint(jax.random.fold_in(key, 12), (), 0, tile_rows * tile_columns)
    position = jnp.arange(tile_rows * tile_columns).reshape(tile_rows, tile_columns)
    flagged = jnp.where((tile_draw == 0) | (position == chosen), 1, 0).astype(jnp.int32)
    return jnp.repeat(jnp.repeat(flagged, TILE, axis=0), TILE, axis=1)


def shard_levels(key, extent, split, low, largest):
    factor_of = 1.0
    for dim, parts in split:
        heights = jax.random.uniform(jax.random.fold_in(jax.random.fold_in(key, 6), dim), (parts,), jnp.float32, low / len(split), largest / len(split))
        factor_of = factor_of * jnp.repeat(jnp.exp(heights), extent[dim] // parts).reshape((-1,) + (1,) * (len(extent) - 1 - dim))
    return factor_of


def setup_inputs(seed: int = 0) -> dict:
    splits = jax.random.split(jax.random.key(seed), 9)
    return {
        "xenon_spin_polarization": jnp.clip(0.6 * jax.random.uniform(splits[0], (LASER_AXIS_SITES, TRANSVERSE_SITES, HEIGHT_SITES), jnp.float32) ** shard_levels(splits[0], (LASER_AXIS_SITES, TRANSVERSE_SITES, HEIGHT_SITES), ((0, 8), (1, 4)), -0.2, 0.2), 0.0, 0.6),
        "heat_ratio": jnp.clip(1.0 + 0.120000005 * jax.random.uniform(splits[1], (LASER_AXIS_SITES, TRANSVERSE_SITES, HEIGHT_SITES), jnp.float32) ** shard_levels(splits[1], (LASER_AXIS_SITES, TRANSVERSE_SITES, HEIGHT_SITES), ((0, 8), (1, 4)), -0.2, 0.2), 1.0, 1.12),
        "rubidium_polarization_old": jnp.clip(0.1 + 0.79999997 * jax.random.uniform(splits[2], (LASER_AXIS_SITES, TRANSVERSE_SITES, HEIGHT_SITES), jnp.float32) ** shard_levels(splits[2], (LASER_AXIS_SITES, TRANSVERSE_SITES, HEIGHT_SITES), ((0, 8), (1, 4)), -0.2, 0.2), 0.1, 0.9),
        "earlier_spectral_power": jnp.clip(2.0 * jax.random.uniform(splits[3], (L, LASER_AXIS_SITES, TRANSVERSE_SITES, HEIGHT_SITES), jnp.float32) ** shard_levels(splits[3], (L, LASER_AXIS_SITES, TRANSVERSE_SITES, HEIGHT_SITES), ((1, 8), (2, 4)), -0.2, 0.2), 0.0, 2.0).astype(jnp.bfloat16),
        "entry_spectral_power": jnp.clip(jnp.exp(math.log(3.0) - 2.3025851 * jax.random.uniform(splits[4], (L, TRANSVERSE_SITES, HEIGHT_SITES), jnp.float32) ** shard_levels(splits[4], (L, TRANSVERSE_SITES, HEIGHT_SITES), ((1, 4),), -0.2, 0.2)), 0.3, 3.0),
        "spectral_attenuation_section": jnp.clip(jnp.exp(jax.random.uniform(splits[5], (L,), jnp.float32, math.log(0.3), math.log(20.0))), 0.3, 20.0),
        "flow_rate_forward": jnp.clip(0.3 + 0.7 * jax.random.uniform(splits[6], (TRANSVERSE_SITES, HEIGHT_SITES), jnp.float32) ** shard_levels(splits[6], (TRANSVERSE_SITES, HEIGHT_SITES), ((0, 4),), -0.2, 0.2), 0.3, 1.0),
        "solid_pillar_flags": draw_solid_pillar_flags(jax.random.fold_in(splits[8], 71), 0),
    }


rubidium_amount_slope = 23.25
rubidium_amount_center = 0.95
absorb_scale = 1.0
glass_depth = 0.07
saturation = 1.0
pump_scale = 0.015625
spin_decay = 0.5
exchange_rate = 0.05
xenon_relax = 0.02
heat_gain = 0.05
cooling = 0.02
xenon_diffusion = 0.09
conduction = 0.09
flow_scale = 0.2
boundary_kelvin = 1.0
neighbor_offsets = ((1, 0, 0), (-1, 0, 0), (0, 1, 0), (0, -1, 0), (0, 0, 1), (0, 0, -1))


def window(source, step_beam, step_cross, step_depth):
    return source[..., 1 + step_beam: source.shape[-3] - 1 + step_beam, 1 + step_cross: source.shape[-2] - 1 + step_cross, 1 + step_depth: source.shape[-1] - 1 + step_depth]


def advance(bordered, rubidium_number_amount, spin_ratio, heating, drift_speed, fluid_occupied_sites):
    center = window(bordered, 0, 0, 0)
    complete_heat_ratio = bordered[1] + boundary_kelvin
    coefficients = jnp.stack([xenon_diffusion * complete_heat_ratio ** 1.5, conduction * complete_heat_ratio ** 0.7])
    coeff_center = window(coefficients, 0, 0, 0)
    diffused = jnp.zeros_like(center)
    for step_beam, step_cross, step_depth in neighbor_offsets:
        neighbor = window(bordered, step_beam, step_cross, step_depth)
        face_coeff = 0.5 * (coeff_center + window(coefficients, step_beam, step_cross, step_depth))
        diffused = diffused + face_coeff * (neighbor - center)
    upstream = window(bordered, -1, 0, 0)
    transport = diffused - drift_speed * (center - upstream)
    xenon_new = center[0] + transport[0] + exchange_rate * rubidium_number_amount * (spin_ratio - center[0]) - xenon_relax * center[0]
    deviation = center[1] + transport[1] + heat_gain * heating - cooling * center[1]
    return jnp.stack([xenon_new * fluid_occupied_sites, deviation * fluid_occupied_sites])


def reference(xenon_spin_polarization, heat_ratio, rubidium_polarization_old, earlier_spectral_power, entry_spectral_power, spectral_attenuation_section, flow_rate_forward, solid_pillar_flags):
    glass_cells = solid_pillar_flags.astype(jnp.float32)[:, :, None]
    fluid_occupied_sites = 1.0 - glass_cells
    rubidium_number_amount = fluid_occupied_sites * jnp.exp(rubidium_amount_slope * (rubidium_amount_center - 1.0 / heat_ratio))
    absorber = (absorb_scale / LASER_AXIS_SITES) * rubidium_number_amount * (1.0 - rubidium_polarization_old)
    glass_term = glass_depth * glass_cells

    def one_line(sums_so_far, inputs):
        pumping, heating = sums_so_far
        earlier_light, entrance, cross_section = inputs
        weight = cross_section / (1.0 + earlier_light.astype(jnp.float32) / saturation)
        optical_depth = absorber * weight + glass_term
        column = jnp.concatenate([jnp.zeros_like(optical_depth[:1]), jnp.cumsum(optical_depth[:-1], axis=0)], axis=0)
        radiance = entrance[None] * jnp.exp(-column)
        pumping = pumping + weight * radiance
        heating = heating + radiance * (1.0 - jnp.exp(-optical_depth))
        return (pumping, heating), radiance.astype(jnp.bfloat16)

    blank_lattice = jnp.zeros(heat_ratio.shape, jnp.float32)
    (pumping, heating), spectral_power = lax.scan(one_line, (blank_lattice, blank_lattice), (earlier_spectral_power, entry_spectral_power, spectral_attenuation_section))
    pumping = pump_scale * pumping
    spin_ratio = pumping / (pumping + spin_decay * (1.0 + rubidium_number_amount))
    rubidium_polarization_new = fluid_occupied_sites * spin_ratio
    drift_speed = flow_scale * flow_rate_forward
    physical_quantities = jnp.stack([xenon_spin_polarization, heat_ratio - boundary_kelvin])
    for substep in range(SUBSTEPS):
        bordered = jnp.pad(physical_quantities, ((0, 0), (1, 1), (1, 1), (1, 1)))
        physical_quantities = advance(bordered, rubidium_number_amount, spin_ratio, heating, drift_speed, fluid_occupied_sites)
    return spectral_power, physical_quantities[0], physical_quantities[1] + boundary_kelvin, rubidium_polarization_new
```

```python
import jax
import jax.numpy as jnp
from jax import lax
from jax.sharding import PartitionSpec as P

SUBSTEPS = 2


rubidium_amount_slope = 23.25
rubidium_amount_center = 0.95
absorb_scale = 1.0
glass_depth = 0.07
saturation = 1.0
pump_scale = 0.015625
spin_decay = 0.5
exchange_rate = 0.05
xenon_relax = 0.02
heat_gain = 0.05
cooling = 0.02
xenon_diffusion = 0.09
conduction = 0.09
flow_scale = 0.2
boundary_kelvin = 1.0
neighbor_offsets = ((1, 0, 0), (-1, 0, 0), (0, 1, 0), (0, -1, 0), (0, 0, 1), (0, 0, -1))


def shifted(block, axis, shift):
    count = lax.axis_size(axis)
    if shift > 0:
        pairs = [(i, i + shift) for i in range(count - shift)]
    else:
        pairs = [(i - shift, i) for i in range(count + shift)]
    return lax.ppermute(block, axis, pairs)


def bordered_fields(block):
    _, rows, columns, _ = block.shape
    low_beam = shifted(block[:, rows - 1 :], "beam", 1)
    high_beam = shifted(block[:, :1], "beam", -1)
    low_cross = shifted(block[:, :, columns - 1 :], "cross", 1)
    high_cross = shifted(block[:, :, :1], "cross", -1)
    middle = jnp.concatenate([low_cross, block, high_cross], axis=2)
    zeros = jnp.zeros_like(low_beam[:, :, :1])
    low_beam = jnp.concatenate([zeros, low_beam, zeros], axis=2)
    high_beam = jnp.concatenate([zeros, high_beam, zeros], axis=2)
    bordered = jnp.concatenate([low_beam, middle, high_beam], axis=1)
    return jnp.pad(bordered, ((0, 0), (0, 0), (0, 0), (1, 1)))


def exclusive_scan(totals, axis):
    count = lax.axis_size(axis)
    if count == 1:
        return jnp.zeros_like(totals)
    before = shifted(totals, axis, 1)
    through = totals + before
    step = 2
    while step < count:
        arrived = shifted(through, axis, step)
        before = before + arrived
        step *= 2
        if step < count:
            through = through + arrived
    return before


def window(source, step_beam, step_cross, step_depth):
    return source[
        ...,
        1 + step_beam : source.shape[-3] - 1 + step_beam,
        1 + step_cross : source.shape[-2] - 1 + step_cross,
        1 + step_depth : source.shape[-1] - 1 + step_depth,
    ]


def advance(
    bordered, rubidium_number_amount, spin_ratio, heating, drift_speed, fluid_occupied_sites
):
    center = window(bordered, 0, 0, 0)
    complete_heat_ratio = bordered[1] + boundary_kelvin
    coefficients = jnp.stack(
        [xenon_diffusion * complete_heat_ratio**1.5, conduction * complete_heat_ratio**0.7]
    )
    coeff_center = window(coefficients, 0, 0, 0)
    diffused = jnp.zeros_like(center)
    for step_beam, step_cross, step_depth in neighbor_offsets:
        neighbor = window(bordered, step_beam, step_cross, step_depth)
        face_coeff = 0.5 * (coeff_center + window(coefficients, step_beam, step_cross, step_depth))
        diffused = diffused + face_coeff * (neighbor - center)
    upstream = window(bordered, -1, 0, 0)
    transport = diffused - drift_speed * (center - upstream)
    xenon_new = (
        center[0]
        + transport[0]
        + exchange_rate * rubidium_number_amount * (spin_ratio - center[0])
        - xenon_relax * center[0]
    )
    deviation = center[1] + transport[1] + heat_gain * heating - cooling * center[1]
    return jnp.stack([xenon_new * fluid_occupied_sites, deviation * fluid_occupied_sites])


def local(
    xenon_spin_polarization,
    heat_ratio,
    rubidium_polarization_old,
    earlier_spectral_power,
    entry_spectral_power,
    spectral_attenuation_section,
    flow_rate_forward,
    solid_pillar_flags,
):
    rows = earlier_spectral_power.shape[1]
    total_rows = rows * lax.axis_size("beam")
    physical_quantities = jnp.stack([xenon_spin_polarization, heat_ratio - boundary_kelvin])
    first_border = bordered_fields(physical_quantities)
    glass_cells = solid_pillar_flags.astype(jnp.float32)[:, :, None]
    fluid_occupied_sites = 1.0 - glass_cells
    rubidium_number_amount = fluid_occupied_sites * jnp.exp(
        rubidium_amount_slope * (rubidium_amount_center - 1.0 / heat_ratio)
    )
    absorber = (
        absorb_scale / total_rows * rubidium_number_amount * (1.0 - rubidium_polarization_old)
    )
    glass_term = glass_depth * glass_cells
    weight = spectral_attenuation_section[:, None, None, None] / (
        1.0 + earlier_spectral_power.astype(jnp.float32) / saturation
    )
    optical_depth = absorber[None] * weight + glass_term[None]
    running = jnp.zeros_like(optical_depth[:, 0])
    prefix = []
    for row in range(rows):
        prefix.append(running)
        running = running + optical_depth[:, row]
    local_column = jnp.stack(prefix, axis=1)
    column = exclusive_scan(running, "beam")[:, None] + local_column
    radiance = entry_spectral_power[:, None] * jnp.exp(-column)
    spectral_power = radiance.astype(jnp.bfloat16)
    pumping = pump_scale * jnp.sum(weight * radiance, axis=0)
    heating = jnp.sum(radiance * (1.0 - jnp.exp(-optical_depth)), axis=0)
    spin_ratio = pumping / (pumping + spin_decay * (1.0 + rubidium_number_amount))
    rubidium_polarization_new = fluid_occupied_sites * spin_ratio
    drift_speed = flow_scale * flow_rate_forward
    for substep in range(SUBSTEPS):
        bordered = first_border if substep == 0 else bordered_fields(physical_quantities)
        physical_quantities = advance(
            bordered, rubidium_number_amount, spin_ratio, heating, drift_speed, fluid_occupied_sites
        )
    return (
        spectral_power,
        physical_quantities[0],
        physical_quantities[1] + boundary_kelvin,
        rubidium_polarization_new,
    )


def solution(mesh):
    in_specs = (
        P("beam", "cross", None),
        P("beam", "cross", None),
        P("beam", "cross", None),
        P(None, "beam", "cross", None),
        P(None, "cross", None),
        P(),
        P("cross", None),
        P("beam", "cross"),
    )
    out_specs = (
        P(None, "beam", "cross", None),
        P("beam", "cross", None),
        P("beam", "cross", None),
        P("beam", "cross", None),
    )
    return jax.shard_map(local, mesh=mesh, in_specs=in_specs, out_specs=out_specs, check_vma=False)
```

```python
import jax
import jax.numpy as jnp
from jax import lax
from jax.sharding import PartitionSpec as P

SUBSTEPS = 2


rubidium_amount_slope = 23.25
rubidium_amount_center = 0.95
absorb_scale = 1.0
glass_depth = 0.07
saturation = 1.0
pump_scale = 0.015625
spin_decay = 0.5
exchange_rate = 0.05
xenon_relax = 0.02
heat_gain = 0.05
cooling = 0.02
xenon_diffusion = 0.09
conduction = 0.09
flow_scale = 0.2
boundary_kelvin = 1.0
neighbor_offsets = ((1, 0, 0), (-1, 0, 0), (0, 1, 0), (0, -1, 0), (0, 0, 1), (0, 0, -1))


def shifted(block, axis, shift):
    count = lax.axis_size(axis)
    if shift > 0:
        pairs = [(i, i + shift) for i in range(count - shift)]
    else:
        pairs = [(i - shift, i) for i in range(count + shift)]
    return lax.ppermute(block, axis, pairs)


def bordered_fields(block):
    _, rows, columns, _ = block.shape
    low_beam = shifted(block[:, rows - 1 :], "beam", 1)
    high_beam = shifted(block[:, :1], "beam", -1)
    low_cross = shifted(block[:, :, columns - 1 :], "cross", 1)
    high_cross = shifted(block[:, :, :1], "cross", -1)
    middle = jnp.concatenate([low_cross, block, high_cross], axis=2)
    zeros = jnp.zeros_like(low_beam[:, :, :1])
    low_beam = jnp.concatenate([zeros, low_beam, zeros], axis=2)
    high_beam = jnp.concatenate([zeros, high_beam, zeros], axis=2)
    bordered = jnp.concatenate([low_beam, middle, high_beam], axis=1)
    return jnp.pad(bordered, ((0, 0), (0, 0), (0, 0), (1, 1)))


def exclusive_scan(totals, axis, stride=1):
    count = lax.axis_size(axis) // stride
    if count == 1:
        return jnp.zeros_like(totals)
    before = shifted(totals, axis, stride)
    through = totals + before
    step = 2
    while step < count:
        arrived = shifted(through, axis, step * stride)
        before = before + arrived
        step *= 2
        if step < count:
            through = through + arrived
    return before


def paired_scan(totals, axis):
    count = lax.axis_size(axis)
    half = totals.shape[0] // 2
    if count % 2 or totals.shape[0] % 2 or count == 2:
        return exclusive_scan(totals, axis)
    is_low = lax.axis_index(axis) % 2 == 0
    first, second = totals[:half], totals[half:]
    mine = jnp.where(is_low, first, second)
    swap = [(i, i ^ 1) for i in range(count)]
    got = lax.ppermute(jnp.where(is_low, second, first), axis, swap)
    before = exclusive_scan(mine + got, axis, stride=2)
    back = lax.ppermute(jnp.where(is_low, before + mine, before), axis, swap)
    low_result = jnp.concatenate([before, back])
    high_result = jnp.concatenate([back, before + got])
    return jnp.where(is_low, low_result, high_result)


def window(source, step_beam, step_cross, step_depth):
    return source[
        ...,
        1 + step_beam : source.shape[-3] - 1 + step_beam,
        1 + step_cross : source.shape[-2] - 1 + step_cross,
        1 + step_depth : source.shape[-1] - 1 + step_depth,
    ]


def advance(
    bordered, rubidium_number_amount, spin_ratio, heating, drift_speed, fluid_occupied_sites
):
    center = window(bordered, 0, 0, 0)
    complete_heat_ratio = bordered[1] + boundary_kelvin
    coefficients = jnp.stack(
        [xenon_diffusion * complete_heat_ratio**1.5, conduction * complete_heat_ratio**0.7]
    )
    coeff_center = window(coefficients, 0, 0, 0)
    diffused = jnp.zeros_like(center)
    for step_beam, step_cross, step_depth in neighbor_offsets:
        neighbor = window(bordered, step_beam, step_cross, step_depth)
        face_coeff = 0.5 * (coeff_center + window(coefficients, step_beam, step_cross, step_depth))
        diffused = diffused + face_coeff * (neighbor - center)
    upstream = window(bordered, -1, 0, 0)
    transport = diffused - drift_speed * (center - upstream)
    xenon_new = (
        center[0]
        + transport[0]
        + exchange_rate * rubidium_number_amount * (spin_ratio - center[0])
        - xenon_relax * center[0]
    )
    deviation = center[1] + transport[1] + heat_gain * heating - cooling * center[1]
    return jnp.stack([xenon_new * fluid_occupied_sites, deviation * fluid_occupied_sites])


def local(
    xenon_spin_polarization,
    heat_ratio,
    rubidium_polarization_old,
    earlier_spectral_power,
    entry_spectral_power,
    spectral_attenuation_section,
    flow_rate_forward,
    solid_pillar_flags,
):
    rows = earlier_spectral_power.shape[1]
    total_rows = rows * lax.axis_size("beam")
    physical_quantities = jnp.stack([xenon_spin_polarization, heat_ratio - boundary_kelvin])
    first_border = bordered_fields(physical_quantities)
    glass_cells = solid_pillar_flags.astype(jnp.float32)[:, :, None]
    fluid_occupied_sites = 1.0 - glass_cells
    rubidium_number_amount = fluid_occupied_sites * jnp.exp(
        rubidium_amount_slope * (rubidium_amount_center - 1.0 / heat_ratio)
    )
    absorber = (
        absorb_scale / total_rows * rubidium_number_amount * (1.0 - rubidium_polarization_old)
    )
    glass_term = glass_depth * glass_cells
    weight = spectral_attenuation_section[:, None, None, None] / (
        1.0 + earlier_spectral_power.astype(jnp.float32) / saturation
    )
    optical_depth = absorber[None] * weight + glass_term[None]
    running = jnp.zeros_like(optical_depth[:, 0])
    prefix = []
    for row in range(rows):
        prefix.append(running)
        running = running + optical_depth[:, row]
    local_column = jnp.stack(prefix, axis=1)
    column = paired_scan(running, "beam")[:, None] + local_column
    radiance = entry_spectral_power[:, None] * jnp.exp(-column)
    spectral_power = radiance.astype(jnp.bfloat16)
    pumping = pump_scale * jnp.sum(weight * radiance, axis=0)
    heating = jnp.sum(radiance * (1.0 - jnp.exp(-optical_depth)), axis=0)
    spin_ratio = pumping / (pumping + spin_decay * (1.0 + rubidium_number_amount))
    rubidium_polarization_new = fluid_occupied_sites * spin_ratio
    drift_speed = flow_scale * flow_rate_forward
    for substep in range(SUBSTEPS):
        bordered = first_border if substep == 0 else bordered_fields(physical_quantities)
        physical_quantities = advance(
            bordered, rubidium_number_amount, spin_ratio, heating, drift_speed, fluid_occupied_sites
        )
    return (
        spectral_power,
        physical_quantities[0],
        physical_quantities[1] + boundary_kelvin,
        rubidium_polarization_new,
    )


def solution(mesh):
    in_specs = (
        P("beam", "cross", None),
        P("beam", "cross", None),
        P("beam", "cross", None),
        P(None, "beam", "cross", None),
        P(None, "cross", None),
        P(),
        P("cross", None),
        P("beam", "cross"),
    )
    out_specs = (
        P(None, "beam", "cross", None),
        P("beam", "cross", None),
        P("beam", "cross", None),
        P("beam", "cross", None),
    )
    return jax.shard_map(local, mesh=mesh, in_specs=in_specs, out_specs=out_specs, check_vma=False)
```

```python
import jax
import jax.numpy as jnp
from jax import lax
from jax.sharding import PartitionSpec as P

SUBSTEPS = 2


rubidium_amount_slope = 23.25
rubidium_amount_center = 0.95
absorb_scale = 1.0
glass_depth = 0.07
saturation = 1.0
pump_scale = 0.015625
spin_decay = 0.5
exchange_rate = 0.05
xenon_relax = 0.02
heat_gain = 0.05
cooling = 0.02
xenon_diffusion = 0.09
conduction = 0.09
flow_scale = 0.2
boundary_kelvin = 1.0
neighbor_offsets = ((1, 0, 0), (-1, 0, 0), (0, 1, 0), (0, -1, 0), (0, 0, 1), (0, 0, -1))


def shifted(block, axis, shift):
    count = lax.axis_size(axis)
    if shift > 0:
        pairs = [(i, i + shift) for i in range(count - shift)]
    else:
        pairs = [(i - shift, i) for i in range(count + shift)]
    return lax.ppermute(block, axis, pairs)


def bordered_fields(block):
    _, rows, columns, _ = block.shape
    low_beam = shifted(block[:, rows - 1 :], "beam", 1)
    high_beam = shifted(block[:, :1], "beam", -1)
    low_cross = shifted(block[:, :, columns - 1 :], "cross", 1)
    high_cross = shifted(block[:, :, :1], "cross", -1)
    middle = jnp.concatenate([low_cross, block, high_cross], axis=2)
    zeros = jnp.zeros_like(low_beam[:, :, :1])
    low_beam = jnp.concatenate([zeros, low_beam, zeros], axis=2)
    high_beam = jnp.concatenate([zeros, high_beam, zeros], axis=2)
    bordered = jnp.concatenate([low_beam, middle, high_beam], axis=1)
    return jnp.pad(bordered, ((0, 0), (0, 0), (0, 0), (1, 1)))


def exclusive_scan(totals, axis, stride=1):
    count = lax.axis_size(axis) // stride
    if count == 1:
        return jnp.zeros_like(totals)
    before = shifted(totals, axis, stride)
    through = totals + before
    step = 2
    while step < count:
        arrived = shifted(through, axis, step * stride)
        before = before + arrived
        step *= 2
        if step < count:
            through = through + arrived
    return before


def paired_scan(totals, axis):
    count = lax.axis_size(axis)
    half = totals.shape[0] // 2
    if count % 2 or totals.shape[0] % 2 or count == 2:
        return exclusive_scan(totals, axis)
    is_low = lax.axis_index(axis) % 2 == 0
    first, second = totals[:half], totals[half:]
    mine = jnp.where(is_low, first, second)
    swap = [(i, i ^ 1) for i in range(count)]
    got = lax.ppermute(jnp.where(is_low, second, first), axis, swap)
    before = exclusive_scan(mine + got, axis, stride=2)
    back = lax.ppermute(jnp.where(is_low, before + mine, before), axis, swap)
    low_result = jnp.concatenate([before, back])
    high_result = jnp.concatenate([back, before + got])
    return jnp.where(is_low, low_result, high_result)


def window(source, step_beam, step_cross, step_depth):
    return source[
        ...,
        1 + step_beam : source.shape[-3] - 1 + step_beam,
        1 + step_cross : source.shape[-2] - 1 + step_cross,
        1 + step_depth : source.shape[-1] - 1 + step_depth,
    ]


def advance(
    bordered, rubidium_number_amount, spin_ratio, heating, drift_speed, fluid_occupied_sites
):
    center = window(bordered, 0, 0, 0)
    complete_heat_ratio = bordered[1] + boundary_kelvin
    coefficients = jnp.stack(
        [xenon_diffusion * complete_heat_ratio**1.5, conduction * complete_heat_ratio**0.7]
    )
    coeff_center = window(coefficients, 0, 0, 0)
    diffused = jnp.zeros_like(center)
    for step_beam, step_cross, step_depth in neighbor_offsets:
        neighbor = window(bordered, step_beam, step_cross, step_depth)
        face_coeff = 0.5 * (coeff_center + window(coefficients, step_beam, step_cross, step_depth))
        diffused = diffused + face_coeff * (neighbor - center)
    upstream = window(bordered, -1, 0, 0)
    transport = diffused - drift_speed * (center - upstream)
    xenon_new = (
        center[0]
        + transport[0]
        + exchange_rate * rubidium_number_amount * (spin_ratio - center[0])
        - xenon_relax * center[0]
    )
    deviation = center[1] + transport[1] + heat_gain * heating - cooling * center[1]
    return jnp.stack([xenon_new * fluid_occupied_sites, deviation * fluid_occupied_sites])


def local(
    xenon_spin_polarization,
    heat_ratio,
    rubidium_polarization_old,
    earlier_spectral_power,
    entry_spectral_power,
    spectral_attenuation_section,
    flow_rate_forward,
    solid_pillar_flags,
):
    rows = earlier_spectral_power.shape[1]
    total_rows = rows * lax.axis_size("beam")
    physical_quantities = jnp.stack([xenon_spin_polarization, heat_ratio - boundary_kelvin])
    first_border = bordered_fields(physical_quantities)
    glass_cells = solid_pillar_flags.astype(jnp.float32)[:, :, None]
    fluid_occupied_sites = 1.0 - glass_cells
    rubidium_number_amount = fluid_occupied_sites * jnp.exp(
        rubidium_amount_slope * (rubidium_amount_center - 1.0 / heat_ratio)
    )
    absorber = (
        absorb_scale / total_rows * rubidium_number_amount * (1.0 - rubidium_polarization_old)
    )
    glass_term = glass_depth * glass_cells
    weight = spectral_attenuation_section[:, None, None, None] / (
        1.0 + earlier_spectral_power.astype(jnp.float32) / saturation
    )
    optical_depth = absorber[None] * weight + glass_term[None]
    totals = jnp.sum(optical_depth, axis=1)
    local_column = jnp.pad(
        jnp.cumsum(optical_depth[:, : rows - 1], axis=1), ((0, 0), (1, 0), (0, 0), (0, 0))
    )
    column = paired_scan(totals, "beam")[:, None] + local_column
    radiance = entry_spectral_power[:, None] * jnp.exp(-column)
    spectral_power = radiance.astype(jnp.bfloat16)
    pumping = pump_scale * jnp.sum(weight * radiance, axis=0)
    heating = jnp.sum(radiance * (1.0 - jnp.exp(-optical_depth)), axis=0)
    spin_ratio = pumping / (pumping + spin_decay * (1.0 + rubidium_number_amount))
    rubidium_polarization_new = fluid_occupied_sites * spin_ratio
    drift_speed = flow_scale * flow_rate_forward
    for substep in range(SUBSTEPS):
        bordered = first_border if substep == 0 else bordered_fields(physical_quantities)
        physical_quantities = advance(
            bordered, rubidium_number_amount, spin_ratio, heating, drift_speed, fluid_occupied_sites
        )
    return (
        spectral_power,
        physical_quantities[0],
        physical_quantities[1] + boundary_kelvin,
        rubidium_polarization_new,
    )


def solution(mesh):
    in_specs = (
        P("beam", "cross", None),
        P("beam", "cross", None),
        P("beam", "cross", None),
        P(None, "beam", "cross", None),
        P(None, "cross", None),
        P(),
        P("cross", None),
        P("beam", "cross"),
    )
    out_specs = (
        P(None, "beam", "cross", None),
        P("beam", "cross", None),
        P("beam", "cross", None),
        P("beam", "cross", None),
    )
    return jax.shard_map(local, mesh=mesh, in_specs=in_specs, out_specs=out_specs, check_vma=False)
```

```python
import jax
import jax.numpy as jnp
from jax import lax
from jax.sharding import PartitionSpec as P

SUBSTEPS = 2


rubidium_amount_slope = 23.25
rubidium_amount_center = 0.95
absorb_scale = 1.0
glass_depth = 0.07
saturation = 1.0
pump_scale = 0.015625
spin_decay = 0.5
exchange_rate = 0.05
xenon_relax = 0.02
heat_gain = 0.05
cooling = 0.02
xenon_diffusion = 0.09
conduction = 0.09
flow_scale = 0.2
boundary_kelvin = 1.0
neighbor_offsets = ((1, 0, 0), (-1, 0, 0), (0, 1, 0), (0, -1, 0), (0, 0, 1), (0, 0, -1))


def shifted(block, axis, shift):
    count = lax.axis_size(axis)
    if shift > 0:
        pairs = [(i, i + shift) for i in range(count - shift)]
    else:
        pairs = [(i - shift, i) for i in range(count + shift)]
    return lax.ppermute(block, axis, pairs)


def bordered_fields(block):
    _, rows, columns, _ = block.shape
    low_beam = shifted(block[:, rows - 1 :], "beam", 1)
    high_beam = shifted(block[:, :1], "beam", -1)
    low_cross = shifted(block[:, :, columns - 1 :], "cross", 1)
    high_cross = shifted(block[:, :, :1], "cross", -1)
    middle = jnp.concatenate([low_cross, block, high_cross], axis=2)
    zeros = jnp.zeros_like(low_beam[:, :, :1])
    low_beam = jnp.concatenate([zeros, low_beam, zeros], axis=2)
    high_beam = jnp.concatenate([zeros, high_beam, zeros], axis=2)
    bordered = jnp.concatenate([low_beam, middle, high_beam], axis=1)
    return jnp.pad(bordered, ((0, 0), (0, 0), (0, 0), (1, 1)))


def exclusive_scan(totals, axis, stride=1):
    count = lax.axis_size(axis) // stride
    if count == 1:
        return jnp.zeros_like(totals)
    before = shifted(totals, axis, stride)
    through = totals + before
    step = 2
    while step < count:
        arrived = shifted(through, axis, step * stride)
        before = before + arrived
        step *= 2
        if step < count:
            through = through + arrived
    return before


def paired_scan(totals, axis, rider):
    count = lax.axis_size(axis)
    half = totals.shape[0] // 2
    if count % 2 or totals.shape[0] % 2 or count == 2:
        return exclusive_scan(totals, axis), rider(None)
    is_low = lax.axis_index(axis) % 2 == 0
    first, second = totals[:half], totals[half:]
    mine = jnp.where(is_low, first, second)
    swap = [(i, i ^ 1) for i in range(count)]
    given = jnp.where(is_low, second, first)
    got = lax.ppermute(given, axis, swap)
    got, carried = lax.optimization_barrier((got, rider(given)))
    before = exclusive_scan(mine + got, axis, stride=2)
    back = lax.ppermute(jnp.where(is_low, before + mine, before), axis, swap)
    low_result = jnp.concatenate([before, back])
    high_result = jnp.concatenate([back, before + got])
    return jnp.where(is_low, low_result, high_result), carried


def window(source, step_beam, step_cross, step_depth):
    return source[
        ...,
        1 + step_beam : source.shape[-3] - 1 + step_beam,
        1 + step_cross : source.shape[-2] - 1 + step_cross,
        1 + step_depth : source.shape[-1] - 1 + step_depth,
    ]


def advance(
    bordered, rubidium_number_amount, spin_ratio, heating, drift_speed, fluid_occupied_sites
):
    center = window(bordered, 0, 0, 0)
    complete_heat_ratio = bordered[1] + boundary_kelvin
    coefficients = jnp.stack(
        [xenon_diffusion * complete_heat_ratio**1.5, conduction * complete_heat_ratio**0.7]
    )
    coeff_center = window(coefficients, 0, 0, 0)
    diffused = jnp.zeros_like(center)
    for step_beam, step_cross, step_depth in neighbor_offsets:
        neighbor = window(bordered, step_beam, step_cross, step_depth)
        face_coeff = 0.5 * (coeff_center + window(coefficients, step_beam, step_cross, step_depth))
        diffused = diffused + face_coeff * (neighbor - center)
    upstream = window(bordered, -1, 0, 0)
    transport = diffused - drift_speed * (center - upstream)
    xenon_new = (
        center[0]
        + transport[0]
        + exchange_rate * rubidium_number_amount * (spin_ratio - center[0])
        - xenon_relax * center[0]
    )
    deviation = center[1] + transport[1] + heat_gain * heating - cooling * center[1]
    return jnp.stack([xenon_new * fluid_occupied_sites, deviation * fluid_occupied_sites])


def local(
    xenon_spin_polarization,
    heat_ratio,
    rubidium_polarization_old,
    earlier_spectral_power,
    entry_spectral_power,
    spectral_attenuation_section,
    flow_rate_forward,
    solid_pillar_flags,
):
    rows = earlier_spectral_power.shape[1]
    total_rows = rows * lax.axis_size("beam")
    physical_quantities = jnp.stack([xenon_spin_polarization, heat_ratio - boundary_kelvin])
    glass_cells = solid_pillar_flags.astype(jnp.float32)[:, :, None]
    fluid_occupied_sites = 1.0 - glass_cells
    rubidium_number_amount = fluid_occupied_sites * jnp.exp(
        rubidium_amount_slope * (rubidium_amount_center - 1.0 / heat_ratio)
    )
    absorber = (
        absorb_scale / total_rows * rubidium_number_amount * (1.0 - rubidium_polarization_old)
    )
    glass_term = glass_depth * glass_cells
    weight = spectral_attenuation_section[:, None, None, None] / (
        1.0 + earlier_spectral_power.astype(jnp.float32) / saturation
    )
    optical_depth = absorber[None] * weight + glass_term[None]
    totals = jnp.sum(optical_depth, axis=1)
    local_column = jnp.pad(
        jnp.cumsum(optical_depth[:, : rows - 1], axis=1), ((0, 0), (1, 0), (0, 0), (0, 0))
    )
    def first_border(after):
        fields = physical_quantities
        if after is not None:
            fields, _ = lax.optimization_barrier((fields, after))
        return bordered_fields(fields)

    prefix, first_bordered = paired_scan(totals, "beam", first_border)
    column = prefix[:, None] + local_column
    radiance = entry_spectral_power[:, None] * jnp.exp(-column)
    spectral_power = radiance.astype(jnp.bfloat16)
    pumping = pump_scale * jnp.sum(weight * radiance, axis=0)
    heating = jnp.sum(radiance * (1.0 - jnp.exp(-optical_depth)), axis=0)
    spin_ratio = pumping / (pumping + spin_decay * (1.0 + rubidium_number_amount))
    rubidium_polarization_new = fluid_occupied_sites * spin_ratio
    drift_speed = flow_scale * flow_rate_forward
    for substep in range(SUBSTEPS):
        bordered = first_bordered if substep == 0 else bordered_fields(physical_quantities)
        physical_quantities = advance(
            bordered, rubidium_number_amount, spin_ratio, heating, drift_speed, fluid_occupied_sites
        )
    return (
        spectral_power,
        physical_quantities[0],
        physical_quantities[1] + boundary_kelvin,
        rubidium_polarization_new,
    )


def solution(mesh):
    in_specs = (
        P("beam", "cross", None),
        P("beam", "cross", None),
        P("beam", "cross", None),
        P(None, "beam", "cross", None),
        P(None, "cross", None),
        P(),
        P("cross", None),
        P("beam", "cross"),
    )
    out_specs = (
        P(None, "beam", "cross", None),
        P("beam", "cross", None),
        P("beam", "cross", None),
        P("beam", "cross", None),
    )
    return jax.shard_map(local, mesh=mesh, in_specs=in_specs, out_specs=out_specs, check_vma=False)
```

```python
import jax
import jax.numpy as jnp
from jax import lax
from jax.sharding import PartitionSpec as P

SUBSTEPS = 2


rubidium_amount_slope = 23.25
rubidium_amount_center = 0.95
absorb_scale = 1.0
glass_depth = 0.07
saturation = 1.0
pump_scale = 0.015625
spin_decay = 0.5
exchange_rate = 0.05
xenon_relax = 0.02
heat_gain = 0.05
cooling = 0.02
xenon_diffusion = 0.09
conduction = 0.09
flow_scale = 0.2
boundary_kelvin = 1.0
neighbor_offsets = ((1, 0, 0), (-1, 0, 0), (0, 1, 0), (0, -1, 0), (0, 0, 1), (0, 0, -1))


def shifted(block, axis, shift):
    count = lax.axis_size(axis)
    if shift > 0:
        pairs = [(i, i + shift) for i in range(count - shift)]
    else:
        pairs = [(i - shift, i) for i in range(count + shift)]
    return lax.ppermute(block, axis, pairs)


def bordered_fields(block):
    _, rows, columns, _ = block.shape
    low_beam = shifted(block[:, rows - 1 :], "beam", 1)
    high_beam = shifted(block[:, :1], "beam", -1)
    low_cross = shifted(block[:, :, columns - 1 :], "cross", 1)
    high_cross = shifted(block[:, :, :1], "cross", -1)
    middle = jnp.concatenate([low_cross, block, high_cross], axis=2)
    zeros = jnp.zeros_like(low_beam[:, :, :1])
    low_beam = jnp.concatenate([zeros, low_beam, zeros], axis=2)
    high_beam = jnp.concatenate([zeros, high_beam, zeros], axis=2)
    bordered = jnp.concatenate([low_beam, middle, high_beam], axis=1)
    return jnp.pad(bordered, ((0, 0), (0, 0), (0, 0), (1, 1)))


def exclusive_scan(totals, axis, stride=1):
    count = lax.axis_size(axis) // stride
    if count == 1:
        return jnp.zeros_like(totals)
    before = shifted(totals, axis, stride)
    through = totals + before
    step = 2
    while step < count:
        arrived = shifted(through, axis, step * stride)
        before = before + arrived
        step *= 2
        if step < count:
            through = through + arrived
    return before


def line_half(block, offset, half):
    return lax.dynamic_slice_in_dim(block, offset, half, axis=0)


def paired_column(depth_of, lines, axis, rider):
    count = lax.axis_size(axis)
    half = lines // 2
    if count % 2 or lines % 2 or count == 2:
        whole = exclusive_scan(jnp.sum(depth_of(0, lines), axis=1), axis)
        return [(0, lines, whole)], rider(None)
    parity = lax.axis_index(axis) % 2
    is_low = parity == 0
    own, other = parity * half, (1 - parity) * half
    given = jnp.sum(depth_of(other, half), axis=1)
    swap = [(i, i ^ 1) for i in range(count)]
    got = lax.ppermute(given, axis, swap)
    got, carried = lax.optimization_barrier((got, rider(given)))
    mine = jnp.sum(depth_of(own, half), axis=1)
    before = exclusive_scan(mine + got, axis, stride=2)
    back = lax.ppermute(jnp.where(is_low, before + mine, before), axis, swap)
    own_prefix = jnp.where(is_low, before, before + got)
    return [(own, half, own_prefix), (other, half, back)], carried


def window(source, step_beam, step_cross, step_depth):
    return source[
        ...,
        1 + step_beam : source.shape[-3] - 1 + step_beam,
        1 + step_cross : source.shape[-2] - 1 + step_cross,
        1 + step_depth : source.shape[-1] - 1 + step_depth,
    ]


def advance(
    bordered, rubidium_number_amount, spin_ratio, heating, drift_speed, fluid_occupied_sites
):
    center = window(bordered, 0, 0, 0)
    complete_heat_ratio = bordered[1] + boundary_kelvin
    coefficients = jnp.stack(
        [xenon_diffusion * complete_heat_ratio**1.5, conduction * complete_heat_ratio**0.7]
    )
    coeff_center = window(coefficients, 0, 0, 0)
    diffused = jnp.zeros_like(center)
    for step_beam, step_cross, step_depth in neighbor_offsets:
        neighbor = window(bordered, step_beam, step_cross, step_depth)
        face_coeff = 0.5 * (coeff_center + window(coefficients, step_beam, step_cross, step_depth))
        diffused = diffused + face_coeff * (neighbor - center)
    upstream = window(bordered, -1, 0, 0)
    transport = diffused - drift_speed * (center - upstream)
    xenon_new = (
        center[0]
        + transport[0]
        + exchange_rate * rubidium_number_amount * (spin_ratio - center[0])
        - xenon_relax * center[0]
    )
    deviation = center[1] + transport[1] + heat_gain * heating - cooling * center[1]
    return jnp.stack([xenon_new * fluid_occupied_sites, deviation * fluid_occupied_sites])


def local(
    xenon_spin_polarization,
    heat_ratio,
    rubidium_polarization_old,
    earlier_spectral_power,
    entry_spectral_power,
    spectral_attenuation_section,
    flow_rate_forward,
    solid_pillar_flags,
):
    rows = earlier_spectral_power.shape[1]
    total_rows = rows * lax.axis_size("beam")
    physical_quantities = jnp.stack([xenon_spin_polarization, heat_ratio - boundary_kelvin])
    glass_cells = solid_pillar_flags.astype(jnp.float32)[:, :, None]
    fluid_occupied_sites = 1.0 - glass_cells
    rubidium_number_amount = fluid_occupied_sites * jnp.exp(
        rubidium_amount_slope * (rubidium_amount_center - 1.0 / heat_ratio)
    )
    absorber = (
        absorb_scale / total_rows * rubidium_number_amount * (1.0 - rubidium_polarization_old)
    )
    glass_term = glass_depth * glass_cells
    lines = earlier_spectral_power.shape[0]

    def depth_of(offset, count):
        weight = line_half(spectral_attenuation_section, offset, count)[:, None, None, None] / (
            1.0 + line_half(earlier_spectral_power, offset, count).astype(jnp.float32) / saturation
        )
        return absorber[None] * weight + glass_term[None], weight

    def first_border(after):
        fields = physical_quantities
        if after is not None:
            fields, _ = lax.optimization_barrier((fields, after))
        return bordered_fields(fields)

    pieces, first_bordered = paired_column(
        lambda offset, count: depth_of(offset, count)[0], lines, "beam", first_border
    )
    spectral_power = jnp.zeros(earlier_spectral_power.shape, jnp.bfloat16)
    pumping = None
    for offset, count, earlier in pieces:
        optical_depth, weight = depth_of(offset, count)
        local_column = jnp.pad(
            jnp.cumsum(optical_depth[:, : rows - 1], axis=1), ((0, 0), (1, 0), (0, 0), (0, 0))
        )
        column = earlier[:, None] + local_column
        radiance = line_half(entry_spectral_power, offset, count)[:, None] * jnp.exp(-column)
        spectral_power = lax.dynamic_update_slice_in_dim(
            spectral_power, radiance.astype(jnp.bfloat16), offset, axis=0
        )
        part_pumping = jnp.sum(weight * radiance, axis=0)
        part_heating = jnp.sum(radiance * (1.0 - jnp.exp(-optical_depth)), axis=0)
        if pumping is None:
            pumping, heating = part_pumping, part_heating
        else:
            pumping, heating = pumping + part_pumping, heating + part_heating
    pumping = pump_scale * pumping
    spin_ratio = pumping / (pumping + spin_decay * (1.0 + rubidium_number_amount))
    rubidium_polarization_new = fluid_occupied_sites * spin_ratio
    drift_speed = flow_scale * flow_rate_forward
    for substep in range(SUBSTEPS):
        bordered = first_bordered if substep == 0 else bordered_fields(physical_quantities)
        physical_quantities = advance(
            bordered, rubidium_number_amount, spin_ratio, heating, drift_speed, fluid_occupied_sites
        )
    return (
        spectral_power,
        physical_quantities[0],
        physical_quantities[1] + boundary_kelvin,
        rubidium_polarization_new,
    )


def solution(mesh):
    in_specs = (
        P("beam", "cross", None),
        P("beam", "cross", None),
        P("beam", "cross", None),
        P(None, "beam", "cross", None),
        P(None, "cross", None),
        P(),
        P("cross", None),
        P("beam", "cross"),
    )
    out_specs = (
        P(None, "beam", "cross", None),
        P("beam", "cross", None),
        P("beam", "cross", None),
        P("beam", "cross", None),
    )
    return jax.shard_map(local, mesh=mesh, in_specs=in_specs, out_specs=out_specs, check_vma=False)
```

```python
import jax
import jax.numpy as jnp
from jax import lax
from jax.sharding import PartitionSpec as P

SUBSTEPS = 2


rubidium_amount_slope = 23.25
rubidium_amount_center = 0.95
absorb_scale = 1.0
glass_depth = 0.07
saturation = 1.0
pump_scale = 0.015625
spin_decay = 0.5
exchange_rate = 0.05
xenon_relax = 0.02
heat_gain = 0.05
cooling = 0.02
xenon_diffusion = 0.09
conduction = 0.09
flow_scale = 0.2
boundary_kelvin = 1.0
neighbor_offsets = ((1, 0, 0), (-1, 0, 0), (0, 1, 0), (0, -1, 0), (0, 0, 1), (0, 0, -1))


def shifted(block, axis, shift):
    count = lax.axis_size(axis)
    if shift > 0:
        pairs = [(i, i + shift) for i in range(count - shift)]
    else:
        pairs = [(i - shift, i) for i in range(count + shift)]
    return lax.ppermute(block, axis, pairs)


def bordered_fields(block):
    _, rows, columns, _ = block.shape
    low_beam = shifted(block[:, rows - 1 :], "beam", 1)
    high_beam = shifted(block[:, :1], "beam", -1)
    low_cross = shifted(block[:, :, columns - 1 :], "cross", 1)
    high_cross = shifted(block[:, :, :1], "cross", -1)
    middle = jnp.concatenate([low_cross, block, high_cross], axis=2)
    zeros = jnp.zeros_like(low_beam[:, :, :1])
    low_beam = jnp.concatenate([zeros, low_beam, zeros], axis=2)
    high_beam = jnp.concatenate([zeros, high_beam, zeros], axis=2)
    bordered = jnp.concatenate([low_beam, middle, high_beam], axis=1)
    return jnp.pad(bordered, ((0, 0), (0, 0), (0, 0), (1, 1)))


def exclusive_scan(totals, axis, stride=1):
    count = lax.axis_size(axis) // stride
    if count == 1:
        return jnp.zeros_like(totals)
    before = shifted(totals, axis, stride)
    through = totals + before
    step = 2
    while step < count:
        arrived = shifted(through, axis, step * stride)
        before = before + arrived
        step *= 2
        if step < count:
            through = through + arrived
    return before


def paired_steps(totals, axis):
    count = lax.axis_size(axis)
    half = totals.shape[0] // 2
    is_low = lax.axis_index(axis) % 2 == 0
    first, second = totals[:half], totals[half:]
    mine = jnp.where(is_low, first, second)
    swap = [(i, i ^ 1) for i in range(count)]
    got = yield jnp.where(is_low, second, first), swap
    pair_total = mine + got
    pairs = count // 2
    before = yield pair_total, shift_pairs(count, 2)
    through = pair_total + before
    step = 2
    while step < pairs:
        arrived = yield through, shift_pairs(count, 2 * step)
        before = before + arrived
        step *= 2
        if step < pairs:
            through = through + arrived
    back = yield jnp.where(is_low, before + mine, before), swap
    return jnp.where(
        is_low, jnp.concatenate([before, back]), jnp.concatenate([back, before + got])
    )


def shift_pairs(count, shift):
    return [(i, i + shift) for i in range(count - shift)]


def pipelined_scan(totals, axis, rider, groups=2):
    count = lax.axis_size(axis)
    lines = totals.shape[0]
    if count % 2 or count <= 2 or lines % (2 * groups):
        return exclusive_scan(totals, axis), rider(None)
    size = lines // groups
    steps = [paired_steps(totals[g * size : (g + 1) * size], axis) for g in range(groups)]
    live, done, carried, stage = {}, {}, None, 0
    while stage < groups or live:
        if stage < groups:
            live[stage] = next(steps[stage])
        arrived = {g: lax.ppermute(payload, axis, pairs) for g, (payload, pairs) in live.items()}
        if stage == 0:
            arrived, carried = lax.optimization_barrier((arrived, rider(live[0][0])))
        else:
            arrived = lax.optimization_barrier(arrived)
        following = {}
        for g, value in arrived.items():
            try:
                following[g] = steps[g].send(value)
            except StopIteration as finished:
                done[g] = finished.value
        live = following
        stage += 1
    return jnp.concatenate([done[g] for g in range(groups)]), carried


def window(source, step_beam, step_cross, step_depth):
    return source[
        ...,
        1 + step_beam : source.shape[-3] - 1 + step_beam,
        1 + step_cross : source.shape[-2] - 1 + step_cross,
        1 + step_depth : source.shape[-1] - 1 + step_depth,
    ]


def advance(
    bordered, rubidium_number_amount, spin_ratio, heating, drift_speed, fluid_occupied_sites
):
    center = window(bordered, 0, 0, 0)
    complete_heat_ratio = bordered[1] + boundary_kelvin
    coefficients = jnp.stack(
        [xenon_diffusion * complete_heat_ratio**1.5, conduction * complete_heat_ratio**0.7]
    )
    coeff_center = window(coefficients, 0, 0, 0)
    diffused = jnp.zeros_like(center)
    for step_beam, step_cross, step_depth in neighbor_offsets:
        neighbor = window(bordered, step_beam, step_cross, step_depth)
        face_coeff = 0.5 * (coeff_center + window(coefficients, step_beam, step_cross, step_depth))
        diffused = diffused + face_coeff * (neighbor - center)
    upstream = window(bordered, -1, 0, 0)
    transport = diffused - drift_speed * (center - upstream)
    xenon_new = (
        center[0]
        + transport[0]
        + exchange_rate * rubidium_number_amount * (spin_ratio - center[0])
        - xenon_relax * center[0]
    )
    deviation = center[1] + transport[1] + heat_gain * heating - cooling * center[1]
    return jnp.stack([xenon_new * fluid_occupied_sites, deviation * fluid_occupied_sites])


def local(
    xenon_spin_polarization,
    heat_ratio,
    rubidium_polarization_old,
    earlier_spectral_power,
    entry_spectral_power,
    spectral_attenuation_section,
    flow_rate_forward,
    solid_pillar_flags,
):
    rows = earlier_spectral_power.shape[1]
    total_rows = rows * lax.axis_size("beam")
    physical_quantities = jnp.stack([xenon_spin_polarization, heat_ratio - boundary_kelvin])
    glass_cells = solid_pillar_flags.astype(jnp.float32)[:, :, None]
    fluid_occupied_sites = 1.0 - glass_cells
    rubidium_number_amount = fluid_occupied_sites * jnp.exp(
        rubidium_amount_slope * (rubidium_amount_center - 1.0 / heat_ratio)
    )
    absorber = (
        absorb_scale / total_rows * rubidium_number_amount * (1.0 - rubidium_polarization_old)
    )
    glass_term = glass_depth * glass_cells
    weight = spectral_attenuation_section[:, None, None, None] / (
        1.0 + earlier_spectral_power.astype(jnp.float32) / saturation
    )
    optical_depth = absorber[None] * weight + glass_term[None]
    totals = jnp.sum(optical_depth, axis=1)
    local_column = jnp.pad(
        jnp.cumsum(optical_depth[:, : rows - 1], axis=1), ((0, 0), (1, 0), (0, 0), (0, 0))
    )
    def first_border(after):
        fields = physical_quantities
        if after is not None:
            fields, _ = lax.optimization_barrier((fields, after))
        return bordered_fields(fields)

    prefix, first_bordered = pipelined_scan(totals, "beam", first_border)
    column = prefix[:, None] + local_column
    radiance = entry_spectral_power[:, None] * jnp.exp(-column)
    spectral_power = radiance.astype(jnp.bfloat16)
    pumping = pump_scale * jnp.sum(weight * radiance, axis=0)
    heating = jnp.sum(radiance * (1.0 - jnp.exp(-optical_depth)), axis=0)
    spin_ratio = pumping / (pumping + spin_decay * (1.0 + rubidium_number_amount))
    rubidium_polarization_new = fluid_occupied_sites * spin_ratio
    drift_speed = flow_scale * flow_rate_forward
    for substep in range(SUBSTEPS):
        bordered = first_bordered if substep == 0 else bordered_fields(physical_quantities)
        physical_quantities = advance(
            bordered, rubidium_number_amount, spin_ratio, heating, drift_speed, fluid_occupied_sites
        )
    return (
        spectral_power,
        physical_quantities[0],
        physical_quantities[1] + boundary_kelvin,
        rubidium_polarization_new,
    )


def solution(mesh):
    in_specs = (
        P("beam", "cross", None),
        P("beam", "cross", None),
        P("beam", "cross", None),
        P(None, "beam", "cross", None),
        P(None, "cross", None),
        P(),
        P("cross", None),
        P("beam", "cross"),
    )
    out_specs = (
        P(None, "beam", "cross", None),
        P("beam", "cross", None),
        P("beam", "cross", None),
        P("beam", "cross", None),
    )
    return jax.shard_map(local, mesh=mesh, in_specs=in_specs, out_specs=out_specs, check_vma=False)
```

```python
import jax
import jax.numpy as jnp
from jax import lax
from jax.sharding import PartitionSpec as P

SUBSTEPS = 2


rubidium_amount_slope = 23.25
rubidium_amount_center = 0.95
absorb_scale = 1.0
glass_depth = 0.07
saturation = 1.0
pump_scale = 0.015625
spin_decay = 0.5
exchange_rate = 0.05
xenon_relax = 0.02
heat_gain = 0.05
cooling = 0.02
xenon_diffusion = 0.09
conduction = 0.09
flow_scale = 0.2
boundary_kelvin = 1.0
neighbor_offsets = ((1, 0, 0), (-1, 0, 0), (0, 1, 0), (0, -1, 0), (0, 0, 1), (0, 0, -1))


def shifted(block, axis, shift):
    count = lax.axis_size(axis)
    if shift > 0:
        pairs = [(i, i + shift) for i in range(count - shift)]
    else:
        pairs = [(i - shift, i) for i in range(count + shift)]
    return lax.ppermute(block, axis, pairs)


def bordered_fields(block):
    _, rows, columns, _ = block.shape
    low_beam = shifted(block[:, rows - 1 :], "beam", 1)
    high_beam = shifted(block[:, :1], "beam", -1)
    low_cross = shifted(block[:, :, columns - 1 :], "cross", 1)
    high_cross = shifted(block[:, :, :1], "cross", -1)
    middle = jnp.concatenate([low_cross, block, high_cross], axis=2)
    zeros = jnp.zeros_like(low_beam[:, :, :1])
    low_beam = jnp.concatenate([zeros, low_beam, zeros], axis=2)
    high_beam = jnp.concatenate([zeros, high_beam, zeros], axis=2)
    bordered = jnp.concatenate([low_beam, middle, high_beam], axis=1)
    return jnp.pad(bordered, ((0, 0), (0, 0), (0, 0), (1, 1)))


def exclusive_scan(totals, axis, stride=1):
    count = lax.axis_size(axis) // stride
    if count == 1:
        return jnp.zeros_like(totals)
    before = shifted(totals, axis, stride)
    through = totals + before
    step = 2
    while step < count:
        arrived = shifted(through, axis, step * stride)
        before = before + arrived
        step *= 2
        if step < count:
            through = through + arrived
    return before


def paired_steps(totals, axis):
    count = lax.axis_size(axis)
    half = totals.shape[0] // 2
    is_low = lax.axis_index(axis) % 2 == 0
    first, second = totals[:half], totals[half:]
    mine = jnp.where(is_low, first, second)
    swap = [(i, i ^ 1) for i in range(count)]
    got = yield jnp.where(is_low, second, first), swap
    pair_total = mine + got
    pairs = count // 2
    before = yield pair_total, shift_pairs(count, 2)
    through = pair_total + before
    step = 2
    while step < pairs:
        arrived = yield through, shift_pairs(count, 2 * step)
        before = before + arrived
        step *= 2
        if step < pairs:
            through = through + arrived
    back = yield jnp.where(is_low, before + mine, before), swap
    return jnp.where(
        is_low, jnp.concatenate([before, back]), jnp.concatenate([back, before + got])
    )


def shift_pairs(count, shift):
    return [(i, i + shift) for i in range(count - shift)]


def pipelined_scan(totals, axis, rider, groups=2):
    count = lax.axis_size(axis)
    lines = totals.shape[0]
    if count % 2 or count <= 2 or lines % (2 * groups):
        return exclusive_scan(totals, axis), rider(None)
    size = lines // groups
    steps = [paired_steps(totals[g * size : (g + 1) * size], axis) for g in range(groups)]
    live, done, carried, stage = {}, {}, None, 0
    while stage < groups or live:
        if stage < groups:
            live[stage] = next(steps[stage])
        arrived = {g: lax.ppermute(payload, axis, pairs) for g, (payload, pairs) in live.items()}
        if stage == 2:
            arrived, carried = lax.optimization_barrier((arrived, rider(live[0][0])))
        else:
            arrived = lax.optimization_barrier(arrived)
        following = {}
        for g, value in arrived.items():
            try:
                following[g] = steps[g].send(value)
            except StopIteration as finished:
                done[g] = finished.value
        live = following
        stage += 1
    return jnp.concatenate([done[g] for g in range(groups)]), carried


def window(source, step_beam, step_cross, step_depth):
    return source[
        ...,
        1 + step_beam : source.shape[-3] - 1 + step_beam,
        1 + step_cross : source.shape[-2] - 1 + step_cross,
        1 + step_depth : source.shape[-1] - 1 + step_depth,
    ]


def advance(
    bordered, rubidium_number_amount, spin_ratio, heating, drift_speed, fluid_occupied_sites
):
    center = window(bordered, 0, 0, 0)
    complete_heat_ratio = bordered[1] + boundary_kelvin
    coefficients = jnp.stack(
        [xenon_diffusion * complete_heat_ratio**1.5, conduction * complete_heat_ratio**0.7]
    )
    coeff_center = window(coefficients, 0, 0, 0)
    diffused = jnp.zeros_like(center)
    for step_beam, step_cross, step_depth in neighbor_offsets:
        neighbor = window(bordered, step_beam, step_cross, step_depth)
        face_coeff = 0.5 * (coeff_center + window(coefficients, step_beam, step_cross, step_depth))
        diffused = diffused + face_coeff * (neighbor - center)
    upstream = window(bordered, -1, 0, 0)
    transport = diffused - drift_speed * (center - upstream)
    xenon_new = (
        center[0]
        + transport[0]
        + exchange_rate * rubidium_number_amount * (spin_ratio - center[0])
        - xenon_relax * center[0]
    )
    deviation = center[1] + transport[1] + heat_gain * heating - cooling * center[1]
    return jnp.stack([xenon_new * fluid_occupied_sites, deviation * fluid_occupied_sites])


def local(
    xenon_spin_polarization,
    heat_ratio,
    rubidium_polarization_old,
    earlier_spectral_power,
    entry_spectral_power,
    spectral_attenuation_section,
    flow_rate_forward,
    solid_pillar_flags,
):
    rows = earlier_spectral_power.shape[1]
    total_rows = rows * lax.axis_size("beam")
    physical_quantities = jnp.stack([xenon_spin_polarization, heat_ratio - boundary_kelvin])
    glass_cells = solid_pillar_flags.astype(jnp.float32)[:, :, None]
    fluid_occupied_sites = 1.0 - glass_cells
    rubidium_number_amount = fluid_occupied_sites * jnp.exp(
        rubidium_amount_slope * (rubidium_amount_center - 1.0 / heat_ratio)
    )
    absorber = (
        absorb_scale / total_rows * rubidium_number_amount * (1.0 - rubidium_polarization_old)
    )
    glass_term = glass_depth * glass_cells
    weight = spectral_attenuation_section[:, None, None, None] / (
        1.0 + earlier_spectral_power.astype(jnp.float32) / saturation
    )
    optical_depth = absorber[None] * weight + glass_term[None]
    totals = jnp.sum(optical_depth, axis=1)
    local_column = jnp.pad(
        jnp.cumsum(optical_depth[:, : rows - 1], axis=1), ((0, 0), (1, 0), (0, 0), (0, 0))
    )
    def first_border(after):
        fields = physical_quantities
        if after is not None:
            fields, _ = lax.optimization_barrier((fields, after))
        return bordered_fields(fields)

    prefix, first_bordered = pipelined_scan(totals, "beam", first_border)
    column = prefix[:, None] + local_column
    radiance = entry_spectral_power[:, None] * jnp.exp(-column)
    spectral_power = radiance.astype(jnp.bfloat16)
    pumping = pump_scale * jnp.sum(weight * radiance, axis=0)
    heating = jnp.sum(radiance * (1.0 - jnp.exp(-optical_depth)), axis=0)
    spin_ratio = pumping / (pumping + spin_decay * (1.0 + rubidium_number_amount))
    rubidium_polarization_new = fluid_occupied_sites * spin_ratio
    drift_speed = flow_scale * flow_rate_forward
    for substep in range(SUBSTEPS):
        bordered = first_bordered if substep == 0 else bordered_fields(physical_quantities)
        physical_quantities = advance(
            bordered, rubidium_number_amount, spin_ratio, heating, drift_speed, fluid_occupied_sites
        )
    return (
        spectral_power,
        physical_quantities[0],
        physical_quantities[1] + boundary_kelvin,
        rubidium_polarization_new,
    )


def solution(mesh):
    in_specs = (
        P("beam", "cross", None),
        P("beam", "cross", None),
        P("beam", "cross", None),
        P(None, "beam", "cross", None),
        P(None, "cross", None),
        P(),
        P("cross", None),
        P("beam", "cross"),
    )
    out_specs = (
        P(None, "beam", "cross", None),
        P("beam", "cross", None),
        P("beam", "cross", None),
        P("beam", "cross", None),
    )
    return jax.shard_map(local, mesh=mesh, in_specs=in_specs, out_specs=out_specs, check_vma=False)
```

```python
import jax
import jax.numpy as jnp
from jax import lax
from jax.sharding import PartitionSpec as P

SUBSTEPS = 2


rubidium_amount_slope = 23.25
rubidium_amount_center = 0.95
absorb_scale = 1.0
glass_depth = 0.07
saturation = 1.0
pump_scale = 0.015625
spin_decay = 0.5
exchange_rate = 0.05
xenon_relax = 0.02
heat_gain = 0.05
cooling = 0.02
xenon_diffusion = 0.09
conduction = 0.09
flow_scale = 0.2
boundary_kelvin = 1.0
neighbor_offsets = ((1, 0, 0), (-1, 0, 0), (0, 1, 0), (0, -1, 0), (0, 0, 1), (0, 0, -1))


def shifted(block, axis, shift):
    count = lax.axis_size(axis)
    if shift > 0:
        pairs = [(i, i + shift) for i in range(count - shift)]
    else:
        pairs = [(i - shift, i) for i in range(count + shift)]
    return lax.ppermute(block, axis, pairs)


def bordered_fields(block):
    _, rows, columns, _ = block.shape
    low_beam = shifted(block[:, rows - 1 :], "beam", 1)
    high_beam = shifted(block[:, :1], "beam", -1)
    low_cross = shifted(block[:, :, columns - 1 :], "cross", 1)
    high_cross = shifted(block[:, :, :1], "cross", -1)
    middle = jnp.concatenate([low_cross, block, high_cross], axis=2)
    zeros = jnp.zeros_like(low_beam[:, :, :1])
    low_beam = jnp.concatenate([zeros, low_beam, zeros], axis=2)
    high_beam = jnp.concatenate([zeros, high_beam, zeros], axis=2)
    bordered = jnp.concatenate([low_beam, middle, high_beam], axis=1)
    return jnp.pad(bordered, ((0, 0), (0, 0), (0, 0), (1, 1)))


def exclusive_scan(totals, axis, stride=1):
    count = lax.axis_size(axis) // stride
    if count == 1:
        return jnp.zeros_like(totals)
    before = shifted(totals, axis, stride)
    through = totals + before
    step = 2
    while step < count:
        arrived = shifted(through, axis, step * stride)
        before = before + arrived
        step *= 2
        if step < count:
            through = through + arrived
    return before


def paired_steps(totals, axis):
    count = lax.axis_size(axis)
    half = totals.shape[0] // 2
    is_low = lax.axis_index(axis) % 2 == 0
    first, second = totals[:half], totals[half:]
    mine = jnp.where(is_low, first, second)
    swap = [(i, i ^ 1) for i in range(count)]
    got = yield jnp.where(is_low, second, first), swap
    pair_total = mine + got
    pairs = count // 2
    before = yield pair_total, shift_pairs(count, 2)
    through = pair_total + before
    step = 2
    while step < pairs:
        arrived = yield through, shift_pairs(count, 2 * step)
        before = before + arrived
        step *= 2
        if step < pairs:
            through = through + arrived
    back = yield jnp.where(is_low, before + mine, before), swap
    return jnp.where(
        is_low, jnp.concatenate([before, back]), jnp.concatenate([back, before + got])
    )


def shift_pairs(count, shift):
    return [(i, i + shift) for i in range(count - shift)]


def pipelined_scan(totals_of, emit, lines, axis, rider, groups=2):
    count = lax.axis_size(axis)
    if count % 2 or count <= 2 or lines % (2 * groups):
        earlier = exclusive_scan(totals_of(0, lines, None), axis)
        return [emit(0, lines, earlier)], rider(None)
    size = lines // groups
    steps = [None] * groups
    steps[0] = paired_steps(totals_of(0, size, None), axis)
    live, made, carried, stage = {}, [], None, 0
    while stage < groups or live:
        if stage < groups:
            live[stage] = next(steps[stage])
        arrived = {g: lax.ppermute(payload, axis, pairs) for g, (payload, pairs) in live.items()}
        if stage == 0:
            for g in range(1, groups):
                steps[g] = paired_steps(totals_of(g * size, size, live[0][0]), axis)
        tied = (arrived, made)
        if stage == 2:
            tied, carried = lax.optimization_barrier((tied, rider(live[0][0])))
        else:
            tied = lax.optimization_barrier(tied)
        arrived, made = tied
        following = {}
        for g, value in arrived.items():
            try:
                following[g] = steps[g].send(value)
            except StopIteration as finished:
                made = made + [emit(g * size, size, finished.value)]
        live = following
        stage += 1
    return made, carried


def window(source, step_beam, step_cross, step_depth):
    return source[
        ...,
        1 + step_beam : source.shape[-3] - 1 + step_beam,
        1 + step_cross : source.shape[-2] - 1 + step_cross,
        1 + step_depth : source.shape[-1] - 1 + step_depth,
    ]


def advance(
    bordered, rubidium_number_amount, spin_ratio, heating, drift_speed, fluid_occupied_sites
):
    center = window(bordered, 0, 0, 0)
    complete_heat_ratio = bordered[1] + boundary_kelvin
    coefficients = jnp.stack(
        [xenon_diffusion * complete_heat_ratio**1.5, conduction * complete_heat_ratio**0.7]
    )
    coeff_center = window(coefficients, 0, 0, 0)
    diffused = jnp.zeros_like(center)
    for step_beam, step_cross, step_depth in neighbor_offsets:
        neighbor = window(bordered, step_beam, step_cross, step_depth)
        face_coeff = 0.5 * (coeff_center + window(coefficients, step_beam, step_cross, step_depth))
        diffused = diffused + face_coeff * (neighbor - center)
    upstream = window(bordered, -1, 0, 0)
    transport = diffused - drift_speed * (center - upstream)
    xenon_new = (
        center[0]
        + transport[0]
        + exchange_rate * rubidium_number_amount * (spin_ratio - center[0])
        - xenon_relax * center[0]
    )
    deviation = center[1] + transport[1] + heat_gain * heating - cooling * center[1]
    return jnp.stack([xenon_new * fluid_occupied_sites, deviation * fluid_occupied_sites])


def local(
    xenon_spin_polarization,
    heat_ratio,
    rubidium_polarization_old,
    earlier_spectral_power,
    entry_spectral_power,
    spectral_attenuation_section,
    flow_rate_forward,
    solid_pillar_flags,
):
    rows = earlier_spectral_power.shape[1]
    total_rows = rows * lax.axis_size("beam")
    physical_quantities = jnp.stack([xenon_spin_polarization, heat_ratio - boundary_kelvin])
    glass_cells = solid_pillar_flags.astype(jnp.float32)[:, :, None]
    fluid_occupied_sites = 1.0 - glass_cells
    rubidium_number_amount = fluid_occupied_sites * jnp.exp(
        rubidium_amount_slope * (rubidium_amount_center - 1.0 / heat_ratio)
    )
    absorber = (
        absorb_scale / total_rows * rubidium_number_amount * (1.0 - rubidium_polarization_old)
    )
    glass_term = glass_depth * glass_cells

    def depth_of(start, size):
        weight = spectral_attenuation_section[start : start + size, None, None, None] / (
            1.0 + earlier_spectral_power[start : start + size].astype(jnp.float32) / saturation
        )
        return absorber[None] * weight + glass_term[None], weight

    def totals_of(start, size, after):
        optical_depth, _ = depth_of(start, size)
        if after is not None:
            optical_depth, _ = lax.optimization_barrier((optical_depth, after))
        return jnp.sum(optical_depth, axis=1)

    def emit(start, size, earlier):
        optical_depth, weight = depth_of(start, size)
        local_column = jnp.pad(
            jnp.cumsum(optical_depth[:, : rows - 1], axis=1), ((0, 0), (1, 0), (0, 0), (0, 0))
        )
        column = earlier[:, None] + local_column
        radiance = entry_spectral_power[start : start + size, None] * jnp.exp(-column)
        return (
            radiance.astype(jnp.bfloat16),
            jnp.sum(weight * radiance, axis=0),
            jnp.sum(radiance * (1.0 - jnp.exp(-optical_depth)), axis=0),
        )

    def first_border(after):
        fields = physical_quantities
        if after is not None:
            fields, _ = lax.optimization_barrier((fields, after))
        return bordered_fields(fields)

    lines = earlier_spectral_power.shape[0]
    made, first_bordered = pipelined_scan(totals_of, emit, lines, "beam", first_border)
    spectral_power = jnp.zeros(earlier_spectral_power.shape, jnp.bfloat16)
    start = 0
    for part, _, _ in made:
        spectral_power = lax.dynamic_update_slice_in_dim(spectral_power, part, start, axis=0)
        start += part.shape[0]
    pumping = made[0][1]
    heating = made[0][2]
    for _, part_pumping, part_heating in made[1:]:
        pumping = pumping + part_pumping
        heating = heating + part_heating
    pumping = pump_scale * pumping
    spin_ratio = pumping / (pumping + spin_decay * (1.0 + rubidium_number_amount))
    rubidium_polarization_new = fluid_occupied_sites * spin_ratio
    drift_speed = flow_scale * flow_rate_forward
    for substep in range(SUBSTEPS):
        bordered = first_bordered if substep == 0 else bordered_fields(physical_quantities)
        physical_quantities = advance(
            bordered, rubidium_number_amount, spin_ratio, heating, drift_speed, fluid_occupied_sites
        )
    return (
        spectral_power,
        physical_quantities[0],
        physical_quantities[1] + boundary_kelvin,
        rubidium_polarization_new,
    )


def solution(mesh):
    in_specs = (
        P("beam", "cross", None),
        P("beam", "cross", None),
        P("beam", "cross", None),
        P(None, "beam", "cross", None),
        P(None, "cross", None),
        P(),
        P("cross", None),
        P("beam", "cross"),
    )
    out_specs = (
        P(None, "beam", "cross", None),
        P("beam", "cross", None),
        P("beam", "cross", None),
        P("beam", "cross", None),
    )
    return jax.shard_map(local, mesh=mesh, in_specs=in_specs, out_specs=out_specs, check_vma=False)
```

```python
import jax
import jax.numpy as jnp
from jax import lax
from jax.sharding import PartitionSpec as P

SUBSTEPS = 2


rubidium_amount_slope = 23.25
rubidium_amount_center = 0.95
absorb_scale = 1.0
glass_depth = 0.07
saturation = 1.0
pump_scale = 0.015625
spin_decay = 0.5
exchange_rate = 0.05
xenon_relax = 0.02
heat_gain = 0.05
cooling = 0.02
xenon_diffusion = 0.09
conduction = 0.09
flow_scale = 0.2
boundary_kelvin = 1.0
neighbor_offsets = ((1, 0, 0), (-1, 0, 0), (0, 1, 0), (0, -1, 0), (0, 0, 1), (0, 0, -1))


def shifted(block, axis, shift):
    count = lax.axis_size(axis)
    if shift > 0:
        pairs = [(i, i + shift) for i in range(count - shift)]
    else:
        pairs = [(i - shift, i) for i in range(count + shift)]
    return lax.ppermute(block, axis, pairs)


def bordered_fields(block):
    _, rows, columns, _ = block.shape
    low_beam = shifted(block[:, rows - 1 :], "beam", 1)
    high_beam = shifted(block[:, :1], "beam", -1)
    low_cross = shifted(block[:, :, columns - 1 :], "cross", 1)
    high_cross = shifted(block[:, :, :1], "cross", -1)
    middle = jnp.concatenate([low_cross, block, high_cross], axis=2)
    zeros = jnp.zeros_like(low_beam[:, :, :1])
    low_beam = jnp.concatenate([zeros, low_beam, zeros], axis=2)
    high_beam = jnp.concatenate([zeros, high_beam, zeros], axis=2)
    bordered = jnp.concatenate([low_beam, middle, high_beam], axis=1)
    return jnp.pad(bordered, ((0, 0), (0, 0), (0, 0), (1, 1)))


def exclusive_scan(totals, axis, stride=1):
    count = lax.axis_size(axis) // stride
    if count == 1:
        return jnp.zeros_like(totals)
    before = shifted(totals, axis, stride)
    through = totals + before
    step = 2
    while step < count:
        arrived = shifted(through, axis, step * stride)
        before = before + arrived
        step *= 2
        if step < count:
            through = through + arrived
    return before


def paired_steps(totals, axis):
    count = lax.axis_size(axis)
    half = totals.shape[0] // 2
    is_low = lax.axis_index(axis) % 2 == 0
    first, second = totals[:half], totals[half:]
    mine = jnp.where(is_low, first, second)
    swap = [(i, i ^ 1) for i in range(count)]
    got = yield jnp.where(is_low, second, first), swap
    pair_total = mine + got
    pairs = count // 2
    before = yield pair_total, shift_pairs(count, 2)
    through = pair_total + before
    step = 2
    while step < pairs:
        arrived = yield through, shift_pairs(count, 2 * step)
        before = before + arrived
        step *= 2
        if step < pairs:
            through = through + arrived
    back = yield jnp.where(is_low, before + mine, before), swap
    return jnp.where(
        is_low, jnp.concatenate([before, back]), jnp.concatenate([back, before + got])
    )


def shift_pairs(count, shift):
    return [(i, i + shift) for i in range(count - shift)]


def pipelined_scan(totals_of, emit, lines, axis, rider, groups=2):
    count = lax.axis_size(axis)
    if count % 2 or count <= 2 or lines % (2 * groups):
        earlier = exclusive_scan(totals_of(0, lines, None), axis)
        return [emit(0, lines, earlier)], rider(None)
    size = lines // groups
    steps = [None] * groups
    steps[0] = paired_steps(totals_of(0, size, None), axis)
    live, made, carried, stage = {}, [], None, 0
    while stage < groups or live:
        if stage < groups:
            live[stage] = next(steps[stage])
        arrived = {g: lax.ppermute(payload, axis, pairs) for g, (payload, pairs) in live.items()}
        if stage == 0:
            for g in range(1, groups):
                steps[g] = paired_steps(totals_of(g * size, size, live[0][0]), axis)
        tied = (arrived, made)
        if stage == 2:
            tied, carried = lax.optimization_barrier((tied, rider(live[0][0])))
        else:
            tied = lax.optimization_barrier(tied)
        arrived, made = tied
        following = {}
        for g, value in arrived.items():
            try:
                following[g] = steps[g].send(value)
            except StopIteration as finished:
                made = made + [emit(g * size, size, finished.value)]
        live = following
        stage += 1
    return made, carried


def window(source, step_beam, step_cross, step_depth):
    return source[
        ...,
        1 + step_beam : source.shape[-3] - 1 + step_beam,
        1 + step_cross : source.shape[-2] - 1 + step_cross,
        1 + step_depth : source.shape[-1] - 1 + step_depth,
    ]


def advance(
    bordered, rubidium_number_amount, spin_ratio, heating, drift_speed, fluid_occupied_sites
):
    center = window(bordered, 0, 0, 0)
    complete_heat_ratio = bordered[1] + boundary_kelvin
    coefficients = jnp.stack(
        [xenon_diffusion * complete_heat_ratio**1.5, conduction * complete_heat_ratio**0.7]
    )
    coeff_center = window(coefficients, 0, 0, 0)
    diffused = jnp.zeros_like(center)
    for step_beam, step_cross, step_depth in neighbor_offsets:
        neighbor = window(bordered, step_beam, step_cross, step_depth)
        face_coeff = 0.5 * (coeff_center + window(coefficients, step_beam, step_cross, step_depth))
        diffused = diffused + face_coeff * (neighbor - center)
    upstream = window(bordered, -1, 0, 0)
    transport = diffused - drift_speed * (center - upstream)
    xenon_new = (
        center[0]
        + transport[0]
        + exchange_rate * rubidium_number_amount * (spin_ratio - center[0])
        - xenon_relax * center[0]
    )
    deviation = center[1] + transport[1] + heat_gain * heating - cooling * center[1]
    return jnp.stack([xenon_new * fluid_occupied_sites, deviation * fluid_occupied_sites])


def local(
    xenon_spin_polarization,
    heat_ratio,
    rubidium_polarization_old,
    earlier_spectral_power,
    entry_spectral_power,
    spectral_attenuation_section,
    flow_rate_forward,
    solid_pillar_flags,
):
    rows = earlier_spectral_power.shape[1]
    total_rows = rows * lax.axis_size("beam")
    physical_quantities = jnp.stack([xenon_spin_polarization, heat_ratio - boundary_kelvin])
    glass_cells = solid_pillar_flags.astype(jnp.float32)[:, :, None]
    fluid_occupied_sites = 1.0 - glass_cells
    rubidium_number_amount = fluid_occupied_sites * jnp.exp(
        rubidium_amount_slope * (rubidium_amount_center - 1.0 / heat_ratio)
    )
    absorber = (
        absorb_scale / total_rows * rubidium_number_amount * (1.0 - rubidium_polarization_old)
    )
    glass_term = glass_depth * glass_cells

    def depth_of(start, size):
        weight = spectral_attenuation_section[start : start + size, None, None, None] / (
            1.0 + earlier_spectral_power[start : start + size].astype(jnp.float32) / saturation
        )
        return absorber[None] * weight + glass_term[None], weight

    def totals_of(start, size, after):
        if after is None:
            earlier, absorbed = lax.optimization_barrier(
                (earlier_spectral_power[start : start + size], absorber)
            )
            weight = spectral_attenuation_section[start : start + size, None, None, None] / (
                1.0 + earlier.astype(jnp.float32) / saturation
            )
            return jnp.sum(absorbed[None] * weight + glass_term[None], axis=1)
        optical_depth, _ = depth_of(start, size)
        optical_depth, _ = lax.optimization_barrier((optical_depth, after))
        return jnp.sum(optical_depth, axis=1)

    def emit(start, size, earlier):
        optical_depth, weight = depth_of(start, size)
        local_column = jnp.pad(
            jnp.cumsum(optical_depth[:, : rows - 1], axis=1), ((0, 0), (1, 0), (0, 0), (0, 0))
        )
        column = earlier[:, None] + local_column
        radiance = entry_spectral_power[start : start + size, None] * jnp.exp(-column)
        return (
            radiance.astype(jnp.bfloat16),
            jnp.sum(weight * radiance, axis=0),
            jnp.sum(radiance * (1.0 - jnp.exp(-optical_depth)), axis=0),
        )

    def first_border(after):
        fields = physical_quantities
        if after is not None:
            fields, _ = lax.optimization_barrier((fields, after))
        return bordered_fields(fields)

    lines = earlier_spectral_power.shape[0]
    made, first_bordered = pipelined_scan(totals_of, emit, lines, "beam", first_border)
    spectral_power = jnp.zeros(earlier_spectral_power.shape, jnp.bfloat16)
    start = 0
    for part, _, _ in made:
        spectral_power = lax.dynamic_update_slice_in_dim(spectral_power, part, start, axis=0)
        start += part.shape[0]
    pumping = made[0][1]
    heating = made[0][2]
    for _, part_pumping, part_heating in made[1:]:
        pumping = pumping + part_pumping
        heating = heating + part_heating
    pumping = pump_scale * pumping
    spin_ratio = pumping / (pumping + spin_decay * (1.0 + rubidium_number_amount))
    rubidium_polarization_new = fluid_occupied_sites * spin_ratio
    drift_speed = flow_scale * flow_rate_forward
    for substep in range(SUBSTEPS):
        bordered = first_bordered if substep == 0 else bordered_fields(physical_quantities)
        physical_quantities = advance(
            bordered, rubidium_number_amount, spin_ratio, heating, drift_speed, fluid_occupied_sites
        )
    return (
        spectral_power,
        physical_quantities[0],
        physical_quantities[1] + boundary_kelvin,
        rubidium_polarization_new,
    )


def solution(mesh):
    in_specs = (
        P("beam", "cross", None),
        P("beam", "cross", None),
        P("beam", "cross", None),
        P(None, "beam", "cross", None),
        P(None, "cross", None),
        P(),
        P("cross", None),
        P("beam", "cross"),
    )
    out_specs = (
        P(None, "beam", "cross", None),
        P("beam", "cross", None),
        P("beam", "cross", None),
        P("beam", "cross", None),
    )
    return jax.shard_map(local, mesh=mesh, in_specs=in_specs, out_specs=out_specs, check_vma=False)
```

```python
import jax
import jax.numpy as jnp
from jax import lax
from jax.sharding import PartitionSpec as P

SUBSTEPS = 2


rubidium_amount_slope = 23.25
rubidium_amount_center = 0.95
absorb_scale = 1.0
glass_depth = 0.07
saturation = 1.0
pump_scale = 0.015625
spin_decay = 0.5
exchange_rate = 0.05
xenon_relax = 0.02
heat_gain = 0.05
cooling = 0.02
xenon_diffusion = 0.09
conduction = 0.09
flow_scale = 0.2
boundary_kelvin = 1.0
neighbor_offsets = ((1, 0, 0), (-1, 0, 0), (0, 1, 0), (0, -1, 0), (0, 0, 1), (0, 0, -1))


def shifted(block, axis, shift):
    count = lax.axis_size(axis)
    if shift > 0:
        pairs = [(i, i + shift) for i in range(count - shift)]
    else:
        pairs = [(i - shift, i) for i in range(count + shift)]
    return lax.ppermute(block, axis, pairs)


def beam_faces(block):
    rows = block.shape[1]
    return shifted(block[:, rows - 1 :], "beam", 1), shifted(block[:, :1], "beam", -1)


def cross_faces(block):
    columns = block.shape[2]
    return shifted(block[:, :, columns - 1 :], "cross", 1), shifted(block[:, :, :1], "cross", -1)


def bordered_fields(block, beam=None, cross=None):
    low_beam, high_beam = beam_faces(block) if beam is None else beam
    low_cross, high_cross = cross_faces(block) if cross is None else cross
    middle = jnp.concatenate([low_cross, block, high_cross], axis=2)
    zeros = jnp.zeros_like(low_beam[:, :, :1])
    low_beam = jnp.concatenate([zeros, low_beam, zeros], axis=2)
    high_beam = jnp.concatenate([zeros, high_beam, zeros], axis=2)
    bordered = jnp.concatenate([low_beam, middle, high_beam], axis=1)
    return jnp.pad(bordered, ((0, 0), (0, 0), (0, 0), (1, 1)))


def exclusive_scan(totals, axis, stride=1):
    count = lax.axis_size(axis) // stride
    if count == 1:
        return jnp.zeros_like(totals)
    before = shifted(totals, axis, stride)
    through = totals + before
    step = 2
    while step < count:
        arrived = shifted(through, axis, step * stride)
        before = before + arrived
        step *= 2
        if step < count:
            through = through + arrived
    return before


def paired_steps(totals, axis):
    count = lax.axis_size(axis)
    half = totals.shape[0] // 2
    is_low = lax.axis_index(axis) % 2 == 0
    first, second = totals[:half], totals[half:]
    mine = jnp.where(is_low, first, second)
    swap = [(i, i ^ 1) for i in range(count)]
    got = yield jnp.where(is_low, second, first), swap
    pair_total = mine + got
    pairs = count // 2
    before = yield pair_total, shift_pairs(count, 2)
    through = pair_total + before
    step = 2
    while step < pairs:
        arrived = yield through, shift_pairs(count, 2 * step)
        before = before + arrived
        step *= 2
        if step < pairs:
            through = through + arrived
    back = yield jnp.where(is_low, before + mine, before), swap
    return jnp.where(
        is_low, jnp.concatenate([before, back]), jnp.concatenate([back, before + got])
    )


def shift_pairs(count, shift):
    return [(i, i + shift) for i in range(count - shift)]


def pipelined_scan(totals_of, emit, lines, axis, riders, groups=2):
    count = lax.axis_size(axis)
    if count % 2 or count <= 2 or lines % (2 * groups):
        earlier = exclusive_scan(totals_of(0, lines, None), axis)
        return [emit(0, lines, earlier)], {stage: rider(None) for stage, rider in riders.items()}
    size = lines // groups
    steps = [None] * groups
    steps[0] = paired_steps(totals_of(0, size, None), axis)
    live, made, carried, stage = {}, [], {}, 0
    while stage < groups or live:
        if stage < groups:
            live[stage] = next(steps[stage])
        arrived = {g: lax.ppermute(payload, axis, pairs) for g, (payload, pairs) in live.items()}
        if stage == 0:
            for g in range(1, groups):
                steps[g] = paired_steps(totals_of(g * size, size, live[0][0]), axis)
        tied = (arrived, made)
        if stage in riders:
            tied, carried[stage] = lax.optimization_barrier((tied, riders[stage](live[0][0])))
        else:
            tied = lax.optimization_barrier(tied)
        arrived, made = tied
        following = {}
        for g, value in arrived.items():
            try:
                following[g] = steps[g].send(value)
            except StopIteration as finished:
                made = made + [emit(g * size, size, finished.value)]
        live = following
        stage += 1
    return made, carried


def window(source, step_beam, step_cross, step_depth):
    return source[
        ...,
        1 + step_beam : source.shape[-3] - 1 + step_beam,
        1 + step_cross : source.shape[-2] - 1 + step_cross,
        1 + step_depth : source.shape[-1] - 1 + step_depth,
    ]


def advance(
    bordered, rubidium_number_amount, spin_ratio, heating, drift_speed, fluid_occupied_sites
):
    center = window(bordered, 0, 0, 0)
    complete_heat_ratio = bordered[1] + boundary_kelvin
    coefficients = jnp.stack(
        [xenon_diffusion * complete_heat_ratio**1.5, conduction * complete_heat_ratio**0.7]
    )
    coeff_center = window(coefficients, 0, 0, 0)
    diffused = jnp.zeros_like(center)
    for step_beam, step_cross, step_depth in neighbor_offsets:
        neighbor = window(bordered, step_beam, step_cross, step_depth)
        face_coeff = 0.5 * (coeff_center + window(coefficients, step_beam, step_cross, step_depth))
        diffused = diffused + face_coeff * (neighbor - center)
    upstream = window(bordered, -1, 0, 0)
    transport = diffused - drift_speed * (center - upstream)
    xenon_new = (
        center[0]
        + transport[0]
        + exchange_rate * rubidium_number_amount * (spin_ratio - center[0])
        - xenon_relax * center[0]
    )
    deviation = center[1] + transport[1] + heat_gain * heating - cooling * center[1]
    return jnp.stack([xenon_new * fluid_occupied_sites, deviation * fluid_occupied_sites])


def local(
    xenon_spin_polarization,
    heat_ratio,
    rubidium_polarization_old,
    earlier_spectral_power,
    entry_spectral_power,
    spectral_attenuation_section,
    flow_rate_forward,
    solid_pillar_flags,
):
    rows = earlier_spectral_power.shape[1]
    total_rows = rows * lax.axis_size("beam")
    physical_quantities = jnp.stack([xenon_spin_polarization, heat_ratio - boundary_kelvin])
    glass_cells = solid_pillar_flags.astype(jnp.float32)[:, :, None]
    fluid_occupied_sites = 1.0 - glass_cells
    rubidium_number_amount = fluid_occupied_sites * jnp.exp(
        rubidium_amount_slope * (rubidium_amount_center - 1.0 / heat_ratio)
    )
    absorber = (
        absorb_scale / total_rows * rubidium_number_amount * (1.0 - rubidium_polarization_old)
    )
    glass_term = glass_depth * glass_cells

    def depth_of(start, size):
        weight = spectral_attenuation_section[start : start + size, None, None, None] / (
            1.0 + earlier_spectral_power[start : start + size].astype(jnp.float32) / saturation
        )
        return absorber[None] * weight + glass_term[None], weight

    def totals_of(start, size, after):
        optical_depth, _ = depth_of(start, size)
        if after is not None:
            optical_depth, _ = lax.optimization_barrier((optical_depth, after))
        return jnp.sum(optical_depth, axis=1)

    def emit(start, size, earlier):
        optical_depth, weight = depth_of(start, size)
        local_column = jnp.pad(
            jnp.cumsum(optical_depth[:, : rows - 1], axis=1), ((0, 0), (1, 0), (0, 0), (0, 0))
        )
        column = earlier[:, None] + local_column
        radiance = entry_spectral_power[start : start + size, None] * jnp.exp(-column)
        return (
            radiance.astype(jnp.bfloat16),
            jnp.sum(weight * radiance, axis=0),
            jnp.sum(radiance * (1.0 - jnp.exp(-optical_depth)), axis=0),
        )

    def tied_faces(faces):
        def exchange(after):
            fields = physical_quantities
            if after is not None:
                fields, _ = lax.optimization_barrier((fields, after))
            return faces(fields)

        return exchange

    lines = earlier_spectral_power.shape[0]
    made, first_faces = pipelined_scan(
        totals_of, emit, lines, "beam", {2: tied_faces(beam_faces), 3: tied_faces(cross_faces)}
    )
    first_bordered = bordered_fields(physical_quantities, first_faces[2], first_faces[3])
    spectral_power = jnp.zeros(earlier_spectral_power.shape, jnp.bfloat16)
    start = 0
    for part, _, _ in made:
        spectral_power = lax.dynamic_update_slice_in_dim(spectral_power, part, start, axis=0)
        start += part.shape[0]
    pumping = made[0][1]
    heating = made[0][2]
    for _, part_pumping, part_heating in made[1:]:
        pumping = pumping + part_pumping
        heating = heating + part_heating
    pumping = pump_scale * pumping
    spin_ratio = pumping / (pumping + spin_decay * (1.0 + rubidium_number_amount))
    rubidium_polarization_new = fluid_occupied_sites * spin_ratio
    drift_speed = flow_scale * flow_rate_forward
    for substep in range(SUBSTEPS):
        bordered = first_bordered if substep == 0 else bordered_fields(physical_quantities)
        physical_quantities = advance(
            bordered, rubidium_number_amount, spin_ratio, heating, drift_speed, fluid_occupied_sites
        )
    return (
        spectral_power,
        physical_quantities[0],
        physical_quantities[1] + boundary_kelvin,
        rubidium_polarization_new,
    )


def solution(mesh):
    in_specs = (
        P("beam", "cross", None),
        P("beam", "cross", None),
        P("beam", "cross", None),
        P(None, "beam", "cross", None),
        P(None, "cross", None),
        P(),
        P("cross", None),
        P("beam", "cross"),
    )
    out_specs = (
        P(None, "beam", "cross", None),
        P("beam", "cross", None),
        P("beam", "cross", None),
        P("beam", "cross", None),
    )
    return jax.shard_map(local, mesh=mesh, in_specs=in_specs, out_specs=out_specs, check_vma=False)
```

```python
import jax
import jax.numpy as jnp
from jax import lax
from jax.sharding import PartitionSpec as P

SUBSTEPS = 2


rubidium_amount_slope = 23.25
rubidium_amount_center = 0.95
absorb_scale = 1.0
glass_depth = 0.07
saturation = 1.0
pump_scale = 0.015625
spin_decay = 0.5
exchange_rate = 0.05
xenon_relax = 0.02
heat_gain = 0.05
cooling = 0.02
xenon_diffusion = 0.09
conduction = 0.09
flow_scale = 0.2
boundary_kelvin = 1.0
neighbor_offsets = ((1, 0, 0), (-1, 0, 0), (0, 1, 0), (0, -1, 0), (0, 0, 1), (0, 0, -1))


def shifted(block, axis, shift):
    count = lax.axis_size(axis)
    if shift > 0:
        pairs = [(i, i + shift) for i in range(count - shift)]
    else:
        pairs = [(i - shift, i) for i in range(count + shift)]
    return lax.ppermute(block, axis, pairs)


def beam_faces(block):
    rows = block.shape[1]
    return shifted(block[:, rows - 1 :], "beam", 1), shifted(block[:, :1], "beam", -1)


def cross_faces(block):
    columns = block.shape[2]
    return shifted(block[:, :, columns - 1 :], "cross", 1), shifted(block[:, :, :1], "cross", -1)


def bordered_fields(block, beam=None, cross=None):
    low_beam, high_beam = beam_faces(block) if beam is None else beam
    low_cross, high_cross = cross_faces(block) if cross is None else cross
    middle = jnp.concatenate([low_cross, block, high_cross], axis=2)
    zeros = jnp.zeros_like(low_beam[:, :, :1])
    low_beam = jnp.concatenate([zeros, low_beam, zeros], axis=2)
    high_beam = jnp.concatenate([zeros, high_beam, zeros], axis=2)
    bordered = jnp.concatenate([low_beam, middle, high_beam], axis=1)
    return jnp.pad(bordered, ((0, 0), (0, 0), (0, 0), (1, 1)))


def exclusive_scan(totals, axis, stride=1):
    count = lax.axis_size(axis) // stride
    if count == 1:
        return jnp.zeros_like(totals)
    before = shifted(totals, axis, stride)
    through = totals + before
    step = 2
    while step < count:
        arrived = shifted(through, axis, step * stride)
        before = before + arrived
        step *= 2
        if step < count:
            through = through + arrived
    return before


def paired_steps(totals, axis):
    count = lax.axis_size(axis)
    half = totals.shape[0] // 2
    is_low = lax.axis_index(axis) % 2 == 0
    first, second = totals[:half], totals[half:]
    mine = jnp.where(is_low, first, second)
    swap = [(i, i ^ 1) for i in range(count)]
    got = yield jnp.where(is_low, second, first), swap
    pair_total = mine + got
    pairs = count // 2
    before = yield pair_total, shift_pairs(count, 2)
    through = pair_total + before
    step = 2
    while step < pairs:
        arrived = yield through, shift_pairs(count, 2 * step)
        before = before + arrived
        step *= 2
        if step < pairs:
            through = through + arrived
    back = yield jnp.where(is_low, before + mine, before), swap
    return jnp.where(
        is_low, jnp.concatenate([before, back]), jnp.concatenate([back, before + got])
    )


def shift_pairs(count, shift):
    return [(i, i + shift) for i in range(count - shift)]


def pipelined_scan(totals_of, emit, lines, axis, riders, groups=2):
    count = lax.axis_size(axis)
    if count % 2 or count <= 2 or lines % (2 * groups):
        earlier = exclusive_scan(totals_of(0, lines, None), axis)
        return [emit(0, lines, earlier)], {stage: rider(None) for stage, rider in riders.items()}
    size = lines // groups
    steps = [None] * groups
    steps[0] = paired_steps(totals_of(0, size, None), axis)
    live, made, carried, stage = {}, [], {}, 0
    while stage < groups or live:
        if stage < groups:
            live[stage] = next(steps[stage])
        arrived = {g: lax.ppermute(payload, axis, pairs) for g, (payload, pairs) in live.items()}
        tied = (arrived, made)
        if stage in riders:
            tied, carried[stage] = lax.optimization_barrier((tied, riders[stage](live[0][0])))
        else:
            tied = lax.optimization_barrier(tied)
        arrived, made = tied
        if stage == 0:
            for g in range(1, groups):
                steps[g] = paired_steps(totals_of(g * size, size, arrived[0]), axis)
        following = {}
        for g, value in arrived.items():
            try:
                following[g] = steps[g].send(value)
            except StopIteration as finished:
                made = made + [emit(g * size, size, finished.value)]
        live = following
        stage += 1
    return made, carried


def window(source, step_beam, step_cross, step_depth):
    return source[
        ...,
        1 + step_beam : source.shape[-3] - 1 + step_beam,
        1 + step_cross : source.shape[-2] - 1 + step_cross,
        1 + step_depth : source.shape[-1] - 1 + step_depth,
    ]


def advance(
    bordered, rubidium_number_amount, spin_ratio, heating, drift_speed, fluid_occupied_sites
):
    center = window(bordered, 0, 0, 0)
    complete_heat_ratio = bordered[1] + boundary_kelvin
    coefficients = jnp.stack(
        [xenon_diffusion * complete_heat_ratio**1.5, conduction * complete_heat_ratio**0.7]
    )
    coeff_center = window(coefficients, 0, 0, 0)
    diffused = jnp.zeros_like(center)
    for step_beam, step_cross, step_depth in neighbor_offsets:
        neighbor = window(bordered, step_beam, step_cross, step_depth)
        face_coeff = 0.5 * (coeff_center + window(coefficients, step_beam, step_cross, step_depth))
        diffused = diffused + face_coeff * (neighbor - center)
    upstream = window(bordered, -1, 0, 0)
    transport = diffused - drift_speed * (center - upstream)
    xenon_new = (
        center[0]
        + transport[0]
        + exchange_rate * rubidium_number_amount * (spin_ratio - center[0])
        - xenon_relax * center[0]
    )
    deviation = center[1] + transport[1] + heat_gain * heating - cooling * center[1]
    return jnp.stack([xenon_new * fluid_occupied_sites, deviation * fluid_occupied_sites])


def local(
    xenon_spin_polarization,
    heat_ratio,
    rubidium_polarization_old,
    earlier_spectral_power,
    entry_spectral_power,
    spectral_attenuation_section,
    flow_rate_forward,
    solid_pillar_flags,
):
    rows = earlier_spectral_power.shape[1]
    total_rows = rows * lax.axis_size("beam")
    physical_quantities = jnp.stack([xenon_spin_polarization, heat_ratio - boundary_kelvin])
    glass_cells = solid_pillar_flags.astype(jnp.float32)[:, :, None]
    fluid_occupied_sites = 1.0 - glass_cells
    rubidium_number_amount = fluid_occupied_sites * jnp.exp(
        rubidium_amount_slope * (rubidium_amount_center - 1.0 / heat_ratio)
    )
    absorber = (
        absorb_scale / total_rows * rubidium_number_amount * (1.0 - rubidium_polarization_old)
    )
    glass_term = glass_depth * glass_cells

    def depth_of(start, size):
        weight = spectral_attenuation_section[start : start + size, None, None, None] / (
            1.0 + earlier_spectral_power[start : start + size].astype(jnp.float32) / saturation
        )
        return absorber[None] * weight + glass_term[None], weight

    computed = {}

    def totals_of(start, size, after):
        if after is None:
            earlier, absorbed = lax.optimization_barrier(
                (earlier_spectral_power[start : start + size], absorber)
            )
            weight = spectral_attenuation_section[start : start + size, None, None, None] / (
                1.0 + earlier.astype(jnp.float32) / saturation
            )
            return jnp.sum(absorbed[None] * weight + glass_term[None], axis=1)
        earlier, absorbed, _ = lax.optimization_barrier((earlier_spectral_power, absorber, after))
        weight = spectral_attenuation_section[start : start + size, None, None, None] / (
            1.0 + earlier[start : start + size].astype(jnp.float32) / saturation
        )
        optical_depth = absorbed[None] * weight + glass_term[None]
        computed[start] = optical_depth, weight
        return jnp.sum(optical_depth, axis=1)

    def emit(start, size, earlier):
        optical_depth, weight = computed[start] if start in computed else depth_of(start, size)
        local_column = jnp.pad(
            jnp.cumsum(optical_depth[:, : rows - 1], axis=1), ((0, 0), (1, 0), (0, 0), (0, 0))
        )
        column = earlier[:, None] + local_column
        radiance = entry_spectral_power[start : start + size, None] * jnp.exp(-column)
        return (
            radiance.astype(jnp.bfloat16),
            jnp.sum(weight * radiance, axis=0),
            jnp.sum(radiance * (1.0 - jnp.exp(-optical_depth)), axis=0),
        )

    def tied_faces(faces):
        def exchange(after):
            fields = physical_quantities
            if after is not None:
                fields, _ = lax.optimization_barrier((fields, after))
            return faces(fields)

        return exchange

    lines = earlier_spectral_power.shape[0]
    made, first_faces = pipelined_scan(
        totals_of, emit, lines, "beam", {2: tied_faces(beam_faces), 3: tied_faces(cross_faces)}
    )
    first_bordered = bordered_fields(physical_quantities, first_faces[2], first_faces[3])
    spectral_power = jnp.zeros(earlier_spectral_power.shape, jnp.bfloat16)
    start = 0
    for part, _, _ in made:
        spectral_power = lax.dynamic_update_slice_in_dim(spectral_power, part, start, axis=0)
        start += part.shape[0]
    pumping = made[0][1]
    heating = made[0][2]
    for _, part_pumping, part_heating in made[1:]:
        pumping = pumping + part_pumping
        heating = heating + part_heating
    pumping = pump_scale * pumping
    spin_ratio = pumping / (pumping + spin_decay * (1.0 + rubidium_number_amount))
    rubidium_polarization_new = fluid_occupied_sites * spin_ratio
    drift_speed = flow_scale * flow_rate_forward
    for substep in range(SUBSTEPS):
        bordered = first_bordered if substep == 0 else bordered_fields(physical_quantities)
        physical_quantities = advance(
            bordered, rubidium_number_amount, spin_ratio, heating, drift_speed, fluid_occupied_sites
        )
    return (
        spectral_power,
        physical_quantities[0],
        physical_quantities[1] + boundary_kelvin,
        rubidium_polarization_new,
    )


def solution(mesh):
    in_specs = (
        P("beam", "cross", None),
        P("beam", "cross", None),
        P("beam", "cross", None),
        P(None, "beam", "cross", None),
        P(None, "cross", None),
        P(),
        P("cross", None),
        P("beam", "cross"),
    )
    out_specs = (
        P(None, "beam", "cross", None),
        P("beam", "cross", None),
        P("beam", "cross", None),
        P("beam", "cross", None),
    )
    return jax.shard_map(local, mesh=mesh, in_specs=in_specs, out_specs=out_specs, check_vma=False)
```

```python
import jax
import jax.numpy as jnp
from jax import lax
from jax.sharding import PartitionSpec as P

SUBSTEPS = 2


rubidium_amount_slope = 23.25
rubidium_amount_center = 0.95
absorb_scale = 1.0
glass_depth = 0.07
saturation = 1.0
pump_scale = 0.015625
spin_decay = 0.5
exchange_rate = 0.05
xenon_relax = 0.02
heat_gain = 0.05
cooling = 0.02
xenon_diffusion = 0.09
conduction = 0.09
flow_scale = 0.2
boundary_kelvin = 1.0
neighbor_offsets = ((1, 0, 0), (-1, 0, 0), (0, 1, 0), (0, -1, 0), (0, 0, 1), (0, 0, -1))


def shifted(block, axis, shift):
    count = lax.axis_size(axis)
    if shift > 0:
        pairs = [(i, i + shift) for i in range(count - shift)]
    else:
        pairs = [(i - shift, i) for i in range(count + shift)]
    return lax.ppermute(block, axis, pairs)


def beam_faces(block):
    rows = block.shape[1]
    return shifted(block[:, rows - 1 :], "beam", 1), shifted(block[:, :1], "beam", -1)


def cross_faces(block):
    columns = block.shape[2]
    return shifted(block[:, :, columns - 1 :], "cross", 1), shifted(block[:, :, :1], "cross", -1)


def bordered_fields(block, beam=None, cross=None):
    low_beam, high_beam = beam_faces(block) if beam is None else beam
    low_cross, high_cross = cross_faces(block) if cross is None else cross
    middle = jnp.concatenate([low_cross, block, high_cross], axis=2)
    zeros = jnp.zeros_like(low_beam[:, :, :1])
    low_beam = jnp.concatenate([zeros, low_beam, zeros], axis=2)
    high_beam = jnp.concatenate([zeros, high_beam, zeros], axis=2)
    bordered = jnp.concatenate([low_beam, middle, high_beam], axis=1)
    return jnp.pad(bordered, ((0, 0), (0, 0), (0, 0), (1, 1)))


def exclusive_scan(totals, axis, stride=1):
    count = lax.axis_size(axis) // stride
    if count == 1:
        return jnp.zeros_like(totals)
    before = shifted(totals, axis, stride)
    through = totals + before
    step = 2
    while step < count:
        arrived = shifted(through, axis, step * stride)
        before = before + arrived
        step *= 2
        if step < count:
            through = through + arrived
    return before


def paired_steps(totals, axis):
    count = lax.axis_size(axis)
    half = totals.shape[0] // 2
    is_low = lax.axis_index(axis) % 2 == 0
    first, second = totals[:half], totals[half:]
    mine = jnp.where(is_low, first, second)
    swap = [(i, i ^ 1) for i in range(count)]
    got = yield jnp.where(is_low, second, first), swap
    pair_total = mine + got
    pairs = count // 2
    before = yield pair_total, shift_pairs(count, 2)
    through = pair_total + before
    step = 2
    while step < pairs:
        arrived = yield through, shift_pairs(count, 2 * step)
        before = before + arrived
        step *= 2
        if step < pairs:
            through = through + arrived
    back = yield jnp.where(is_low, before + mine, before), swap
    return jnp.where(
        is_low, jnp.concatenate([before, back]), jnp.concatenate([back, before + got])
    )


def shift_pairs(count, shift):
    return [(i, i + shift) for i in range(count - shift)]


def pipelined(count, lines, groups=2):
    return count % 2 == 0 and count > 2 and lines % (2 * groups) == 0


def pipelined_scan(totals_of, emit, lines, axis, riders, passenger, groups=2):
    count = lax.axis_size(axis)
    if not pipelined(count, lines, groups):
        earlier = exclusive_scan(totals_of(0, lines, None), axis)
        carried = {stage: rider(None) for stage, rider in riders.items()}
        return [emit(0, lines, earlier)], carried, None
    size = lines // groups
    steps = [None] * groups
    steps[0] = paired_steps(totals_of(0, size, None), axis)
    live, made, carried, stage = {}, [], {}, 0
    while stage < groups or live:
        if stage < groups:
            live[stage] = next(steps[stage])
        sent = dict(live)
        if stage == 0:
            payload, pairs = live[0]
            rides = passenger.reshape((-1,) + payload.shape[1:])
            sent[0] = jnp.concatenate([payload, rides]), pairs
        arrived = {g: lax.ppermute(payload, axis, pairs) for g, (payload, pairs) in sent.items()}
        if stage == 0:
            held = live[0][0].shape[0]
            passenger = arrived[0][held:].reshape(passenger.shape)
            arrived[0] = arrived[0][:held]
        if stage == 0:
            for g in range(1, groups):
                steps[g] = paired_steps(totals_of(g * size, size, live[0][0]), axis)
        tied = (arrived, made)
        if stage in riders:
            tied, carried[stage] = lax.optimization_barrier((tied, riders[stage](live[0][0])))
        else:
            tied = lax.optimization_barrier(tied)
        arrived, made = tied
        following = {}
        for g, value in arrived.items():
            try:
                following[g] = steps[g].send(value)
            except StopIteration as finished:
                made = made + [emit(g * size, size, finished.value)]
        live = following
        stage += 1
    return made, carried, passenger


def window(source, step_beam, step_cross, step_depth):
    return source[
        ...,
        1 + step_beam : source.shape[-3] - 1 + step_beam,
        1 + step_cross : source.shape[-2] - 1 + step_cross,
        1 + step_depth : source.shape[-1] - 1 + step_depth,
    ]


def advance(
    bordered, rubidium_number_amount, spin_ratio, heating, drift_speed, fluid_occupied_sites
):
    center = window(bordered, 0, 0, 0)
    complete_heat_ratio = bordered[1] + boundary_kelvin
    coefficients = jnp.stack(
        [xenon_diffusion * complete_heat_ratio**1.5, conduction * complete_heat_ratio**0.7]
    )
    coeff_center = window(coefficients, 0, 0, 0)
    diffused = jnp.zeros_like(center)
    for step_beam, step_cross, step_depth in neighbor_offsets:
        neighbor = window(bordered, step_beam, step_cross, step_depth)
        face_coeff = 0.5 * (coeff_center + window(coefficients, step_beam, step_cross, step_depth))
        diffused = diffused + face_coeff * (neighbor - center)
    upstream = window(bordered, -1, 0, 0)
    transport = diffused - drift_speed * (center - upstream)
    xenon_new = (
        center[0]
        + transport[0]
        + exchange_rate * rubidium_number_amount * (spin_ratio - center[0])
        - xenon_relax * center[0]
    )
    deviation = center[1] + transport[1] + heat_gain * heating - cooling * center[1]
    return jnp.stack([xenon_new * fluid_occupied_sites, deviation * fluid_occupied_sites])


def local(
    xenon_spin_polarization,
    heat_ratio,
    rubidium_polarization_old,
    earlier_spectral_power,
    entry_spectral_power,
    spectral_attenuation_section,
    flow_rate_forward,
    solid_pillar_flags,
):
    rows = earlier_spectral_power.shape[1]
    total_rows = rows * lax.axis_size("beam")
    physical_quantities = jnp.stack([xenon_spin_polarization, heat_ratio - boundary_kelvin])
    glass_cells = solid_pillar_flags.astype(jnp.float32)[:, :, None]
    fluid_occupied_sites = 1.0 - glass_cells
    rubidium_number_amount = fluid_occupied_sites * jnp.exp(
        rubidium_amount_slope * (rubidium_amount_center - 1.0 / heat_ratio)
    )
    absorber = (
        absorb_scale / total_rows * rubidium_number_amount * (1.0 - rubidium_polarization_old)
    )
    glass_term = glass_depth * glass_cells

    def depth_of(start, size):
        weight = spectral_attenuation_section[start : start + size, None, None, None] / (
            1.0 + earlier_spectral_power[start : start + size].astype(jnp.float32) / saturation
        )
        return absorber[None] * weight + glass_term[None], weight

    def totals_of(start, size, after):
        optical_depth, _ = depth_of(start, size)
        if after is not None:
            optical_depth, _ = lax.optimization_barrier((optical_depth, after))
        return jnp.sum(optical_depth, axis=1)

    def emit(start, size, earlier):
        optical_depth, weight = depth_of(start, size)
        local_column = jnp.pad(
            jnp.cumsum(optical_depth[:, : rows - 1], axis=1), ((0, 0), (1, 0), (0, 0), (0, 0))
        )
        column = earlier[:, None] + local_column
        radiance = entry_spectral_power[start : start + size, None] * jnp.exp(-column)
        return (
            radiance.astype(jnp.bfloat16),
            jnp.sum(weight * radiance, axis=0),
            jnp.sum(radiance * (1.0 - jnp.exp(-optical_depth)), axis=0),
        )

    def tied_faces(faces):
        def exchange(after):
            fields = physical_quantities
            if after is not None:
                fields, _ = lax.optimization_barrier((fields, after))
            return faces(fields)

        return exchange

    lines = earlier_spectral_power.shape[0]
    count = lax.axis_size("beam")
    is_low = lax.axis_index("beam") % 2 == 0
    last, first = physical_quantities[:, rows - 1 :], physical_quantities[:, :1]

    def across_pairs(fields):
        pairs = [(i, i + 1) for i in range(1, count - 1, 2)]
        pairs += [(target, source) for source, target in pairs]
        rows_now = fields.shape[1]
        sent = jnp.where(is_low, fields[:, :1], fields[:, rows_now - 1 :])
        return lax.ppermute(sent, "beam", pairs)

    paired = pipelined(count, lines)
    beam_rider = tied_faces(across_pairs if paired else beam_faces)
    made, first_faces, partner_face = pipelined_scan(
        totals_of,
        emit,
        lines,
        "beam",
        {2: beam_rider, 3: tied_faces(cross_faces)},
        jnp.where(is_low, last, first),
    )
    if paired:
        across = first_faces[2]
        beam = (jnp.where(is_low, across, partner_face), jnp.where(is_low, partner_face, across))
    else:
        beam = first_faces[2]
    first_bordered = bordered_fields(physical_quantities, beam, first_faces[3])
    spectral_power = jnp.zeros(earlier_spectral_power.shape, jnp.bfloat16)
    start = 0
    for part, _, _ in made:
        spectral_power = lax.dynamic_update_slice_in_dim(spectral_power, part, start, axis=0)
        start += part.shape[0]
    pumping = made[0][1]
    heating = made[0][2]
    for _, part_pumping, part_heating in made[1:]:
        pumping = pumping + part_pumping
        heating = heating + part_heating
    pumping = pump_scale * pumping
    spin_ratio = pumping / (pumping + spin_decay * (1.0 + rubidium_number_amount))
    rubidium_polarization_new = fluid_occupied_sites * spin_ratio
    drift_speed = flow_scale * flow_rate_forward
    for substep in range(SUBSTEPS):
        bordered = first_bordered if substep == 0 else bordered_fields(physical_quantities)
        physical_quantities = advance(
            bordered, rubidium_number_amount, spin_ratio, heating, drift_speed, fluid_occupied_sites
        )
    return (
        spectral_power,
        physical_quantities[0],
        physical_quantities[1] + boundary_kelvin,
        rubidium_polarization_new,
    )


def solution(mesh):
    in_specs = (
        P("beam", "cross", None),
        P("beam", "cross", None),
        P("beam", "cross", None),
        P(None, "beam", "cross", None),
        P(None, "cross", None),
        P(),
        P("cross", None),
        P("beam", "cross"),
    )
    out_specs = (
        P(None, "beam", "cross", None),
        P("beam", "cross", None),
        P("beam", "cross", None),
        P("beam", "cross", None),
    )
    return jax.shard_map(local, mesh=mesh, in_specs=in_specs, out_specs=out_specs, check_vma=False)
```

```python
import jax
import jax.numpy as jnp
from jax import lax
from jax.sharding import PartitionSpec as P

SUBSTEPS = 2


rubidium_amount_slope = 23.25
rubidium_amount_center = 0.95
absorb_scale = 1.0
glass_depth = 0.07
saturation = 1.0
pump_scale = 0.015625
spin_decay = 0.5
exchange_rate = 0.05
xenon_relax = 0.02
heat_gain = 0.05
cooling = 0.02
xenon_diffusion = 0.09
conduction = 0.09
flow_scale = 0.2
boundary_kelvin = 1.0
neighbor_offsets = ((1, 0, 0), (-1, 0, 0), (0, 1, 0), (0, -1, 0), (0, 0, 1), (0, 0, -1))


def shifted(block, axis, shift):
    count = lax.axis_size(axis)
    if shift > 0:
        pairs = [(i, i + shift) for i in range(count - shift)]
    else:
        pairs = [(i - shift, i) for i in range(count + shift)]
    return lax.ppermute(block, axis, pairs)


def beam_faces(block):
    rows = block.shape[1]
    return shifted(block[:, rows - 1 :], "beam", 1), shifted(block[:, :1], "beam", -1)


def cross_faces(block):
    columns = block.shape[2]
    return shifted(block[:, :, columns - 1 :], "cross", 1), shifted(block[:, :, :1], "cross", -1)


def bordered_fields(block, beam=None, cross=None):
    low_beam, high_beam = beam_faces(block) if beam is None else beam
    low_cross, high_cross = cross_faces(block) if cross is None else cross
    middle = jnp.concatenate([low_cross, block, high_cross], axis=2)
    zeros = jnp.zeros_like(low_beam[:, :, :1])
    low_beam = jnp.concatenate([zeros, low_beam, zeros], axis=2)
    high_beam = jnp.concatenate([zeros, high_beam, zeros], axis=2)
    bordered = jnp.concatenate([low_beam, middle, high_beam], axis=1)
    return jnp.pad(bordered, ((0, 0), (0, 0), (0, 0), (1, 1)))


def exclusive_scan(totals, axis, stride=1):
    count = lax.axis_size(axis) // stride
    if count == 1:
        return jnp.zeros_like(totals)
    before = shifted(totals, axis, stride)
    through = totals + before
    step = 2
    while step < count:
        arrived = shifted(through, axis, step * stride)
        before = before + arrived
        step *= 2
        if step < count:
            through = through + arrived
    return before


def paired_steps(totals, axis):
    count = lax.axis_size(axis)
    half = totals.shape[0] // 2
    is_low = lax.axis_index(axis) % 2 == 0
    first, second = totals[:half], totals[half:]
    mine = jnp.where(is_low, first, second)
    swap = [(i, i ^ 1) for i in range(count)]
    got = yield jnp.where(is_low, second, first), swap
    pair_total = mine + got
    pairs = count // 2
    before = yield pair_total, shift_pairs(count, 2)
    through = pair_total + before
    step = 2
    while step < pairs:
        arrived = yield through, shift_pairs(count, 2 * step)
        before = before + arrived
        step *= 2
        if step < pairs:
            through = through + arrived
    back = yield jnp.where(is_low, before + mine, before), swap
    return jnp.where(
        is_low, jnp.concatenate([before, back]), jnp.concatenate([back, before + got])
    )


def shift_pairs(count, shift):
    return [(i, i + shift) for i in range(count - shift)]


def pipelined_scan(totals_of, emit, lines, axis, riders, groups=2):
    count = lax.axis_size(axis)
    if count % 2 or count <= 2 or lines % (2 * groups):
        earlier = exclusive_scan(totals_of(0, lines, None), axis)
        return [emit(0, lines, earlier)], {stage: rider(None) for stage, rider in riders.items()}
    size = lines // groups
    steps = [None] * groups
    steps[0] = paired_steps(totals_of(0, size, None), axis)
    live, made, carried, stage = {}, [], {}, 0
    while stage < groups or live:
        if stage < groups:
            live[stage] = next(steps[stage])
        arrived = {g: lax.ppermute(payload, axis, pairs) for g, (payload, pairs) in live.items()}
        if stage == 0:
            for g in range(1, groups):
                steps[g] = paired_steps(totals_of(g * size, size, live[0][0]), axis)
        tied = (arrived, made)
        if stage in riders:
            tied, carried[stage] = lax.optimization_barrier((tied, riders[stage](live[0][0])))
        else:
            tied = lax.optimization_barrier(tied)
        arrived, made = tied
        following = {}
        for g, value in arrived.items():
            try:
                following[g] = steps[g].send(value)
            except StopIteration as finished:
                made = made + [emit(g * size, size, finished.value)]
        live = following
        stage += 1
    return made, carried


def window(source, step_beam, step_cross, step_depth):
    return source[
        ...,
        1 + step_beam : source.shape[-3] - 1 + step_beam,
        1 + step_cross : source.shape[-2] - 1 + step_cross,
        1 + step_depth : source.shape[-1] - 1 + step_depth,
    ]


def advance(
    bordered, rubidium_number_amount, spin_ratio, heating, drift_speed, fluid_occupied_sites
):
    center = window(bordered, 0, 0, 0)
    complete_heat_ratio = bordered[1] + boundary_kelvin
    coefficients = jnp.stack(
        [xenon_diffusion * complete_heat_ratio**1.5, conduction * complete_heat_ratio**0.7]
    )
    coeff_center = window(coefficients, 0, 0, 0)
    diffused = jnp.zeros_like(center)
    for step_beam, step_cross, step_depth in neighbor_offsets:
        neighbor = window(bordered, step_beam, step_cross, step_depth)
        face_coeff = 0.5 * (coeff_center + window(coefficients, step_beam, step_cross, step_depth))
        diffused = diffused + face_coeff * (neighbor - center)
    upstream = window(bordered, -1, 0, 0)
    transport = diffused - drift_speed * (center - upstream)
    xenon_new = (
        center[0]
        + transport[0]
        + exchange_rate * rubidium_number_amount * (spin_ratio - center[0])
        - xenon_relax * center[0]
    )
    deviation = center[1] + transport[1] + heat_gain * heating - cooling * center[1]
    return jnp.stack([xenon_new * fluid_occupied_sites, deviation * fluid_occupied_sites])


def local(
    xenon_spin_polarization,
    heat_ratio,
    rubidium_polarization_old,
    earlier_spectral_power,
    entry_spectral_power,
    spectral_attenuation_section,
    flow_rate_forward,
    solid_pillar_flags,
):
    rows = earlier_spectral_power.shape[1]
    total_rows = rows * lax.axis_size("beam")
    physical_quantities = jnp.stack([xenon_spin_polarization, heat_ratio - boundary_kelvin])
    glass_cells = solid_pillar_flags.astype(jnp.float32)[:, :, None]
    fluid_occupied_sites = 1.0 - glass_cells
    rubidium_number_amount = fluid_occupied_sites * jnp.exp(
        rubidium_amount_slope * (rubidium_amount_center - 1.0 / heat_ratio)
    )
    absorber = (
        absorb_scale / total_rows * rubidium_number_amount * (1.0 - rubidium_polarization_old)
    )
    glass_term = glass_depth * glass_cells

    def depth_of(start, size):
        weight = spectral_attenuation_section[start : start + size, None, None, None] / (
            1.0 + earlier_spectral_power[start : start + size].astype(jnp.float32) / saturation
        )
        return absorber[None] * weight + glass_term[None], weight

    def totals_of(start, size, after):
        optical_depth, _ = depth_of(start, size)
        if after is not None:
            optical_depth, _ = lax.optimization_barrier((optical_depth, after))
        return jnp.sum(optical_depth, axis=1)

    def emit(start, size, earlier):
        optical_depth, weight = depth_of(start, size)
        local_column = jnp.pad(
            jnp.cumsum(optical_depth[:, : rows - 1], axis=1), ((0, 0), (1, 0), (0, 0), (0, 0))
        )
        column = earlier[:, None] + local_column
        radiance = entry_spectral_power[start : start + size, None] * jnp.exp(-column)
        return (
            radiance.astype(jnp.bfloat16),
            jnp.sum(weight * radiance, axis=0),
            jnp.sum(radiance * (1.0 - jnp.exp(-optical_depth)), axis=0),
        )

    def tied_faces(faces):
        def exchange(after):
            fields = physical_quantities
            if after is not None:
                fields, _ = lax.optimization_barrier((fields, after))
            return faces(fields)

        return exchange

    lines = earlier_spectral_power.shape[0]
    made, first_faces = pipelined_scan(
        totals_of, emit, lines, "beam", {1: tied_faces(cross_faces), 2: tied_faces(beam_faces)}
    )
    first_bordered = bordered_fields(physical_quantities, first_faces[2], first_faces[1])
    spectral_power = jnp.zeros(earlier_spectral_power.shape, jnp.bfloat16)
    start = 0
    for part, _, _ in made:
        spectral_power = lax.dynamic_update_slice_in_dim(spectral_power, part, start, axis=0)
        start += part.shape[0]
    pumping = made[0][1]
    heating = made[0][2]
    for _, part_pumping, part_heating in made[1:]:
        pumping = pumping + part_pumping
        heating = heating + part_heating
    pumping = pump_scale * pumping
    spin_ratio = pumping / (pumping + spin_decay * (1.0 + rubidium_number_amount))
    rubidium_polarization_new = fluid_occupied_sites * spin_ratio
    drift_speed = flow_scale * flow_rate_forward
    for substep in range(SUBSTEPS):
        bordered = first_bordered if substep == 0 else bordered_fields(physical_quantities)
        physical_quantities = advance(
            bordered, rubidium_number_amount, spin_ratio, heating, drift_speed, fluid_occupied_sites
        )
    return (
        spectral_power,
        physical_quantities[0],
        physical_quantities[1] + boundary_kelvin,
        rubidium_polarization_new,
    )


def solution(mesh):
    in_specs = (
        P("beam", "cross", None),
        P("beam", "cross", None),
        P("beam", "cross", None),
        P(None, "beam", "cross", None),
        P(None, "cross", None),
        P(),
        P("cross", None),
        P("beam", "cross"),
    )
    out_specs = (
        P(None, "beam", "cross", None),
        P("beam", "cross", None),
        P("beam", "cross", None),
        P("beam", "cross", None),
    )
    return jax.shard_map(local, mesh=mesh, in_specs=in_specs, out_specs=out_specs, check_vma=False)
```

```python
import jax
import jax.numpy as jnp
from jax import lax
from jax.sharding import PartitionSpec as P

SUBSTEPS = 2


rubidium_amount_slope = 23.25
rubidium_amount_center = 0.95
absorb_scale = 1.0
glass_depth = 0.07
saturation = 1.0
pump_scale = 0.015625
spin_decay = 0.5
exchange_rate = 0.05
xenon_relax = 0.02
heat_gain = 0.05
cooling = 0.02
xenon_diffusion = 0.09
conduction = 0.09
flow_scale = 0.2
boundary_kelvin = 1.0
neighbor_offsets = ((1, 0, 0), (-1, 0, 0), (0, 1, 0), (0, -1, 0), (0, 0, 1), (0, 0, -1))


def shifted(block, axis, shift):
    count = lax.axis_size(axis)
    if shift > 0:
        pairs = [(i, i + shift) for i in range(count - shift)]
    else:
        pairs = [(i - shift, i) for i in range(count + shift)]
    return lax.ppermute(block, axis, pairs)


def beam_faces(block):
    rows = block.shape[1]
    return shifted(block[:, rows - 1 :], "beam", 1), shifted(block[:, :1], "beam", -1)


def cross_faces(block):
    columns = block.shape[2]
    return shifted(block[:, :, columns - 1 :], "cross", 1), shifted(block[:, :, :1], "cross", -1)


def bordered_fields(block, beam=None, cross=None):
    low_beam, high_beam = beam_faces(block) if beam is None else beam
    low_cross, high_cross = cross_faces(block) if cross is None else cross
    middle = jnp.concatenate([low_cross, block, high_cross], axis=2)
    zeros = jnp.zeros_like(low_beam[:, :, :1])
    low_beam = jnp.concatenate([zeros, low_beam, zeros], axis=2)
    high_beam = jnp.concatenate([zeros, high_beam, zeros], axis=2)
    bordered = jnp.concatenate([low_beam, middle, high_beam], axis=1)
    return jnp.pad(bordered, ((0, 0), (0, 0), (0, 0), (1, 1)))


def exclusive_scan(totals, axis, stride=1):
    count = lax.axis_size(axis) // stride
    if count == 1:
        return jnp.zeros_like(totals)
    before = shifted(totals, axis, stride)
    through = totals + before
    step = 2
    while step < count:
        arrived = shifted(through, axis, step * stride)
        before = before + arrived
        step *= 2
        if step < count:
            through = through + arrived
    return before


def paired_steps(totals, axis):
    count = lax.axis_size(axis)
    half = totals.shape[0] // 2
    is_low = lax.axis_index(axis) % 2 == 0
    first, second = totals[:half], totals[half:]
    mine = jnp.where(is_low, first, second)
    swap = [(i, i ^ 1) for i in range(count)]
    got = yield jnp.where(is_low, second, first), swap
    pair_total = mine + got
    pairs = count // 2
    before = yield pair_total, shift_pairs(count, 2)
    through = pair_total + before
    step = 2
    while step < pairs:
        arrived = yield through, shift_pairs(count, 2 * step)
        before = before + arrived
        step *= 2
        if step < pairs:
            through = through + arrived
    back = yield jnp.where(is_low, before + mine, before), swap
    return jnp.where(
        is_low, jnp.concatenate([before, back]), jnp.concatenate([back, before + got])
    )


def shift_pairs(count, shift):
    return [(i, i + shift) for i in range(count - shift)]


def pipelined_scan(totals_of, emit, lines, axis, riders, groups=2):
    count = lax.axis_size(axis)
    if count % 2 or count <= 2 or lines % (2 * groups):
        earlier = exclusive_scan(totals_of(0, lines, None), axis)
        return [emit(0, lines, earlier)], {stage: rider(None) for stage, rider in riders.items()}
    size = lines // groups
    steps = [None] * groups
    steps[0] = paired_steps(totals_of(0, size, None), axis)
    live, made, carried, in_flight, stage = {}, [], {}, {}, 0
    while stage < groups or live:
        if stage < groups:
            live[stage] = next(steps[stage])
        arrived = {g: lax.ppermute(payload, axis, pairs) for g, (payload, pairs) in live.items()}
        if stage == 0:
            for g in range(1, groups):
                steps[g] = paired_steps(totals_of(g * size, size, live[0][0]), axis)
        issued = riders[stage](live[0][0]) if stage in riders else None
        arrived, made, landed = lax.optimization_barrier((arrived, made, in_flight))
        carried.update(landed)
        in_flight = {} if issued is None else {stage: issued}
        following = {}
        for g, value in arrived.items():
            try:
                following[g] = steps[g].send(value)
            except StopIteration as finished:
                made = made + [emit(g * size, size, finished.value)]
        live = following
        stage += 1
    carried.update(in_flight)
    return made, carried


def window(source, step_beam, step_cross, step_depth):
    return source[
        ...,
        1 + step_beam : source.shape[-3] - 1 + step_beam,
        1 + step_cross : source.shape[-2] - 1 + step_cross,
        1 + step_depth : source.shape[-1] - 1 + step_depth,
    ]


def advance(
    bordered, rubidium_number_amount, spin_ratio, heating, drift_speed, fluid_occupied_sites
):
    center = window(bordered, 0, 0, 0)
    complete_heat_ratio = bordered[1] + boundary_kelvin
    coefficients = jnp.stack(
        [xenon_diffusion * complete_heat_ratio**1.5, conduction * complete_heat_ratio**0.7]
    )
    coeff_center = window(coefficients, 0, 0, 0)
    diffused = jnp.zeros_like(center)
    for step_beam, step_cross, step_depth in neighbor_offsets:
        neighbor = window(bordered, step_beam, step_cross, step_depth)
        face_coeff = 0.5 * (coeff_center + window(coefficients, step_beam, step_cross, step_depth))
        diffused = diffused + face_coeff * (neighbor - center)
    upstream = window(bordered, -1, 0, 0)
    transport = diffused - drift_speed * (center - upstream)
    xenon_new = (
        center[0]
        + transport[0]
        + exchange_rate * rubidium_number_amount * (spin_ratio - center[0])
        - xenon_relax * center[0]
    )
    deviation = center[1] + transport[1] + heat_gain * heating - cooling * center[1]
    return jnp.stack([xenon_new * fluid_occupied_sites, deviation * fluid_occupied_sites])


def local(
    xenon_spin_polarization,
    heat_ratio,
    rubidium_polarization_old,
    earlier_spectral_power,
    entry_spectral_power,
    spectral_attenuation_section,
    flow_rate_forward,
    solid_pillar_flags,
):
    rows = earlier_spectral_power.shape[1]
    total_rows = rows * lax.axis_size("beam")
    physical_quantities = jnp.stack([xenon_spin_polarization, heat_ratio - boundary_kelvin])
    glass_cells = solid_pillar_flags.astype(jnp.float32)[:, :, None]
    fluid_occupied_sites = 1.0 - glass_cells
    rubidium_number_amount = fluid_occupied_sites * jnp.exp(
        rubidium_amount_slope * (rubidium_amount_center - 1.0 / heat_ratio)
    )
    absorber = (
        absorb_scale / total_rows * rubidium_number_amount * (1.0 - rubidium_polarization_old)
    )
    glass_term = glass_depth * glass_cells

    def depth_of(start, size):
        weight = spectral_attenuation_section[start : start + size, None, None, None] / (
            1.0 + earlier_spectral_power[start : start + size].astype(jnp.float32) / saturation
        )
        return absorber[None] * weight + glass_term[None], weight

    def totals_of(start, size, after):
        optical_depth, _ = depth_of(start, size)
        if after is not None:
            optical_depth, _ = lax.optimization_barrier((optical_depth, after))
        return jnp.sum(optical_depth, axis=1)

    def emit(start, size, earlier):
        optical_depth, weight = depth_of(start, size)
        local_column = jnp.pad(
            jnp.cumsum(optical_depth[:, : rows - 1], axis=1), ((0, 0), (1, 0), (0, 0), (0, 0))
        )
        column = earlier[:, None] + local_column
        radiance = entry_spectral_power[start : start + size, None] * jnp.exp(-column)
        return (
            radiance.astype(jnp.bfloat16),
            jnp.sum(weight * radiance, axis=0),
            jnp.sum(radiance * (1.0 - jnp.exp(-optical_depth)), axis=0),
        )

    def tied_faces(faces):
        def exchange(after):
            fields = physical_quantities
            if after is not None:
                fields, _ = lax.optimization_barrier((fields, after))
            return faces(fields)

        return exchange

    lines = earlier_spectral_power.shape[0]
    made, first_faces = pipelined_scan(
        totals_of, emit, lines, "beam", {2: tied_faces(beam_faces), 3: tied_faces(cross_faces)}
    )
    first_bordered = bordered_fields(physical_quantities, first_faces[2], first_faces[3])
    spectral_power = jnp.zeros(earlier_spectral_power.shape, jnp.bfloat16)
    start = 0
    for part, _, _ in made:
        spectral_power = lax.dynamic_update_slice_in_dim(spectral_power, part, start, axis=0)
        start += part.shape[0]
    pumping = made[0][1]
    heating = made[0][2]
    for _, part_pumping, part_heating in made[1:]:
        pumping = pumping + part_pumping
        heating = heating + part_heating
    pumping = pump_scale * pumping
    spin_ratio = pumping / (pumping + spin_decay * (1.0 + rubidium_number_amount))
    rubidium_polarization_new = fluid_occupied_sites * spin_ratio
    drift_speed = flow_scale * flow_rate_forward
    for substep in range(SUBSTEPS):
        bordered = first_bordered if substep == 0 else bordered_fields(physical_quantities)
        physical_quantities = advance(
            bordered, rubidium_number_amount, spin_ratio, heating, drift_speed, fluid_occupied_sites
        )
    return (
        spectral_power,
        physical_quantities[0],
        physical_quantities[1] + boundary_kelvin,
        rubidium_polarization_new,
    )


def solution(mesh):
    in_specs = (
        P("beam", "cross", None),
        P("beam", "cross", None),
        P("beam", "cross", None),
        P(None, "beam", "cross", None),
        P(None, "cross", None),
        P(),
        P("cross", None),
        P("beam", "cross"),
    )
    out_specs = (
        P(None, "beam", "cross", None),
        P("beam", "cross", None),
        P("beam", "cross", None),
        P("beam", "cross", None),
    )
    return jax.shard_map(local, mesh=mesh, in_specs=in_specs, out_specs=out_specs, check_vma=False)
```

```python
import jax
import jax.numpy as jnp
from jax import lax
from jax.sharding import PartitionSpec as P

SUBSTEPS = 2


rubidium_amount_slope = 23.25
rubidium_amount_center = 0.95
absorb_scale = 1.0
glass_depth = 0.07
saturation = 1.0
pump_scale = 0.015625
spin_decay = 0.5
exchange_rate = 0.05
xenon_relax = 0.02
heat_gain = 0.05
cooling = 0.02
xenon_diffusion = 0.09
conduction = 0.09
flow_scale = 0.2
boundary_kelvin = 1.0
neighbor_offsets = ((1, 0, 0), (-1, 0, 0), (0, 1, 0), (0, -1, 0), (0, 0, 1), (0, 0, -1))


def shifted(block, axis, shift):
    count = lax.axis_size(axis)
    if shift > 0:
        pairs = [(i, i + shift) for i in range(count - shift)]
    else:
        pairs = [(i - shift, i) for i in range(count + shift)]
    return lax.ppermute(block, axis, pairs)


def beam_faces(block):
    rows = block.shape[1]
    return shifted(block[:, rows - 1 :], "beam", 1), shifted(block[:, :1], "beam", -1)


def cross_faces(block):
    columns = block.shape[2]
    return shifted(block[:, :, columns - 1 :], "cross", 1), shifted(block[:, :, :1], "cross", -1)


def bordered_fields(block, beam=None, cross=None):
    low_beam, high_beam = beam_faces(block) if beam is None else beam
    low_cross, high_cross = cross_faces(block) if cross is None else cross
    middle = jnp.concatenate([low_cross, block, high_cross], axis=2)
    zeros = jnp.zeros_like(low_beam[:, :, :1])
    low_beam = jnp.concatenate([zeros, low_beam, zeros], axis=2)
    high_beam = jnp.concatenate([zeros, high_beam, zeros], axis=2)
    bordered = jnp.concatenate([low_beam, middle, high_beam], axis=1)
    return jnp.pad(bordered, ((0, 0), (0, 0), (0, 0), (1, 1)))


def exclusive_scan(totals, axis, stride=1):
    count = lax.axis_size(axis) // stride
    if count == 1:
        return jnp.zeros_like(totals)
    before = shifted(totals, axis, stride)
    through = totals + before
    step = 2
    while step < count:
        arrived = shifted(through, axis, step * stride)
        before = before + arrived
        step *= 2
        if step < count:
            through = through + arrived
    return before


def paired_steps(totals, axis):
    count = lax.axis_size(axis)
    half = totals.shape[0] // 2
    is_low = lax.axis_index(axis) % 2 == 0
    first, second = totals[:half], totals[half:]
    mine = jnp.where(is_low, first, second)
    swap = [(i, i ^ 1) for i in range(count)]
    got = yield jnp.where(is_low, second, first), swap
    pair_total = mine + got
    pairs = count // 2
    before = yield pair_total, shift_pairs(count, 2)
    through = pair_total + before
    step = 2
    while step < pairs:
        arrived = yield through, shift_pairs(count, 2 * step)
        before = before + arrived
        step *= 2
        if step < pairs:
            through = through + arrived
    back = yield jnp.where(is_low, before + mine, before), swap
    return jnp.where(
        is_low, jnp.concatenate([before, back]), jnp.concatenate([back, before + got])
    )


def shift_pairs(count, shift):
    return [(i, i + shift) for i in range(count - shift)]


def pipelined_scan(totals_of, emit, lines, axis, riders, groups=2):
    count = lax.axis_size(axis)
    if count % 2 or count <= 2 or lines % (2 * groups):
        earlier = exclusive_scan(totals_of(0, lines, None), axis)
        return [emit(0, lines, earlier)], {stage: rider(None) for stage, rider in riders.items()}
    size = lines // groups
    steps = [None] * groups
    steps[0] = paired_steps(totals_of(0, size, None), axis)
    live, made, carried, stage = {}, [], {}, 0
    while stage < groups or live:
        if stage < groups:
            live[stage] = next(steps[stage])
        arrived = {g: lax.ppermute(payload, axis, pairs) for g, (payload, pairs) in live.items()}
        if stage == 0:
            for g in range(1, groups):
                steps[g] = paired_steps(totals_of(g * size, size, live[0][0]), axis)
        tied = (arrived, made)
        if stage in riders:
            tied, carried[stage] = lax.optimization_barrier((tied, riders[stage](live[0][0])))
        else:
            tied = lax.optimization_barrier(tied)
        arrived, made = tied
        following = {}
        for g, value in arrived.items():
            try:
                following[g] = steps[g].send(value)
            except StopIteration as finished:
                made = made + [emit(g * size, size, finished.value)]
        live = following
        stage += 1
    return made, carried


def window(source, step_beam, step_cross, step_depth):
    return source[
        ...,
        1 + step_beam : source.shape[-3] - 1 + step_beam,
        1 + step_cross : source.shape[-2] - 1 + step_cross,
        1 + step_depth : source.shape[-1] - 1 + step_depth,
    ]


def advance(
    bordered, rubidium_number_amount, spin_ratio, heating, drift_speed, fluid_occupied_sites
):
    center = window(bordered, 0, 0, 0)
    complete_heat_ratio = bordered[1] + boundary_kelvin
    coefficients = jnp.stack(
        [xenon_diffusion * complete_heat_ratio**1.5, conduction * complete_heat_ratio**0.7]
    )
    coeff_center = window(coefficients, 0, 0, 0)
    diffused = jnp.zeros_like(center)
    for step_beam, step_cross, step_depth in neighbor_offsets:
        neighbor = window(bordered, step_beam, step_cross, step_depth)
        face_coeff = 0.5 * (coeff_center + window(coefficients, step_beam, step_cross, step_depth))
        diffused = diffused + face_coeff * (neighbor - center)
    upstream = window(bordered, -1, 0, 0)
    transport = diffused - drift_speed * (center - upstream)
    xenon_new = (
        center[0]
        + transport[0]
        + exchange_rate * rubidium_number_amount * (spin_ratio - center[0])
        - xenon_relax * center[0]
    )
    deviation = center[1] + transport[1] + heat_gain * heating - cooling * center[1]
    return jnp.stack([xenon_new * fluid_occupied_sites, deviation * fluid_occupied_sites])


def local(
    xenon_spin_polarization,
    heat_ratio,
    rubidium_polarization_old,
    earlier_spectral_power,
    entry_spectral_power,
    spectral_attenuation_section,
    flow_rate_forward,
    solid_pillar_flags,
):
    rows = earlier_spectral_power.shape[1]
    total_rows = rows * lax.axis_size("beam")
    physical_quantities = jnp.stack([xenon_spin_polarization, heat_ratio - boundary_kelvin])
    glass_cells = solid_pillar_flags.astype(jnp.float32)[:, :, None]
    fluid_occupied_sites = 1.0 - glass_cells
    rubidium_number_amount = fluid_occupied_sites * jnp.exp(
        rubidium_amount_slope * (rubidium_amount_center - 1.0 / heat_ratio)
    )
    absorber = (
        absorb_scale / total_rows * rubidium_number_amount * (1.0 - rubidium_polarization_old)
    )
    glass_term = glass_depth * glass_cells

    def depth_of(start, size):
        weight = spectral_attenuation_section[start : start + size, None, None, None] / (
            1.0 + earlier_spectral_power[start : start + size].astype(jnp.float32) / saturation
        )
        return absorber[None] * weight + glass_term[None], weight

    def totals_of(start, size, after):
        optical_depth, _ = depth_of(start, size)
        if after is not None:
            optical_depth, _ = lax.optimization_barrier((optical_depth, after))
        return jnp.sum(optical_depth, axis=1)

    def emit(start, size, earlier):
        optical_depth, weight = depth_of(start, size)
        local_column = jnp.pad(
            jnp.cumsum(optical_depth[:, : rows - 1], axis=1), ((0, 0), (1, 0), (0, 0), (0, 0))
        )
        column = earlier[:, None] + local_column
        radiance = entry_spectral_power[start : start + size, None] * jnp.exp(-column)
        return (
            radiance.astype(jnp.bfloat16),
            jnp.sum(weight * radiance, axis=0),
            jnp.sum(radiance * (1.0 - jnp.exp(-optical_depth)), axis=0),
        )

    def tied_faces(faces):
        def exchange(after):
            fields = physical_quantities
            if after is not None:
                fields, _ = lax.optimization_barrier((fields, after))
            return faces(fields)

        return exchange

    lines = earlier_spectral_power.shape[0]
    made, first_faces = pipelined_scan(
        totals_of, emit, lines, "beam", {2: tied_faces(cross_faces), 3: tied_faces(beam_faces)}
    )
    first_bordered = bordered_fields(physical_quantities, first_faces[3], first_faces[2])
    spectral_power = jnp.zeros(earlier_spectral_power.shape, jnp.bfloat16)
    start = 0
    for part, _, _ in made:
        spectral_power = lax.dynamic_update_slice_in_dim(spectral_power, part, start, axis=0)
        start += part.shape[0]
    pumping = made[0][1]
    heating = made[0][2]
    for _, part_pumping, part_heating in made[1:]:
        pumping = pumping + part_pumping
        heating = heating + part_heating
    pumping = pump_scale * pumping
    spin_ratio = pumping / (pumping + spin_decay * (1.0 + rubidium_number_amount))
    rubidium_polarization_new = fluid_occupied_sites * spin_ratio
    drift_speed = flow_scale * flow_rate_forward
    for substep in range(SUBSTEPS):
        bordered = first_bordered if substep == 0 else bordered_fields(physical_quantities)
        physical_quantities = advance(
            bordered, rubidium_number_amount, spin_ratio, heating, drift_speed, fluid_occupied_sites
        )
    return (
        spectral_power,
        physical_quantities[0],
        physical_quantities[1] + boundary_kelvin,
        rubidium_polarization_new,
    )


def solution(mesh):
    in_specs = (
        P("beam", "cross", None),
        P("beam", "cross", None),
        P("beam", "cross", None),
        P(None, "beam", "cross", None),
        P(None, "cross", None),
        P(),
        P("cross", None),
        P("beam", "cross"),
    )
    out_specs = (
        P(None, "beam", "cross", None),
        P("beam", "cross", None),
        P("beam", "cross", None),
        P("beam", "cross", None),
    )
    return jax.shard_map(local, mesh=mesh, in_specs=in_specs, out_specs=out_specs, check_vma=False)
```

```python
import jax
import jax.numpy as jnp
from jax import lax
from jax.sharding import PartitionSpec as P

SUBSTEPS = 2


rubidium_amount_slope = 23.25
rubidium_amount_center = 0.95
absorb_scale = 1.0
glass_depth = 0.07
saturation = 1.0
pump_scale = 0.015625
spin_decay = 0.5
exchange_rate = 0.05
xenon_relax = 0.02
heat_gain = 0.05
cooling = 0.02
xenon_diffusion = 0.09
conduction = 0.09
flow_scale = 0.2
boundary_kelvin = 1.0
neighbor_offsets = ((1, 0, 0), (-1, 0, 0), (0, 1, 0), (0, -1, 0), (0, 0, 1), (0, 0, -1))


def shifted(block, axis, shift):
    count = lax.axis_size(axis)
    if shift > 0:
        pairs = [(i, i + shift) for i in range(count - shift)]
    else:
        pairs = [(i - shift, i) for i in range(count + shift)]
    return lax.ppermute(block, axis, pairs)


def beam_faces(block):
    rows = block.shape[1]
    return shifted(block[:, rows - 1 :], "beam", 1), shifted(block[:, :1], "beam", -1)


def cross_faces(block):
    columns = block.shape[2]
    return shifted(block[:, :, columns - 1 :], "cross", 1), shifted(block[:, :, :1], "cross", -1)


def bordered_fields(block, beam=None, cross=None):
    low_beam, high_beam = beam_faces(block) if beam is None else beam
    low_cross, high_cross = cross_faces(block) if cross is None else cross
    middle = jnp.concatenate([low_cross, block, high_cross], axis=2)
    zeros = jnp.zeros_like(low_beam[:, :, :1])
    low_beam = jnp.concatenate([zeros, low_beam, zeros], axis=2)
    high_beam = jnp.concatenate([zeros, high_beam, zeros], axis=2)
    bordered = jnp.concatenate([low_beam, middle, high_beam], axis=1)
    return jnp.pad(bordered, ((0, 0), (0, 0), (0, 0), (1, 1)))


def exclusive_scan(totals, axis, stride=1):
    count = lax.axis_size(axis) // stride
    if count == 1:
        return jnp.zeros_like(totals)
    before = shifted(totals, axis, stride)
    through = totals + before
    step = 2
    while step < count:
        arrived = shifted(through, axis, step * stride)
        before = before + arrived
        step *= 2
        if step < count:
            through = through + arrived
    return before


def paired_steps(totals, axis):
    count = lax.axis_size(axis)
    half = totals.shape[0] // 2
    is_low = lax.axis_index(axis) % 2 == 0
    first, second = totals[:half], totals[half:]
    mine = jnp.where(is_low, first, second)
    swap = [(i, i ^ 1) for i in range(count)]
    got = yield jnp.where(is_low, second, first), swap
    pair_total = mine + got
    pairs = count // 2
    before = yield pair_total, shift_pairs(count, 2)
    through = pair_total + before
    step = 2
    while step < pairs:
        arrived = yield through, shift_pairs(count, 2 * step)
        before = before + arrived
        step *= 2
        if step < pairs:
            through = through + arrived
    back = yield jnp.where(is_low, before + mine, before), swap
    return jnp.where(
        is_low, jnp.concatenate([before, back]), jnp.concatenate([back, before + got])
    )


def shift_pairs(count, shift):
    return [(i, i + shift) for i in range(count - shift)]


def pipelined_scan(totals_of, emit, lines, axis, riders, groups=2):
    count = lax.axis_size(axis)
    if count % 2 or count <= 2 or lines % (2 * groups):
        earlier = exclusive_scan(totals_of(0, lines, None), axis)
        return [emit(0, lines, earlier)], {stage: rider(None) for stage, rider in riders.items()}
    size = lines // groups
    steps = [None] * groups
    steps[0] = paired_steps(totals_of(0, size, None), axis)
    live, made, carried, stage = {}, [], {}, 0
    while stage < groups or live:
        if stage < groups:
            live[stage] = next(steps[stage])
        arrived = {g: lax.ppermute(payload, axis, pairs) for g, (payload, pairs) in live.items()}
        if stage == 0:
            for g in range(1, groups):
                steps[g] = paired_steps(totals_of(g * size, size, live[0][0]), axis)
        tied = (arrived, made)
        if stage in riders:
            tied, carried[stage] = lax.optimization_barrier((tied, riders[stage](live[0][0])))
        else:
            tied = lax.optimization_barrier(tied)
        arrived, made = tied
        following = {}
        for g, value in arrived.items():
            try:
                following[g] = steps[g].send(value)
            except StopIteration as finished:
                made = made + [emit(g * size, size, finished.value)]
        live = following
        stage += 1
    return made, carried


def window(source, step_beam, step_cross, step_depth):
    return source[
        ...,
        1 + step_beam : source.shape[-3] - 1 + step_beam,
        1 + step_cross : source.shape[-2] - 1 + step_cross,
        1 + step_depth : source.shape[-1] - 1 + step_depth,
    ]


def advance(
    bordered, rubidium_number_amount, spin_ratio, heating, drift_speed, fluid_occupied_sites
):
    center = window(bordered, 0, 0, 0)
    complete_heat_ratio = bordered[1] + boundary_kelvin
    coefficients = jnp.stack(
        [xenon_diffusion * complete_heat_ratio**1.5, conduction * complete_heat_ratio**0.7]
    )
    coeff_center = window(coefficients, 0, 0, 0)
    diffused = jnp.zeros_like(center)
    for step_beam, step_cross, step_depth in neighbor_offsets:
        neighbor = window(bordered, step_beam, step_cross, step_depth)
        face_coeff = 0.5 * (coeff_center + window(coefficients, step_beam, step_cross, step_depth))
        diffused = diffused + face_coeff * (neighbor - center)
    upstream = window(bordered, -1, 0, 0)
    transport = diffused - drift_speed * (center - upstream)
    xenon_new = (
        center[0]
        + transport[0]
        + exchange_rate * rubidium_number_amount * (spin_ratio - center[0])
        - xenon_relax * center[0]
    )
    deviation = center[1] + transport[1] + heat_gain * heating - cooling * center[1]
    return jnp.stack([xenon_new * fluid_occupied_sites, deviation * fluid_occupied_sites])


def local(
    xenon_spin_polarization,
    heat_ratio,
    rubidium_polarization_old,
    earlier_spectral_power,
    entry_spectral_power,
    spectral_attenuation_section,
    flow_rate_forward,
    solid_pillar_flags,
):
    rows = earlier_spectral_power.shape[1]
    total_rows = rows * lax.axis_size("beam")
    physical_quantities = jnp.stack([xenon_spin_polarization, heat_ratio - boundary_kelvin])
    glass_cells = solid_pillar_flags.astype(jnp.float32)[:, :, None]
    fluid_occupied_sites = 1.0 - glass_cells
    rubidium_number_amount = fluid_occupied_sites * jnp.exp(
        rubidium_amount_slope * (rubidium_amount_center - 1.0 / heat_ratio)
    )
    absorber = (
        absorb_scale / total_rows * rubidium_number_amount * (1.0 - rubidium_polarization_old)
    )
    glass_term = glass_depth * glass_cells

    def depth_of(start, size):
        weight = spectral_attenuation_section[start : start + size, None, None, None] / (
            1.0 + earlier_spectral_power[start : start + size].astype(jnp.float32) / saturation
        )
        return absorber[None] * weight + glass_term[None], weight

    def totals_of(start, size, after):
        optical_depth, _ = depth_of(start, size)
        if after is not None:
            optical_depth, _ = lax.optimization_barrier((optical_depth, after))
        return jnp.sum(optical_depth, axis=1)

    def emit(start, size, earlier):
        optical_depth, weight = depth_of(start, size)
        local_column = jnp.pad(
            jnp.cumsum(optical_depth[:, : rows - 1], axis=1), ((0, 0), (1, 0), (0, 0), (0, 0))
        )
        column = earlier[:, None] + local_column
        radiance = entry_spectral_power[start : start + size, None] * jnp.exp(-column)
        return (
            radiance.astype(jnp.bfloat16),
            jnp.sum(weight * radiance, axis=0),
            jnp.sum(radiance * (1.0 - jnp.exp(-optical_depth)), axis=0),
        )

    def tied_faces(faces):
        def exchange(after):
            fields = physical_quantities
            if after is not None:
                fields, _ = lax.optimization_barrier((fields, after))
            return faces(fields)

        return exchange

    lines = earlier_spectral_power.shape[0]
    made, first_faces = pipelined_scan(
        totals_of, emit, lines, "beam", {2: tied_faces(cross_faces), 3: tied_faces(beam_faces)}
    )
    first_bordered = bordered_fields(physical_quantities, first_faces[3], first_faces[2])
    spectral_power = jnp.zeros(earlier_spectral_power.shape, jnp.bfloat16)
    start = jnp.minimum(lax.axis_index("beam"), 0)
    for part, _, _ in made:
        spectral_power = lax.dynamic_update_slice_in_dim(spectral_power, part, start, axis=0)
        start = start + part.shape[0]
    pumping = made[0][1]
    heating = made[0][2]
    for _, part_pumping, part_heating in made[1:]:
        pumping = pumping + part_pumping
        heating = heating + part_heating
    pumping = pump_scale * pumping
    spin_ratio = pumping / (pumping + spin_decay * (1.0 + rubidium_number_amount))
    rubidium_polarization_new = fluid_occupied_sites * spin_ratio
    drift_speed = flow_scale * flow_rate_forward
    for substep in range(SUBSTEPS):
        bordered = first_bordered if substep == 0 else bordered_fields(physical_quantities)
        physical_quantities = advance(
            bordered, rubidium_number_amount, spin_ratio, heating, drift_speed, fluid_occupied_sites
        )
    return (
        spectral_power,
        physical_quantities[0],
        physical_quantities[1] + boundary_kelvin,
        rubidium_polarization_new,
    )


def solution(mesh):
    in_specs = (
        P("beam", "cross", None),
        P("beam", "cross", None),
        P("beam", "cross", None),
        P(None, "beam", "cross", None),
        P(None, "cross", None),
        P(),
        P("cross", None),
        P("beam", "cross"),
    )
    out_specs = (
        P(None, "beam", "cross", None),
        P("beam", "cross", None),
        P("beam", "cross", None),
        P("beam", "cross", None),
    )
    return jax.shard_map(local, mesh=mesh, in_specs=in_specs, out_specs=out_specs, check_vma=False)
```

```python
import jax
import jax.numpy as jnp
from jax import lax
from jax.sharding import PartitionSpec as P

SUBSTEPS = 2


rubidium_amount_slope = 23.25
rubidium_amount_center = 0.95
absorb_scale = 1.0
glass_depth = 0.07
saturation = 1.0
pump_scale = 0.015625
spin_decay = 0.5
exchange_rate = 0.05
xenon_relax = 0.02
heat_gain = 0.05
cooling = 0.02
xenon_diffusion = 0.09
conduction = 0.09
flow_scale = 0.2
boundary_kelvin = 1.0
neighbor_offsets = ((1, 0, 0), (-1, 0, 0), (0, 1, 0), (0, -1, 0), (0, 0, 1), (0, 0, -1))


def shifted(block, axis, shift):
    count = lax.axis_size(axis)
    if shift > 0:
        pairs = [(i, i + shift) for i in range(count - shift)]
    else:
        pairs = [(i - shift, i) for i in range(count + shift)]
    return lax.ppermute(block, axis, pairs)


def beam_faces(block):
    rows = block.shape[1]
    return shifted(block[:, rows - 1 :], "beam", 1), shifted(block[:, :1], "beam", -1)


def cross_faces(block):
    columns = block.shape[2]
    return shifted(block[:, :, columns - 1 :], "cross", 1), shifted(block[:, :, :1], "cross", -1)


def bordered_fields(block, beam=None, cross=None):
    low_beam, high_beam = beam_faces(block) if beam is None else beam
    low_cross, high_cross = cross_faces(block) if cross is None else cross
    middle = jnp.concatenate([low_cross, block, high_cross], axis=2)
    zeros = jnp.zeros_like(low_beam[:, :, :1])
    low_beam = jnp.concatenate([zeros, low_beam, zeros], axis=2)
    high_beam = jnp.concatenate([zeros, high_beam, zeros], axis=2)
    bordered = jnp.concatenate([low_beam, middle, high_beam], axis=1)
    return jnp.pad(bordered, ((0, 0), (0, 0), (0, 0), (1, 1)))


def exclusive_scan(totals, axis, stride=1):
    count = lax.axis_size(axis) // stride
    if count == 1:
        return jnp.zeros_like(totals)
    before = shifted(totals, axis, stride)
    through = totals + before
    step = 2
    while step < count:
        arrived = shifted(through, axis, step * stride)
        before = before + arrived
        step *= 2
        if step < count:
            through = through + arrived
    return before


def paired_steps(totals, axis):
    count = lax.axis_size(axis)
    half = totals.shape[0] // 2
    is_low = lax.axis_index(axis) % 2 == 0
    first, second = totals[:half], totals[half:]
    mine = jnp.where(is_low, first, second)
    swap = [(i, i ^ 1) for i in range(count)]
    got = yield jnp.where(is_low, second, first), swap
    pair_total = mine + got
    pairs = count // 2
    before = yield pair_total, shift_pairs(count, 2)
    through = pair_total + before
    step = 2
    while step < pairs:
        arrived = yield through, shift_pairs(count, 2 * step)
        before = before + arrived
        step *= 2
        if step < pairs:
            through = through + arrived
    back = yield jnp.where(is_low, before + mine, before), swap
    return jnp.where(
        is_low, jnp.concatenate([before, back]), jnp.concatenate([back, before + got])
    )


def shift_pairs(count, shift):
    return [(i, i + shift) for i in range(count - shift)]


def pipelined_scan(totals_of, emit, lines, axis, riders, groups=2):
    count = lax.axis_size(axis)
    if count % 2 or count <= 2 or lines % (2 * groups):
        earlier = exclusive_scan(totals_of(0, lines, None), axis)
        return [emit(0, lines, earlier)], {stage: rider(None) for stage, rider in riders.items()}
    first = max(2, lines // (2 * groups) // 2 * 2)
    sizes = [first] + [(lines - first) // (groups - 1) // 2 * 2] * (groups - 1)
    sizes[-1] += lines - sum(sizes)
    starts = [sum(sizes[:g]) for g in range(groups)]
    steps = [None] * groups
    steps[0] = paired_steps(totals_of(0, sizes[0], None), axis)
    live, made, carried, stage = {}, [], {}, 0
    while stage < groups or live:
        if stage < groups:
            live[stage] = next(steps[stage])
        arrived = {g: lax.ppermute(payload, axis, pairs) for g, (payload, pairs) in live.items()}
        if stage == 0:
            for g in range(1, groups):
                steps[g] = paired_steps(totals_of(starts[g], sizes[g], live[0][0]), axis)
        tied = (arrived, made)
        if stage in riders:
            tied, carried[stage] = lax.optimization_barrier((tied, riders[stage](live[0][0])))
        else:
            tied = lax.optimization_barrier(tied)
        arrived, made = tied
        following = {}
        for g, value in arrived.items():
            try:
                following[g] = steps[g].send(value)
            except StopIteration as finished:
                made = made + [emit(starts[g], sizes[g], finished.value)]
        live = following
        stage += 1
    return made, carried


def window(source, step_beam, step_cross, step_depth):
    return source[
        ...,
        1 + step_beam : source.shape[-3] - 1 + step_beam,
        1 + step_cross : source.shape[-2] - 1 + step_cross,
        1 + step_depth : source.shape[-1] - 1 + step_depth,
    ]


def advance(
    bordered, rubidium_number_amount, spin_ratio, heating, drift_speed, fluid_occupied_sites
):
    center = window(bordered, 0, 0, 0)
    complete_heat_ratio = bordered[1] + boundary_kelvin
    coefficients = jnp.stack(
        [xenon_diffusion * complete_heat_ratio**1.5, conduction * complete_heat_ratio**0.7]
    )
    coeff_center = window(coefficients, 0, 0, 0)
    diffused = jnp.zeros_like(center)
    for step_beam, step_cross, step_depth in neighbor_offsets:
        neighbor = window(bordered, step_beam, step_cross, step_depth)
        face_coeff = 0.5 * (coeff_center + window(coefficients, step_beam, step_cross, step_depth))
        diffused = diffused + face_coeff * (neighbor - center)
    upstream = window(bordered, -1, 0, 0)
    transport = diffused - drift_speed * (center - upstream)
    xenon_new = (
        center[0]
        + transport[0]
        + exchange_rate * rubidium_number_amount * (spin_ratio - center[0])
        - xenon_relax * center[0]
    )
    deviation = center[1] + transport[1] + heat_gain * heating - cooling * center[1]
    return jnp.stack([xenon_new * fluid_occupied_sites, deviation * fluid_occupied_sites])


def local(
    xenon_spin_polarization,
    heat_ratio,
    rubidium_polarization_old,
    earlier_spectral_power,
    entry_spectral_power,
    spectral_attenuation_section,
    flow_rate_forward,
    solid_pillar_flags,
):
    rows = earlier_spectral_power.shape[1]
    total_rows = rows * lax.axis_size("beam")
    physical_quantities = jnp.stack([xenon_spin_polarization, heat_ratio - boundary_kelvin])
    glass_cells = solid_pillar_flags.astype(jnp.float32)[:, :, None]
    fluid_occupied_sites = 1.0 - glass_cells
    rubidium_number_amount = fluid_occupied_sites * jnp.exp(
        rubidium_amount_slope * (rubidium_amount_center - 1.0 / heat_ratio)
    )
    absorber = (
        absorb_scale / total_rows * rubidium_number_amount * (1.0 - rubidium_polarization_old)
    )
    glass_term = glass_depth * glass_cells

    def depth_of(start, size):
        weight = spectral_attenuation_section[start : start + size, None, None, None] / (
            1.0 + earlier_spectral_power[start : start + size].astype(jnp.float32) / saturation
        )
        return absorber[None] * weight + glass_term[None], weight

    def totals_of(start, size, after):
        optical_depth, _ = depth_of(start, size)
        if after is not None:
            optical_depth, _ = lax.optimization_barrier((optical_depth, after))
        return jnp.sum(optical_depth, axis=1)

    def emit(start, size, earlier):
        optical_depth, weight = depth_of(start, size)
        local_column = jnp.pad(
            jnp.cumsum(optical_depth[:, : rows - 1], axis=1), ((0, 0), (1, 0), (0, 0), (0, 0))
        )
        column = earlier[:, None] + local_column
        radiance = entry_spectral_power[start : start + size, None] * jnp.exp(-column)
        return (
            radiance.astype(jnp.bfloat16),
            jnp.sum(weight * radiance, axis=0),
            jnp.sum(radiance * (1.0 - jnp.exp(-optical_depth)), axis=0),
        )

    def tied_faces(faces):
        def exchange(after):
            fields = physical_quantities
            if after is not None:
                fields, _ = lax.optimization_barrier((fields, after))
            return faces(fields)

        return exchange

    lines = earlier_spectral_power.shape[0]
    made, first_faces = pipelined_scan(
        totals_of, emit, lines, "beam", {2: tied_faces(cross_faces), 3: tied_faces(beam_faces)}
    )
    first_bordered = bordered_fields(physical_quantities, first_faces[3], first_faces[2])
    spectral_power = jnp.zeros(earlier_spectral_power.shape, jnp.bfloat16)
    start = 0
    for part, _, _ in made:
        spectral_power = lax.dynamic_update_slice_in_dim(spectral_power, part, start, axis=0)
        start += part.shape[0]
    pumping = made[0][1]
    heating = made[0][2]
    for _, part_pumping, part_heating in made[1:]:
        pumping = pumping + part_pumping
        heating = heating + part_heating
    pumping = pump_scale * pumping
    spin_ratio = pumping / (pumping + spin_decay * (1.0 + rubidium_number_amount))
    rubidium_polarization_new = fluid_occupied_sites * spin_ratio
    drift_speed = flow_scale * flow_rate_forward
    for substep in range(SUBSTEPS):
        bordered = first_bordered if substep == 0 else bordered_fields(physical_quantities)
        physical_quantities = advance(
            bordered, rubidium_number_amount, spin_ratio, heating, drift_speed, fluid_occupied_sites
        )
    return (
        spectral_power,
        physical_quantities[0],
        physical_quantities[1] + boundary_kelvin,
        rubidium_polarization_new,
    )


def solution(mesh):
    in_specs = (
        P("beam", "cross", None),
        P("beam", "cross", None),
        P("beam", "cross", None),
        P(None, "beam", "cross", None),
        P(None, "cross", None),
        P(),
        P("cross", None),
        P("beam", "cross"),
    )
    out_specs = (
        P(None, "beam", "cross", None),
        P("beam", "cross", None),
        P("beam", "cross", None),
        P("beam", "cross", None),
    )
    return jax.shard_map(local, mesh=mesh, in_specs=in_specs, out_specs=out_specs, check_vma=False)
```

```python
import jax
import jax.numpy as jnp
from jax import lax
from jax.sharding import PartitionSpec as P

SUBSTEPS = 2


rubidium_amount_slope = 23.25
rubidium_amount_center = 0.95
absorb_scale = 1.0
glass_depth = 0.07
saturation = 1.0
pump_scale = 0.015625
spin_decay = 0.5
exchange_rate = 0.05
xenon_relax = 0.02
heat_gain = 0.05
cooling = 0.02
xenon_diffusion = 0.09
conduction = 0.09
flow_scale = 0.2
boundary_kelvin = 1.0
neighbor_offsets = ((1, 0, 0), (-1, 0, 0), (0, 1, 0), (0, -1, 0), (0, 0, 1), (0, 0, -1))


def shifted(block, axis, shift):
    count = lax.axis_size(axis)
    if shift > 0:
        pairs = [(i, i + shift) for i in range(count - shift)]
    else:
        pairs = [(i - shift, i) for i in range(count + shift)]
    return lax.ppermute(block, axis, pairs)


def beam_faces(block):
    rows = block.shape[1]
    return shifted(block[:, rows - 1 :], "beam", 1), shifted(block[:, :1], "beam", -1)


def cross_faces(block):
    columns = block.shape[2]
    return shifted(block[:, :, columns - 1 :], "cross", 1), shifted(block[:, :, :1], "cross", -1)


def bordered_fields(block, beam=None, cross=None):
    low_beam, high_beam = beam_faces(block) if beam is None else beam
    low_cross, high_cross = cross_faces(block) if cross is None else cross
    middle = jnp.concatenate([low_cross, block, high_cross], axis=2)
    zeros = jnp.zeros_like(low_beam[:, :, :1])
    low_beam = jnp.concatenate([zeros, low_beam, zeros], axis=2)
    high_beam = jnp.concatenate([zeros, high_beam, zeros], axis=2)
    bordered = jnp.concatenate([low_beam, middle, high_beam], axis=1)
    return jnp.pad(bordered, ((0, 0), (0, 0), (0, 0), (1, 1)))


def exclusive_scan(totals, axis, stride=1):
    count = lax.axis_size(axis) // stride
    if count == 1:
        return jnp.zeros_like(totals)
    before = shifted(totals, axis, stride)
    through = totals + before
    step = 2
    while step < count:
        arrived = shifted(through, axis, step * stride)
        before = before + arrived
        step *= 2
        if step < count:
            through = through + arrived
    return before


def paired_steps(totals, axis):
    count = lax.axis_size(axis)
    half = totals.shape[0] // 2
    is_low = lax.axis_index(axis) % 2 == 0
    first, second = totals[:half], totals[half:]
    mine = jnp.where(is_low, first, second)
    swap = [(i, i ^ 1) for i in range(count)]
    got = yield jnp.where(is_low, second, first), swap
    pair_total = mine + got
    pairs = count // 2
    before = yield pair_total, shift_pairs(count, 2)
    through = pair_total + before
    step = 2
    while step < pairs:
        arrived = yield through, shift_pairs(count, 2 * step)
        before = before + arrived
        step *= 2
        if step < pairs:
            through = through + arrived
    back = yield jnp.where(is_low, before + mine, before), swap
    return jnp.where(
        is_low, jnp.concatenate([before, back]), jnp.concatenate([back, before + got])
    )


def shift_pairs(count, shift):
    return [(i, i + shift) for i in range(count - shift)]


def pipelined_scan(totals_of, emit, lines, axis, riders, groups=2):
    count = lax.axis_size(axis)
    if count % 2 or count <= 2 or lines % (2 * groups):
        earlier = exclusive_scan(totals_of(0, lines, None), axis)
        return [emit(0, lines, earlier)], {stage: rider(None) for stage, rider in riders.items()}
    last = max(2, lines // (2 * groups) // 2 * 2)
    sizes = [(lines - last) // (groups - 1) // 2 * 2] * (groups - 1) + [last]
    sizes[0] += lines - sum(sizes)
    starts = [sum(sizes[:g]) for g in range(groups)]
    steps = [None] * groups
    steps[0] = paired_steps(totals_of(0, sizes[0], None), axis)
    live, made, carried, stage = {}, [], {}, 0
    while stage < groups or live:
        if stage < groups:
            live[stage] = next(steps[stage])
        arrived = {g: lax.ppermute(payload, axis, pairs) for g, (payload, pairs) in live.items()}
        if stage == 0:
            for g in range(1, groups):
                steps[g] = paired_steps(totals_of(starts[g], sizes[g], live[0][0]), axis)
        tied = (arrived, made)
        if stage in riders:
            tied, carried[stage] = lax.optimization_barrier((tied, riders[stage](live[0][0])))
        else:
            tied = lax.optimization_barrier(tied)
        arrived, made = tied
        following = {}
        for g, value in arrived.items():
            try:
                following[g] = steps[g].send(value)
            except StopIteration as finished:
                made = made + [emit(starts[g], sizes[g], finished.value)]
        live = following
        stage += 1
    return made, carried


def window(source, step_beam, step_cross, step_depth):
    return source[
        ...,
        1 + step_beam : source.shape[-3] - 1 + step_beam,
        1 + step_cross : source.shape[-2] - 1 + step_cross,
        1 + step_depth : source.shape[-1] - 1 + step_depth,
    ]


def advance(
    bordered, rubidium_number_amount, spin_ratio, heating, drift_speed, fluid_occupied_sites
):
    center = window(bordered, 0, 0, 0)
    complete_heat_ratio = bordered[1] + boundary_kelvin
    coefficients = jnp.stack(
        [xenon_diffusion * complete_heat_ratio**1.5, conduction * complete_heat_ratio**0.7]
    )
    coeff_center = window(coefficients, 0, 0, 0)
    diffused = jnp.zeros_like(center)
    for step_beam, step_cross, step_depth in neighbor_offsets:
        neighbor = window(bordered, step_beam, step_cross, step_depth)
        face_coeff = 0.5 * (coeff_center + window(coefficients, step_beam, step_cross, step_depth))
        diffused = diffused + face_coeff * (neighbor - center)
    upstream = window(bordered, -1, 0, 0)
    transport = diffused - drift_speed * (center - upstream)
    xenon_new = (
        center[0]
        + transport[0]
        + exchange_rate * rubidium_number_amount * (spin_ratio - center[0])
        - xenon_relax * center[0]
    )
    deviation = center[1] + transport[1] + heat_gain * heating - cooling * center[1]
    return jnp.stack([xenon_new * fluid_occupied_sites, deviation * fluid_occupied_sites])


def local(
    xenon_spin_polarization,
    heat_ratio,
    rubidium_polarization_old,
    earlier_spectral_power,
    entry_spectral_power,
    spectral_attenuation_section,
    flow_rate_forward,
    solid_pillar_flags,
):
    rows = earlier_spectral_power.shape[1]
    total_rows = rows * lax.axis_size("beam")
    physical_quantities = jnp.stack([xenon_spin_polarization, heat_ratio - boundary_kelvin])
    glass_cells = solid_pillar_flags.astype(jnp.float32)[:, :, None]
    fluid_occupied_sites = 1.0 - glass_cells
    rubidium_number_amount = fluid_occupied_sites * jnp.exp(
        rubidium_amount_slope * (rubidium_amount_center - 1.0 / heat_ratio)
    )
    absorber = (
        absorb_scale / total_rows * rubidium_number_amount * (1.0 - rubidium_polarization_old)
    )
    glass_term = glass_depth * glass_cells

    def depth_of(start, size):
        weight = spectral_attenuation_section[start : start + size, None, None, None] / (
            1.0 + earlier_spectral_power[start : start + size].astype(jnp.float32) / saturation
        )
        return absorber[None] * weight + glass_term[None], weight

    def totals_of(start, size, after):
        optical_depth, _ = depth_of(start, size)
        if after is not None:
            optical_depth, _ = lax.optimization_barrier((optical_depth, after))
        return jnp.sum(optical_depth, axis=1)

    def emit(start, size, earlier):
        optical_depth, weight = depth_of(start, size)
        local_column = jnp.pad(
            jnp.cumsum(optical_depth[:, : rows - 1], axis=1), ((0, 0), (1, 0), (0, 0), (0, 0))
        )
        column = earlier[:, None] + local_column
        radiance = entry_spectral_power[start : start + size, None] * jnp.exp(-column)
        return (
            radiance.astype(jnp.bfloat16),
            jnp.sum(weight * radiance, axis=0),
            jnp.sum(radiance * (1.0 - jnp.exp(-optical_depth)), axis=0),
        )

    def tied_faces(faces):
        def exchange(after):
            fields = physical_quantities
            if after is not None:
                fields, _ = lax.optimization_barrier((fields, after))
            return faces(fields)

        return exchange

    lines = earlier_spectral_power.shape[0]
    made, first_faces = pipelined_scan(
        totals_of, emit, lines, "beam", {2: tied_faces(cross_faces), 3: tied_faces(beam_faces)}
    )
    first_bordered = bordered_fields(physical_quantities, first_faces[3], first_faces[2])
    spectral_power = jnp.zeros(earlier_spectral_power.shape, jnp.bfloat16)
    start = 0
    for part, _, _ in made:
        spectral_power = lax.dynamic_update_slice_in_dim(spectral_power, part, start, axis=0)
        start += part.shape[0]
    pumping = made[0][1]
    heating = made[0][2]
    for _, part_pumping, part_heating in made[1:]:
        pumping = pumping + part_pumping
        heating = heating + part_heating
    pumping = pump_scale * pumping
    spin_ratio = pumping / (pumping + spin_decay * (1.0 + rubidium_number_amount))
    rubidium_polarization_new = fluid_occupied_sites * spin_ratio
    drift_speed = flow_scale * flow_rate_forward
    for substep in range(SUBSTEPS):
        bordered = first_bordered if substep == 0 else bordered_fields(physical_quantities)
        physical_quantities = advance(
            bordered, rubidium_number_amount, spin_ratio, heating, drift_speed, fluid_occupied_sites
        )
    return (
        spectral_power,
        physical_quantities[0],
        physical_quantities[1] + boundary_kelvin,
        rubidium_polarization_new,
    )


def solution(mesh):
    in_specs = (
        P("beam", "cross", None),
        P("beam", "cross", None),
        P("beam", "cross", None),
        P(None, "beam", "cross", None),
        P(None, "cross", None),
        P(),
        P("cross", None),
        P("beam", "cross"),
    )
    out_specs = (
        P(None, "beam", "cross", None),
        P("beam", "cross", None),
        P("beam", "cross", None),
        P("beam", "cross", None),
    )
    return jax.shard_map(local, mesh=mesh, in_specs=in_specs, out_specs=out_specs, check_vma=False)
```

```python
import jax
import jax.numpy as jnp
from jax import lax
from jax.sharding import PartitionSpec as P

SUBSTEPS = 2


rubidium_amount_slope = 23.25
rubidium_amount_center = 0.95
absorb_scale = 1.0
glass_depth = 0.07
saturation = 1.0
pump_scale = 0.015625
spin_decay = 0.5
exchange_rate = 0.05
xenon_relax = 0.02
heat_gain = 0.05
cooling = 0.02
xenon_diffusion = 0.09
conduction = 0.09
flow_scale = 0.2
boundary_kelvin = 1.0
neighbor_offsets = ((1, 0, 0), (-1, 0, 0), (0, 1, 0), (0, -1, 0), (0, 0, 1), (0, 0, -1))


def shifted(block, axis, shift):
    count = lax.axis_size(axis)
    if shift > 0:
        pairs = [(i, i + shift) for i in range(count - shift)]
    else:
        pairs = [(i - shift, i) for i in range(count + shift)]
    return lax.ppermute(block, axis, pairs)


def faces(block, axis, dim):
    size = block.shape[dim]
    last = lax.slice_in_dim(block, size - 1, size, axis=dim)
    first = lax.slice_in_dim(block, 0, 1, axis=dim)
    count = lax.axis_size(axis)
    if count % 2:
        return shifted(last, axis, 1), shifted(first, axis, -1)
    is_even = lax.axis_index(axis) % 2 == 0
    within = lax.ppermute(jnp.where(is_even, last, first), axis, [(i, i ^ 1) for i in range(count)])
    pairs = [(i, i + 1) for i in range(1, count - 1, 2)]
    pairs += [(target, source) for source, target in pairs]
    across = lax.ppermute(jnp.where(is_even, first, last), axis, pairs)
    return jnp.where(is_even, across, within), jnp.where(is_even, within, across)


def beam_faces(block):
    return faces(block, "beam", 1)


def cross_faces(block):
    return faces(block, "cross", 2)


def bordered_fields(block, beam=None, cross=None):
    low_beam, high_beam = beam_faces(block) if beam is None else beam
    low_cross, high_cross = cross_faces(block) if cross is None else cross
    middle = jnp.concatenate([low_cross, block, high_cross], axis=2)
    zeros = jnp.zeros_like(low_beam[:, :, :1])
    low_beam = jnp.concatenate([zeros, low_beam, zeros], axis=2)
    high_beam = jnp.concatenate([zeros, high_beam, zeros], axis=2)
    bordered = jnp.concatenate([low_beam, middle, high_beam], axis=1)
    return jnp.pad(bordered, ((0, 0), (0, 0), (0, 0), (1, 1)))


def exclusive_scan(totals, axis, stride=1):
    count = lax.axis_size(axis) // stride
    if count == 1:
        return jnp.zeros_like(totals)
    before = shifted(totals, axis, stride)
    through = totals + before
    step = 2
    while step < count:
        arrived = shifted(through, axis, step * stride)
        before = before + arrived
        step *= 2
        if step < count:
            through = through + arrived
    return before


def paired_steps(totals, axis):
    count = lax.axis_size(axis)
    half = totals.shape[0] // 2
    is_low = lax.axis_index(axis) % 2 == 0
    first, second = totals[:half], totals[half:]
    mine = jnp.where(is_low, first, second)
    swap = [(i, i ^ 1) for i in range(count)]
    got = yield jnp.where(is_low, second, first), swap
    pair_total = mine + got
    pairs = count // 2
    before = yield pair_total, shift_pairs(count, 2)
    through = pair_total + before
    step = 2
    while step < pairs:
        arrived = yield through, shift_pairs(count, 2 * step)
        before = before + arrived
        step *= 2
        if step < pairs:
            through = through + arrived
    back = yield jnp.where(is_low, before + mine, before), swap
    return jnp.where(
        is_low, jnp.concatenate([before, back]), jnp.concatenate([back, before + got])
    )


def shift_pairs(count, shift):
    return [(i, i + shift) for i in range(count - shift)]


def pipelined_scan(totals_of, emit, lines, axis, riders, groups=2):
    count = lax.axis_size(axis)
    if count % 2 or count <= 2 or lines % (2 * groups):
        earlier = exclusive_scan(totals_of(0, lines, None), axis)
        return [emit(0, lines, earlier)], {stage: rider(None) for stage, rider in riders.items()}
    size = lines // groups
    steps = [None] * groups
    steps[0] = paired_steps(totals_of(0, size, None), axis)
    live, made, carried, stage = {}, [], {}, 0
    while stage < groups or live:
        if stage < groups:
            live[stage] = next(steps[stage])
        arrived = {g: lax.ppermute(payload, axis, pairs) for g, (payload, pairs) in live.items()}
        if stage == 0:
            for g in range(1, groups):
                steps[g] = paired_steps(totals_of(g * size, size, live[0][0]), axis)
        tied = (arrived, made)
        if stage in riders:
            tied, carried[stage] = lax.optimization_barrier((tied, riders[stage](live[0][0])))
        else:
            tied = lax.optimization_barrier(tied)
        arrived, made = tied
        following = {}
        for g, value in arrived.items():
            try:
                following[g] = steps[g].send(value)
            except StopIteration as finished:
                made = made + [emit(g * size, size, finished.value)]
        live = following
        stage += 1
    return made, carried


def window(source, step_beam, step_cross, step_depth):
    return source[
        ...,
        1 + step_beam : source.shape[-3] - 1 + step_beam,
        1 + step_cross : source.shape[-2] - 1 + step_cross,
        1 + step_depth : source.shape[-1] - 1 + step_depth,
    ]


def advance(
    bordered, rubidium_number_amount, spin_ratio, heating, drift_speed, fluid_occupied_sites
):
    center = window(bordered, 0, 0, 0)
    complete_heat_ratio = bordered[1] + boundary_kelvin
    coefficients = jnp.stack(
        [xenon_diffusion * complete_heat_ratio**1.5, conduction * complete_heat_ratio**0.7]
    )
    coeff_center = window(coefficients, 0, 0, 0)
    diffused = jnp.zeros_like(center)
    for step_beam, step_cross, step_depth in neighbor_offsets:
        neighbor = window(bordered, step_beam, step_cross, step_depth)
        face_coeff = 0.5 * (coeff_center + window(coefficients, step_beam, step_cross, step_depth))
        diffused = diffused + face_coeff * (neighbor - center)
    upstream = window(bordered, -1, 0, 0)
    transport = diffused - drift_speed * (center - upstream)
    xenon_new = (
        center[0]
        + transport[0]
        + exchange_rate * rubidium_number_amount * (spin_ratio - center[0])
        - xenon_relax * center[0]
    )
    deviation = center[1] + transport[1] + heat_gain * heating - cooling * center[1]
    return jnp.stack([xenon_new * fluid_occupied_sites, deviation * fluid_occupied_sites])


def local(
    xenon_spin_polarization,
    heat_ratio,
    rubidium_polarization_old,
    earlier_spectral_power,
    entry_spectral_power,
    spectral_attenuation_section,
    flow_rate_forward,
    solid_pillar_flags,
):
    rows = earlier_spectral_power.shape[1]
    total_rows = rows * lax.axis_size("beam")
    physical_quantities = jnp.stack([xenon_spin_polarization, heat_ratio - boundary_kelvin])
    glass_cells = solid_pillar_flags.astype(jnp.float32)[:, :, None]
    fluid_occupied_sites = 1.0 - glass_cells
    rubidium_number_amount = fluid_occupied_sites * jnp.exp(
        rubidium_amount_slope * (rubidium_amount_center - 1.0 / heat_ratio)
    )
    absorber = (
        absorb_scale / total_rows * rubidium_number_amount * (1.0 - rubidium_polarization_old)
    )
    glass_term = glass_depth * glass_cells

    def depth_of(start, size):
        weight = spectral_attenuation_section[start : start + size, None, None, None] / (
            1.0 + earlier_spectral_power[start : start + size].astype(jnp.float32) / saturation
        )
        return absorber[None] * weight + glass_term[None], weight

    def totals_of(start, size, after):
        optical_depth, _ = depth_of(start, size)
        if after is not None:
            optical_depth, _ = lax.optimization_barrier((optical_depth, after))
        return jnp.sum(optical_depth, axis=1)

    def emit(start, size, earlier):
        optical_depth, weight = depth_of(start, size)
        local_column = jnp.pad(
            jnp.cumsum(optical_depth[:, : rows - 1], axis=1), ((0, 0), (1, 0), (0, 0), (0, 0))
        )
        column = earlier[:, None] + local_column
        radiance = entry_spectral_power[start : start + size, None] * jnp.exp(-column)
        return (
            radiance.astype(jnp.bfloat16),
            jnp.sum(weight * radiance, axis=0),
            jnp.sum(radiance * (1.0 - jnp.exp(-optical_depth)), axis=0),
        )

    def tied_faces(faces):
        def exchange(after):
            fields = physical_quantities
            if after is not None:
                fields, _ = lax.optimization_barrier((fields, after))
            return faces(fields)

        return exchange

    lines = earlier_spectral_power.shape[0]
    made, first_faces = pipelined_scan(
        totals_of, emit, lines, "beam", {2: tied_faces(cross_faces), 3: tied_faces(beam_faces)}
    )
    first_bordered = bordered_fields(physical_quantities, first_faces[3], first_faces[2])
    spectral_power = jnp.zeros(earlier_spectral_power.shape, jnp.bfloat16)
    start = 0
    for part, _, _ in made:
        spectral_power = lax.dynamic_update_slice_in_dim(spectral_power, part, start, axis=0)
        start += part.shape[0]
    pumping = made[0][1]
    heating = made[0][2]
    for _, part_pumping, part_heating in made[1:]:
        pumping = pumping + part_pumping
        heating = heating + part_heating
    pumping = pump_scale * pumping
    spin_ratio = pumping / (pumping + spin_decay * (1.0 + rubidium_number_amount))
    rubidium_polarization_new = fluid_occupied_sites * spin_ratio
    drift_speed = flow_scale * flow_rate_forward
    for substep in range(SUBSTEPS):
        bordered = first_bordered if substep == 0 else bordered_fields(physical_quantities)
        physical_quantities = advance(
            bordered, rubidium_number_amount, spin_ratio, heating, drift_speed, fluid_occupied_sites
        )
    return (
        spectral_power,
        physical_quantities[0],
        physical_quantities[1] + boundary_kelvin,
        rubidium_polarization_new,
    )


def solution(mesh):
    in_specs = (
        P("beam", "cross", None),
        P("beam", "cross", None),
        P("beam", "cross", None),
        P(None, "beam", "cross", None),
        P(None, "cross", None),
        P(),
        P("cross", None),
        P("beam", "cross"),
    )
    out_specs = (
        P(None, "beam", "cross", None),
        P("beam", "cross", None),
        P("beam", "cross", None),
        P("beam", "cross", None),
    )
    return jax.shard_map(local, mesh=mesh, in_specs=in_specs, out_specs=out_specs, check_vma=False)
```

```python
import jax
import jax.numpy as jnp
from jax import lax
from jax.sharding import PartitionSpec as P

SUBSTEPS = 2


rubidium_amount_slope = 23.25
rubidium_amount_center = 0.95
absorb_scale = 1.0
glass_depth = 0.07
saturation = 1.0
pump_scale = 0.015625
spin_decay = 0.5
exchange_rate = 0.05
xenon_relax = 0.02
heat_gain = 0.05
cooling = 0.02
xenon_diffusion = 0.09
conduction = 0.09
flow_scale = 0.2
boundary_kelvin = 1.0
neighbor_offsets = ((1, 0, 0), (-1, 0, 0), (0, 1, 0), (0, -1, 0), (0, 0, 1), (0, 0, -1))


def shifted(block, axis, shift):
    count = lax.axis_size(axis)
    if shift > 0:
        pairs = [(i, i + shift) for i in range(count - shift)]
    else:
        pairs = [(i - shift, i) for i in range(count + shift)]
    return lax.ppermute(block, axis, pairs)


def faces(block, axis, dim):
    size = block.shape[dim]
    last = lax.slice_in_dim(block, size - 1, size, axis=dim)
    first = lax.slice_in_dim(block, 0, 1, axis=dim)
    count = lax.axis_size(axis)
    if count % 2:
        return shifted(last, axis, 1), shifted(first, axis, -1)
    is_even = lax.axis_index(axis) % 2 == 0
    within = lax.ppermute(jnp.where(is_even, last, first), axis, [(i, i ^ 1) for i in range(count)])
    pairs = [(i, i + 1) for i in range(1, count - 1, 2)]
    pairs += [(target, source) for source, target in pairs]
    across = lax.ppermute(jnp.where(is_even, first, last), axis, pairs)
    return jnp.where(is_even, across, within), jnp.where(is_even, within, across)


def beam_faces(block):
    return faces(block, "beam", 1)


def cross_faces(block):
    return faces(block, "cross", 2)


def bordered_fields(block, beam=None, cross=None):
    low_beam, high_beam = beam_faces(block) if beam is None else beam
    low_cross, high_cross = cross_faces(block) if cross is None else cross
    middle = jnp.concatenate([low_cross, block, high_cross], axis=2)
    zeros = jnp.zeros_like(low_beam[:, :, :1])
    low_beam = jnp.concatenate([zeros, low_beam, zeros], axis=2)
    high_beam = jnp.concatenate([zeros, high_beam, zeros], axis=2)
    bordered = jnp.concatenate([low_beam, middle, high_beam], axis=1)
    return jnp.pad(bordered, ((0, 0), (0, 0), (0, 0), (1, 1)))


def exclusive_scan(totals, axis, stride=1):
    count = lax.axis_size(axis) // stride
    if count == 1:
        return jnp.zeros_like(totals)
    before = shifted(totals, axis, stride)
    through = totals + before
    step = 2
    while step < count:
        arrived = shifted(through, axis, step * stride)
        before = before + arrived
        step *= 2
        if step < count:
            through = through + arrived
    return before


def paired_steps(totals, axis):
    count = lax.axis_size(axis)
    half = totals.shape[0] // 2
    is_low = lax.axis_index(axis) % 2 == 0
    first, second = totals[:half], totals[half:]
    mine = jnp.where(is_low, first, second)
    swap = [(i, i ^ 1) for i in range(count)]
    got = yield jnp.where(is_low, second, first), swap
    pair_total = mine + got
    pairs = count // 2
    before = from_below((yield pair_total, shift_pairs(count, 2)), axis, 2)
    through = pair_total + before
    step = 2
    while step < pairs:
        arrived = from_below((yield through, shift_pairs(count, 2 * step)), axis, 2 * step)
        before = before + arrived
        step *= 2
        if step < pairs:
            through = through + arrived
    back = yield jnp.where(is_low, before + mine, before), swap
    return jnp.where(
        is_low, jnp.concatenate([before, back]), jnp.concatenate([back, before + got])
    )


def shift_pairs(count, shift):
    return [(i, (i + shift) % count) for i in range(count)]


def from_below(arrived, axis, shift):
    return jnp.where(lax.axis_index(axis) >= shift, arrived, jnp.zeros_like(arrived))


def pipelined_scan(totals_of, emit, lines, axis, riders, groups=2):
    count = lax.axis_size(axis)
    if count % 2 or count <= 2 or lines % (2 * groups):
        earlier = exclusive_scan(totals_of(0, lines, None), axis)
        return [emit(0, lines, earlier)], {stage: rider(None) for stage, rider in riders.items()}
    size = lines // groups
    steps = [None] * groups
    steps[0] = paired_steps(totals_of(0, size, None), axis)
    live, made, carried, stage = {}, [], {}, 0
    while stage < groups or live:
        if stage < groups:
            live[stage] = next(steps[stage])
        arrived = {g: lax.ppermute(payload, axis, pairs) for g, (payload, pairs) in live.items()}
        if stage == 0:
            for g in range(1, groups):
                steps[g] = paired_steps(totals_of(g * size, size, live[0][0]), axis)
        tied = (arrived, made)
        if stage in riders:
            tied, carried[stage] = lax.optimization_barrier((tied, riders[stage](live[0][0])))
        else:
            tied = lax.optimization_barrier(tied)
        arrived, made = tied
        following = {}
        for g, value in arrived.items():
            try:
                following[g] = steps[g].send(value)
            except StopIteration as finished:
                made = made + [emit(g * size, size, finished.value)]
        live = following
        stage += 1
    return made, carried


def window(source, step_beam, step_cross, step_depth):
    return source[
        ...,
        1 + step_beam : source.shape[-3] - 1 + step_beam,
        1 + step_cross : source.shape[-2] - 1 + step_cross,
        1 + step_depth : source.shape[-1] - 1 + step_depth,
    ]


def advance(
    bordered, rubidium_number_amount, spin_ratio, heating, drift_speed, fluid_occupied_sites
):
    center = window(bordered, 0, 0, 0)
    complete_heat_ratio = bordered[1] + boundary_kelvin
    coefficients = jnp.stack(
        [xenon_diffusion * complete_heat_ratio**1.5, conduction * complete_heat_ratio**0.7]
    )
    coeff_center = window(coefficients, 0, 0, 0)
    diffused = jnp.zeros_like(center)
    for step_beam, step_cross, step_depth in neighbor_offsets:
        neighbor = window(bordered, step_beam, step_cross, step_depth)
        face_coeff = 0.5 * (coeff_center + window(coefficients, step_beam, step_cross, step_depth))
        diffused = diffused + face_coeff * (neighbor - center)
    upstream = window(bordered, -1, 0, 0)
    transport = diffused - drift_speed * (center - upstream)
    xenon_new = (
        center[0]
        + transport[0]
        + exchange_rate * rubidium_number_amount * (spin_ratio - center[0])
        - xenon_relax * center[0]
    )
    deviation = center[1] + transport[1] + heat_gain * heating - cooling * center[1]
    return jnp.stack([xenon_new * fluid_occupied_sites, deviation * fluid_occupied_sites])


def local(
    xenon_spin_polarization,
    heat_ratio,
    rubidium_polarization_old,
    earlier_spectral_power,
    entry_spectral_power,
    spectral_attenuation_section,
    flow_rate_forward,
    solid_pillar_flags,
):
    rows = earlier_spectral_power.shape[1]
    total_rows = rows * lax.axis_size("beam")
    physical_quantities = jnp.stack([xenon_spin_polarization, heat_ratio - boundary_kelvin])
    glass_cells = solid_pillar_flags.astype(jnp.float32)[:, :, None]
    fluid_occupied_sites = 1.0 - glass_cells
    rubidium_number_amount = fluid_occupied_sites * jnp.exp(
        rubidium_amount_slope * (rubidium_amount_center - 1.0 / heat_ratio)
    )
    absorber = (
        absorb_scale / total_rows * rubidium_number_amount * (1.0 - rubidium_polarization_old)
    )
    glass_term = glass_depth * glass_cells

    def depth_of(start, size):
        weight = spectral_attenuation_section[start : start + size, None, None, None] / (
            1.0 + earlier_spectral_power[start : start + size].astype(jnp.float32) / saturation
        )
        return absorber[None] * weight + glass_term[None], weight

    def totals_of(start, size, after):
        optical_depth, _ = depth_of(start, size)
        if after is not None:
            optical_depth, _ = lax.optimization_barrier((optical_depth, after))
        return jnp.sum(optical_depth, axis=1)

    def emit(start, size, earlier):
        optical_depth, weight = depth_of(start, size)
        local_column = jnp.pad(
            jnp.cumsum(optical_depth[:, : rows - 1], axis=1), ((0, 0), (1, 0), (0, 0), (0, 0))
        )
        column = earlier[:, None] + local_column
        radiance = entry_spectral_power[start : start + size, None] * jnp.exp(-column)
        return (
            radiance.astype(jnp.bfloat16),
            jnp.sum(weight * radiance, axis=0),
            jnp.sum(radiance * (1.0 - jnp.exp(-optical_depth)), axis=0),
        )

    def tied_faces(faces):
        def exchange(after):
            fields = physical_quantities
            if after is not None:
                fields, _ = lax.optimization_barrier((fields, after))
            return faces(fields)

        return exchange

    lines = earlier_spectral_power.shape[0]
    made, first_faces = pipelined_scan(
        totals_of, emit, lines, "beam", {2: tied_faces(cross_faces), 3: tied_faces(beam_faces)}
    )
    first_bordered = bordered_fields(physical_quantities, first_faces[3], first_faces[2])
    spectral_power = jnp.zeros(earlier_spectral_power.shape, jnp.bfloat16)
    start = 0
    for part, _, _ in made:
        spectral_power = lax.dynamic_update_slice_in_dim(spectral_power, part, start, axis=0)
        start += part.shape[0]
    pumping = made[0][1]
    heating = made[0][2]
    for _, part_pumping, part_heating in made[1:]:
        pumping = pumping + part_pumping
        heating = heating + part_heating
    pumping = pump_scale * pumping
    spin_ratio = pumping / (pumping + spin_decay * (1.0 + rubidium_number_amount))
    rubidium_polarization_new = fluid_occupied_sites * spin_ratio
    drift_speed = flow_scale * flow_rate_forward
    for substep in range(SUBSTEPS):
        bordered = first_bordered if substep == 0 else bordered_fields(physical_quantities)
        physical_quantities = advance(
            bordered, rubidium_number_amount, spin_ratio, heating, drift_speed, fluid_occupied_sites
        )
    return (
        spectral_power,
        physical_quantities[0],
        physical_quantities[1] + boundary_kelvin,
        rubidium_polarization_new,
    )


def solution(mesh):
    in_specs = (
        P("beam", "cross", None),
        P("beam", "cross", None),
        P("beam", "cross", None),
        P(None, "beam", "cross", None),
        P(None, "cross", None),
        P(),
        P("cross", None),
        P("beam", "cross"),
    )
    out_specs = (
        P(None, "beam", "cross", None),
        P("beam", "cross", None),
        P("beam", "cross", None),
        P("beam", "cross", None),
    )
    return jax.shard_map(local, mesh=mesh, in_specs=in_specs, out_specs=out_specs, check_vma=False)
```

```python
import jax
import jax.numpy as jnp
from jax import lax
from jax.sharding import PartitionSpec as P

SUBSTEPS = 2


rubidium_amount_slope = 23.25
rubidium_amount_center = 0.95
absorb_scale = 1.0
glass_depth = 0.07
saturation = 1.0
pump_scale = 0.015625
spin_decay = 0.5
exchange_rate = 0.05
xenon_relax = 0.02
heat_gain = 0.05
cooling = 0.02
xenon_diffusion = 0.09
conduction = 0.09
flow_scale = 0.2
boundary_kelvin = 1.0
neighbor_offsets = ((1, 0, 0), (-1, 0, 0), (0, 1, 0), (0, -1, 0), (0, 0, 1), (0, 0, -1))


def shifted(block, axis, shift):
    count = lax.axis_size(axis)
    if shift > 0:
        pairs = [(i, i + shift) for i in range(count - shift)]
    else:
        pairs = [(i - shift, i) for i in range(count + shift)]
    return lax.ppermute(block, axis, pairs)


def faces(block, axis, dim):
    size = block.shape[dim]
    last = lax.slice_in_dim(block, size - 1, size, axis=dim)
    first = lax.slice_in_dim(block, 0, 1, axis=dim)
    count = lax.axis_size(axis)
    if count % 2:
        return shifted(last, axis, 1), shifted(first, axis, -1)
    is_even = lax.axis_index(axis) % 2 == 0
    within = lax.ppermute(jnp.where(is_even, last, first), axis, [(i, i ^ 1) for i in range(count)])
    pairs = [(i, i + 1) for i in range(1, count - 1, 2)]
    pairs += [(target, source) for source, target in pairs]
    across = lax.ppermute(jnp.where(is_even, first, last), axis, pairs)
    return jnp.where(is_even, across, within), jnp.where(is_even, within, across)


def beam_faces(block):
    return faces(block, "beam", 1)


def cross_faces(block):
    return faces(block, "cross", 2)


def bordered_fields(block, beam=None, cross=None):
    low_beam, high_beam = beam_faces(block) if beam is None else beam
    low_cross, high_cross = cross_faces(block) if cross is None else cross
    middle = jnp.concatenate([low_cross, block, high_cross], axis=2)
    zeros = jnp.zeros_like(low_beam[:, :, :1])
    low_beam = jnp.concatenate([zeros, low_beam, zeros], axis=2)
    high_beam = jnp.concatenate([zeros, high_beam, zeros], axis=2)
    bordered = jnp.concatenate([low_beam, middle, high_beam], axis=1)
    return jnp.pad(bordered, ((0, 0), (0, 0), (0, 0), (1, 1)))


def exclusive_scan(totals, axis, stride=1):
    count = lax.axis_size(axis) // stride
    if count == 1:
        return jnp.zeros_like(totals)
    before = shifted(totals, axis, stride)
    through = totals + before
    step = 2
    while step < count:
        arrived = shifted(through, axis, step * stride)
        before = before + arrived
        step *= 2
        if step < count:
            through = through + arrived
    return before


def paired_steps(totals, axis):
    count = lax.axis_size(axis)
    half = totals.shape[0] // 2
    is_low = lax.axis_index(axis) % 2 == 0
    first, second = totals[:half], totals[half:]
    mine = jnp.where(is_low, first, second)
    swap = [(i, i ^ 1) for i in range(count)]
    got = yield jnp.where(is_low, second, first), swap
    pair_total = mine + got
    pairs = count // 2
    before = yield pair_total, shift_pairs(count, 2)
    through = pair_total + before
    step = 2
    while step < pairs:
        arrived = yield through, shift_pairs(count, 2 * step)
        before = before + arrived
        step *= 2
        if step < pairs:
            through = through + arrived
    back = yield jnp.where(is_low, before + mine, before), swap
    return jnp.where(
        is_low, jnp.concatenate([before, back]), jnp.concatenate([back, before + got])
    )


def shift_pairs(count, shift):
    return [(i, i + shift) for i in range(count - shift)]


def pipelined_scan(totals_of, emit, lines, axis, riders, groups=2):
    count = lax.axis_size(axis)
    if count % 2 or count <= 2 or lines % (2 * groups):
        earlier = exclusive_scan(totals_of(0, lines, None), axis)
        return [emit(0, lines, earlier)], {stage: rider(None) for stage, rider in riders.items()}
    size = lines // groups
    steps = [None] * groups
    steps[0] = paired_steps(totals_of(0, size, None), axis)
    live, made, carried, stage = {}, [], {}, 0
    while stage < groups or live:
        if stage < groups:
            live[stage] = next(steps[stage])
        arrived = {g: lax.ppermute(payload, axis, pairs) for g, (payload, pairs) in live.items()}
        if stage == 0:
            for g in range(1, groups):
                steps[g] = paired_steps(totals_of(g * size, size, live[0][0]), axis)
        tied = (arrived, made)
        if stage in riders:
            tied, carried[stage] = lax.optimization_barrier((tied, riders[stage](live[0][0])))
        else:
            tied = lax.optimization_barrier(tied)
        arrived, made = tied
        following = {}
        for g, value in arrived.items():
            try:
                following[g] = steps[g].send(value)
            except StopIteration as finished:
                made = made + [emit(g * size, size, finished.value)]
        live = following
        stage += 1
    return made, carried


def window(source, step_beam, step_cross, step_depth):
    return source[
        ...,
        1 + step_beam : source.shape[-3] - 1 + step_beam,
        1 + step_cross : source.shape[-2] - 1 + step_cross,
        1 + step_depth : source.shape[-1] - 1 + step_depth,
    ]


def advance(
    bordered, rubidium_number_amount, spin_ratio, heating, drift_speed, fluid_occupied_sites
):
    center = window(bordered, 0, 0, 0)
    complete_heat_ratio = bordered[1] + boundary_kelvin
    coefficients = jnp.stack(
        [xenon_diffusion * complete_heat_ratio**1.5, conduction * complete_heat_ratio**0.7]
    )
    coeff_center = window(coefficients, 0, 0, 0)
    diffused = jnp.zeros_like(center)
    for step_beam, step_cross, step_depth in neighbor_offsets:
        neighbor = window(bordered, step_beam, step_cross, step_depth)
        face_coeff = 0.5 * (coeff_center + window(coefficients, step_beam, step_cross, step_depth))
        diffused = diffused + face_coeff * (neighbor - center)
    upstream = window(bordered, -1, 0, 0)
    transport = diffused - drift_speed * (center - upstream)
    xenon_new = (
        center[0]
        + transport[0]
        + exchange_rate * rubidium_number_amount * (spin_ratio - center[0])
        - xenon_relax * center[0]
    )
    deviation = center[1] + transport[1] + heat_gain * heating - cooling * center[1]
    return jnp.stack([xenon_new * fluid_occupied_sites, deviation * fluid_occupied_sites])


def local(
    xenon_spin_polarization,
    heat_ratio,
    rubidium_polarization_old,
    earlier_spectral_power,
    entry_spectral_power,
    spectral_attenuation_section,
    flow_rate_forward,
    solid_pillar_flags,
):
    rows = earlier_spectral_power.shape[1]
    total_rows = rows * lax.axis_size("beam")
    physical_quantities = jnp.stack([xenon_spin_polarization, heat_ratio - boundary_kelvin])
    glass_cells = solid_pillar_flags.astype(jnp.float32)[:, :, None]
    fluid_occupied_sites = 1.0 - glass_cells
    rubidium_number_amount = fluid_occupied_sites * jnp.exp(
        rubidium_amount_slope * (rubidium_amount_center - 1.0 / heat_ratio)
    )
    absorber = (
        absorb_scale / total_rows * rubidium_number_amount * (1.0 - rubidium_polarization_old)
    )
    glass_term = glass_depth * glass_cells

    def depth_of(start, size):
        weight = spectral_attenuation_section[start : start + size, None, None, None] / (
            1.0 + earlier_spectral_power[start : start + size].astype(jnp.float32) / saturation
        )
        return absorber[None] * weight + glass_term[None], weight

    def totals_of(start, size, after):
        optical_depth, _ = depth_of(start, size)
        if after is not None:
            optical_depth, _ = lax.optimization_barrier((optical_depth, after))
        return jnp.sum(optical_depth, axis=1)

    def emit(start, size, earlier):
        optical_depth, weight = depth_of(start, size)
        local_column = jnp.pad(
            jnp.cumsum(optical_depth[:, : rows - 1], axis=1), ((0, 0), (1, 0), (0, 0), (0, 0))
        )
        column = earlier[:, None] + local_column
        radiance = entry_spectral_power[start : start + size, None] * jnp.exp(-column)
        return (
            radiance.astype(jnp.bfloat16),
            jnp.sum(weight * radiance, axis=0),
            jnp.sum(radiance * (1.0 - jnp.exp(-optical_depth)), axis=0),
        )

    def tied_faces(faces):
        def exchange(after):
            fields = physical_quantities
            if after is not None:
                fields, _ = lax.optimization_barrier((fields, after))
            return faces(fields)

        return exchange

    lines = earlier_spectral_power.shape[0]
    made, first_faces = pipelined_scan(
        totals_of, emit, lines, "beam", {2: tied_faces(beam_faces), 3: tied_faces(cross_faces)}
    )
    first_bordered = bordered_fields(physical_quantities, first_faces[2], first_faces[3])
    spectral_power = jnp.zeros(earlier_spectral_power.shape, jnp.bfloat16)
    start = 0
    for part, _, _ in made:
        spectral_power = lax.dynamic_update_slice_in_dim(spectral_power, part, start, axis=0)
        start += part.shape[0]
    pumping = made[0][1]
    heating = made[0][2]
    for _, part_pumping, part_heating in made[1:]:
        pumping = pumping + part_pumping
        heating = heating + part_heating
    pumping = pump_scale * pumping
    spin_ratio = pumping / (pumping + spin_decay * (1.0 + rubidium_number_amount))
    rubidium_polarization_new = fluid_occupied_sites * spin_ratio
    drift_speed = flow_scale * flow_rate_forward
    for substep in range(SUBSTEPS):
        bordered = first_bordered if substep == 0 else bordered_fields(physical_quantities)
        physical_quantities = advance(
            bordered, rubidium_number_amount, spin_ratio, heating, drift_speed, fluid_occupied_sites
        )
    return (
        spectral_power,
        physical_quantities[0],
        physical_quantities[1] + boundary_kelvin,
        rubidium_polarization_new,
    )


def solution(mesh):
    in_specs = (
        P("beam", "cross", None),
        P("beam", "cross", None),
        P("beam", "cross", None),
        P(None, "beam", "cross", None),
        P(None, "cross", None),
        P(),
        P("cross", None),
        P("beam", "cross"),
    )
    out_specs = (
        P(None, "beam", "cross", None),
        P("beam", "cross", None),
        P("beam", "cross", None),
        P("beam", "cross", None),
    )
    return jax.shard_map(local, mesh=mesh, in_specs=in_specs, out_specs=out_specs, check_vma=False)
```

```python
import jax
import jax.numpy as jnp
from jax import lax
from jax.sharding import PartitionSpec as P

SUBSTEPS = 2


rubidium_amount_slope = 23.25
rubidium_amount_center = 0.95
absorb_scale = 1.0
glass_depth = 0.07
saturation = 1.0
pump_scale = 0.015625
spin_decay = 0.5
exchange_rate = 0.05
xenon_relax = 0.02
heat_gain = 0.05
cooling = 0.02
xenon_diffusion = 0.09
conduction = 0.09
flow_scale = 0.2
boundary_kelvin = 1.0
neighbor_offsets = ((1, 0, 0), (-1, 0, 0), (0, 1, 0), (0, -1, 0), (0, 0, 1), (0, 0, -1))


def shifted(block, axis, shift):
    count = lax.axis_size(axis)
    if shift > 0:
        pairs = [(i, i + shift) for i in range(count - shift)]
    else:
        pairs = [(i - shift, i) for i in range(count + shift)]
    return lax.ppermute(block, axis, pairs)


def faces(block, axis, dim):
    size = block.shape[dim]
    last = lax.slice_in_dim(block, size - 1, size, axis=dim)
    first = lax.slice_in_dim(block, 0, 1, axis=dim)
    count = lax.axis_size(axis)
    if count % 2:
        return shifted(last, axis, 1), shifted(first, axis, -1)
    is_even = lax.axis_index(axis) % 2 == 0
    within = lax.ppermute(jnp.where(is_even, last, first), axis, [(i, i ^ 1) for i in range(count)])
    pairs = [(i, i + 1) for i in range(1, count - 1, 2)]
    pairs += [(target, source) for source, target in pairs]
    across = lax.ppermute(jnp.where(is_even, first, last), axis, pairs)
    return jnp.where(is_even, across, within), jnp.where(is_even, within, across)


def beam_faces(block):
    return faces(block, "beam", 1)


def cross_faces(block):
    return faces(block, "cross", 2)


def bordered_fields(block, beam=None, cross=None):
    low_beam, high_beam = beam_faces(block) if beam is None else beam
    low_cross, high_cross = cross_faces(block) if cross is None else cross
    middle = jnp.concatenate([low_cross, block, high_cross], axis=2)
    zeros = jnp.zeros_like(low_beam[:, :, :1])
    low_beam = jnp.concatenate([zeros, low_beam, zeros], axis=2)
    high_beam = jnp.concatenate([zeros, high_beam, zeros], axis=2)
    bordered = jnp.concatenate([low_beam, middle, high_beam], axis=1)
    return jnp.pad(bordered, ((0, 0), (0, 0), (0, 0), (1, 1)))


def exclusive_scan(totals, axis, stride=1):
    count = lax.axis_size(axis) // stride
    if count == 1:
        return jnp.zeros_like(totals)
    before = shifted(totals, axis, stride)
    through = totals + before
    step = 2
    while step < count:
        arrived = shifted(through, axis, step * stride)
        before = before + arrived
        step *= 2
        if step < count:
            through = through + arrived
    return before


def paired_steps(totals, axis):
    count = lax.axis_size(axis)
    half = totals.shape[0] // 2
    is_low = lax.axis_index(axis) % 2 == 0
    first, second = totals[:half], totals[half:]
    mine = jnp.where(is_low, first, second)
    swap = [(i, i ^ 1) for i in range(count)]
    got = yield jnp.where(is_low, second, first), swap
    pair_total = mine + got
    pairs = count // 2
    before = yield pair_total, shift_pairs(count, 2)
    through = pair_total + before
    step = 2
    while step < pairs:
        arrived = yield through, shift_pairs(count, 2 * step)
        before = before + arrived
        step *= 2
        if step < pairs:
            through = through + arrived
    back = yield jnp.where(is_low, before + mine, before), swap
    return jnp.where(
        is_low, jnp.concatenate([before, back]), jnp.concatenate([back, before + got])
    )


def shift_pairs(count, shift):
    return [(i, i + shift) for i in range(count - shift)]


def pipelined_scan(totals_of, emit, lines, axis, riders, passenger, groups=2):
    count = lax.axis_size(axis)
    if count % 2 or count <= 2 or lines % (2 * groups):
        earlier = exclusive_scan(totals_of(0, lines, None), axis)
        carried = {stage: rider(None) for stage, rider in riders.items()}
        return [emit(0, lines, earlier)], carried, None
    size = lines // groups
    steps = [None] * groups
    steps[0] = paired_steps(totals_of(0, size, None), axis)
    live, made, carried, stage = {}, [], {}, 0
    while stage < groups or live:
        if stage < groups:
            live[stage] = next(steps[stage])
        sent = dict(live)
        if stage == 0:
            payload, pairs = live[0]
            sent[0] = jnp.concatenate([payload, passenger.reshape((-1,) + payload.shape[1:])]), pairs
        arrived = {g: lax.ppermute(payload, axis, pairs) for g, (payload, pairs) in sent.items()}
        if stage == 0:
            held = live[0][0].shape[0]
            passenger = arrived[0][held:].reshape(passenger.shape)
            arrived[0] = arrived[0][:held]
        if stage == 0:
            for g in range(1, groups):
                steps[g] = paired_steps(totals_of(g * size, size, live[0][0]), axis)
        tied = (arrived, made)
        if stage in riders:
            tied, carried[stage] = lax.optimization_barrier((tied, riders[stage](live[0][0])))
        else:
            tied = lax.optimization_barrier(tied)
        arrived, made = tied
        following = {}
        for g, value in arrived.items():
            try:
                following[g] = steps[g].send(value)
            except StopIteration as finished:
                made = made + [emit(g * size, size, finished.value)]
        live = following
        stage += 1
    return made, carried, passenger


def window(source, step_beam, step_cross, step_depth):
    return source[
        ...,
        1 + step_beam : source.shape[-3] - 1 + step_beam,
        1 + step_cross : source.shape[-2] - 1 + step_cross,
        1 + step_depth : source.shape[-1] - 1 + step_depth,
    ]


def advance(
    bordered, rubidium_number_amount, spin_ratio, heating, drift_speed, fluid_occupied_sites
):
    center = window(bordered, 0, 0, 0)
    complete_heat_ratio = bordered[1] + boundary_kelvin
    coefficients = jnp.stack(
        [xenon_diffusion * complete_heat_ratio**1.5, conduction * complete_heat_ratio**0.7]
    )
    coeff_center = window(coefficients, 0, 0, 0)
    diffused = jnp.zeros_like(center)
    for step_beam, step_cross, step_depth in neighbor_offsets:
        neighbor = window(bordered, step_beam, step_cross, step_depth)
        face_coeff = 0.5 * (coeff_center + window(coefficients, step_beam, step_cross, step_depth))
        diffused = diffused + face_coeff * (neighbor - center)
    upstream = window(bordered, -1, 0, 0)
    transport = diffused - drift_speed * (center - upstream)
    xenon_new = (
        center[0]
        + transport[0]
        + exchange_rate * rubidium_number_amount * (spin_ratio - center[0])
        - xenon_relax * center[0]
    )
    deviation = center[1] + transport[1] + heat_gain * heating - cooling * center[1]
    return jnp.stack([xenon_new * fluid_occupied_sites, deviation * fluid_occupied_sites])


def local(
    xenon_spin_polarization,
    heat_ratio,
    rubidium_polarization_old,
    earlier_spectral_power,
    entry_spectral_power,
    spectral_attenuation_section,
    flow_rate_forward,
    solid_pillar_flags,
):
    rows = earlier_spectral_power.shape[1]
    total_rows = rows * lax.axis_size("beam")
    physical_quantities = jnp.stack([xenon_spin_polarization, heat_ratio - boundary_kelvin])
    glass_cells = solid_pillar_flags.astype(jnp.float32)[:, :, None]
    fluid_occupied_sites = 1.0 - glass_cells
    rubidium_number_amount = fluid_occupied_sites * jnp.exp(
        rubidium_amount_slope * (rubidium_amount_center - 1.0 / heat_ratio)
    )
    absorber = (
        absorb_scale / total_rows * rubidium_number_amount * (1.0 - rubidium_polarization_old)
    )
    glass_term = glass_depth * glass_cells

    def depth_of(start, size):
        weight = spectral_attenuation_section[start : start + size, None, None, None] / (
            1.0 + earlier_spectral_power[start : start + size].astype(jnp.float32) / saturation
        )
        return absorber[None] * weight + glass_term[None], weight

    def totals_of(start, size, after):
        optical_depth, _ = depth_of(start, size)
        if after is not None:
            optical_depth, _ = lax.optimization_barrier((optical_depth, after))
        return jnp.sum(optical_depth, axis=1)

    def emit(start, size, earlier):
        optical_depth, weight = depth_of(start, size)
        local_column = jnp.pad(
            jnp.cumsum(optical_depth[:, : rows - 1], axis=1), ((0, 0), (1, 0), (0, 0), (0, 0))
        )
        column = earlier[:, None] + local_column
        radiance = entry_spectral_power[start : start + size, None] * jnp.exp(-column)
        return (
            radiance.astype(jnp.bfloat16),
            jnp.sum(weight * radiance, axis=0),
            jnp.sum(radiance * (1.0 - jnp.exp(-optical_depth)), axis=0),
        )

    def tied_faces(faces):
        def exchange(after):
            fields = physical_quantities
            if after is not None:
                fields, _ = lax.optimization_barrier((fields, after))
            return faces(fields)

        return exchange

    lines = earlier_spectral_power.shape[0]
    count = lax.axis_size("beam")
    is_even = lax.axis_index("beam") % 2 == 0
    last, first = physical_quantities[:, rows - 1 :], physical_quantities[:, :1]

    def across_pairs(fields):
        pairs = [(i, i + 1) for i in range(1, count - 1, 2)]
        pairs += [(target, source) for source, target in pairs]
        size = fields.shape[1]
        return lax.ppermute(jnp.where(is_even, fields[:, :1], fields[:, size - 1 :]), "beam", pairs)

    paired = count % 2 == 0 and count > 2 and lines % 4 == 0
    made, first_faces, within = pipelined_scan(
        totals_of,
        emit,
        lines,
        "beam",
        {2: tied_faces(cross_faces), 3: tied_faces(across_pairs if paired else beam_faces)},
        jnp.where(is_even, last, first),
    )
    if paired:
        across = first_faces[3]
        beam = (jnp.where(is_even, across, within), jnp.where(is_even, within, across))
    else:
        beam = first_faces[3]
    first_bordered = bordered_fields(physical_quantities, beam, first_faces[2])
    spectral_power = jnp.zeros(earlier_spectral_power.shape, jnp.bfloat16)
    start = 0
    for part, _, _ in made:
        spectral_power = lax.dynamic_update_slice_in_dim(spectral_power, part, start, axis=0)
        start += part.shape[0]
    pumping = made[0][1]
    heating = made[0][2]
    for _, part_pumping, part_heating in made[1:]:
        pumping = pumping + part_pumping
        heating = heating + part_heating
    pumping = pump_scale * pumping
    spin_ratio = pumping / (pumping + spin_decay * (1.0 + rubidium_number_amount))
    rubidium_polarization_new = fluid_occupied_sites * spin_ratio
    drift_speed = flow_scale * flow_rate_forward
    for substep in range(SUBSTEPS):
        bordered = first_bordered if substep == 0 else bordered_fields(physical_quantities)
        physical_quantities = advance(
            bordered, rubidium_number_amount, spin_ratio, heating, drift_speed, fluid_occupied_sites
        )
    return (
        spectral_power,
        physical_quantities[0],
        physical_quantities[1] + boundary_kelvin,
        rubidium_polarization_new,
    )


def solution(mesh):
    in_specs = (
        P("beam", "cross", None),
        P("beam", "cross", None),
        P("beam", "cross", None),
        P(None, "beam", "cross", None),
        P(None, "cross", None),
        P(),
        P("cross", None),
        P("beam", "cross"),
    )
    out_specs = (
        P(None, "beam", "cross", None),
        P("beam", "cross", None),
        P("beam", "cross", None),
        P("beam", "cross", None),
    )
    return jax.shard_map(local, mesh=mesh, in_specs=in_specs, out_specs=out_specs, check_vma=False)
```

```python
import jax
import jax.numpy as jnp
from jax import lax
from jax.sharding import PartitionSpec as P

SUBSTEPS = 2


rubidium_amount_slope = 23.25
rubidium_amount_center = 0.95
absorb_scale = 1.0
glass_depth = 0.07
saturation = 1.0
pump_scale = 0.015625
spin_decay = 0.5
exchange_rate = 0.05
xenon_relax = 0.02
heat_gain = 0.05
cooling = 0.02
xenon_diffusion = 0.09
conduction = 0.09
flow_scale = 0.2
boundary_kelvin = 1.0
neighbor_offsets = ((1, 0, 0), (-1, 0, 0), (0, 1, 0), (0, -1, 0), (0, 0, 1), (0, 0, -1))


def shifted(block, axis, shift):
    count = lax.axis_size(axis)
    if shift > 0:
        pairs = [(i, i + shift) for i in range(count - shift)]
    else:
        pairs = [(i - shift, i) for i in range(count + shift)]
    return lax.ppermute(block, axis, pairs)


def faces(block, axis, dim):
    size = block.shape[dim]
    last = lax.slice_in_dim(block, size - 1, size, axis=dim)
    first = lax.slice_in_dim(block, 0, 1, axis=dim)
    count = lax.axis_size(axis)
    if count % 2:
        return shifted(last, axis, 1), shifted(first, axis, -1)
    is_even = lax.axis_index(axis) % 2 == 0
    within = lax.ppermute(jnp.where(is_even, last, first), axis, [(i, i ^ 1) for i in range(count)])
    pairs = [(i, i + 1) for i in range(1, count - 1, 2)]
    pairs += [(target, source) for source, target in pairs]
    across = lax.ppermute(jnp.where(is_even, first, last), axis, pairs)
    return jnp.where(is_even, across, within), jnp.where(is_even, within, across)


def beam_faces(block):
    return faces(block, "beam", 1)


def cross_faces(block):
    return faces(block, "cross", 2)


def bordered_fields(block, beam=None, cross=None):
    low_beam, high_beam = beam_faces(block) if beam is None else beam
    low_cross, high_cross = cross_faces(block) if cross is None else cross
    middle = jnp.concatenate([low_cross, block, high_cross], axis=2)
    zeros = jnp.zeros_like(low_beam[:, :, :1])
    low_beam = jnp.concatenate([zeros, low_beam, zeros], axis=2)
    high_beam = jnp.concatenate([zeros, high_beam, zeros], axis=2)
    bordered = jnp.concatenate([low_beam, middle, high_beam], axis=1)
    return jnp.pad(bordered, ((0, 0), (0, 0), (0, 0), (1, 1)))


def exclusive_scan(totals, axis, stride=1):
    count = lax.axis_size(axis) // stride
    if count == 1:
        return jnp.zeros_like(totals)
    before = shifted(totals, axis, stride)
    through = totals + before
    step = 2
    while step < count:
        arrived = shifted(through, axis, step * stride)
        before = before + arrived
        step *= 2
        if step < count:
            through = through + arrived
    return before


def paired_steps(totals, axis):
    count = lax.axis_size(axis)
    half = totals.shape[0] // 2
    is_low = lax.axis_index(axis) % 2 == 0
    first, second = totals[:half], totals[half:]
    mine = jnp.where(is_low, first, second)
    swap = [(i, i ^ 1) for i in range(count)]
    got = yield jnp.where(is_low, second, first), swap
    pair_total = mine + got
    pairs = count // 2
    before = yield pair_total, shift_pairs(count, 2)
    through = pair_total + before
    step = 2
    while step < pairs:
        arrived = yield through, shift_pairs(count, 2 * step)
        before = before + arrived
        step *= 2
        if step < pairs:
            through = through + arrived
    back = yield jnp.where(is_low, before + mine, before), swap
    return jnp.where(
        is_low, jnp.concatenate([before, back]), jnp.concatenate([back, before + got])
    )


def shift_pairs(count, shift):
    return [(i, i + shift) for i in range(count - shift)]


def pipelined_scan(totals_of, emit, lines, axis, riders, groups=2):
    count = lax.axis_size(axis)
    if count % 2 or count <= 2 or lines % (2 * groups):
        earlier = exclusive_scan(totals_of(0, lines, None), axis)
        return [emit(0, lines, earlier)], {stage: rider(None) for stage, rider in riders.items()}
    size = lines // groups
    steps = [None] * groups
    steps[0] = paired_steps(totals_of(0, size, None), axis)
    live, made, carried, stage = {}, [], {}, 0
    while stage < groups or live:
        if stage < groups:
            live[stage] = next(steps[stage])
        arrived = {g: lax.ppermute(payload, axis, pairs) for g, (payload, pairs) in live.items()}
        if stage == 0:
            for g in range(1, groups):
                steps[g] = paired_steps(totals_of(g * size, size, live[0][0]), axis)
        tied = (arrived, made)
        if stage in riders:
            tied, carried[stage] = lax.optimization_barrier((tied, riders[stage](live[0][0])))
        else:
            tied = lax.optimization_barrier(tied)
        arrived, made = tied
        following = {}
        for g, value in arrived.items():
            try:
                following[g] = steps[g].send(value)
            except StopIteration as finished:
                made = made + [emit(g * size, size, finished.value)]
        live = following
        stage += 1
    return made, carried


def window(source, step_beam, step_cross, step_depth):
    return source[
        ...,
        1 + step_beam : source.shape[-3] - 1 + step_beam,
        1 + step_cross : source.shape[-2] - 1 + step_cross,
        1 + step_depth : source.shape[-1] - 1 + step_depth,
    ]


def advance(
    bordered, rubidium_number_amount, spin_ratio, heating, drift_speed, fluid_occupied_sites
):
    center = window(bordered, 0, 0, 0)
    complete_heat_ratio = bordered[1] + boundary_kelvin
    coefficients = jnp.stack(
        [xenon_diffusion * complete_heat_ratio**1.5, conduction * complete_heat_ratio**0.7]
    )
    coeff_center = window(coefficients, 0, 0, 0)
    diffused = jnp.zeros_like(center)
    for step_beam, step_cross, step_depth in neighbor_offsets:
        neighbor = window(bordered, step_beam, step_cross, step_depth)
        face_coeff = 0.5 * (coeff_center + window(coefficients, step_beam, step_cross, step_depth))
        diffused = diffused + face_coeff * (neighbor - center)
    upstream = window(bordered, -1, 0, 0)
    transport = diffused - drift_speed * (center - upstream)
    xenon_new = (
        center[0]
        + transport[0]
        + exchange_rate * rubidium_number_amount * (spin_ratio - center[0])
        - xenon_relax * center[0]
    )
    deviation = center[1] + transport[1] + heat_gain * heating - cooling * center[1]
    return jnp.stack([xenon_new * fluid_occupied_sites, deviation * fluid_occupied_sites])


def local(
    xenon_spin_polarization,
    heat_ratio,
    rubidium_polarization_old,
    earlier_spectral_power,
    entry_spectral_power,
    spectral_attenuation_section,
    flow_rate_forward,
    solid_pillar_flags,
):
    rows = earlier_spectral_power.shape[1]
    total_rows = rows * lax.axis_size("beam")
    physical_quantities = jnp.stack([xenon_spin_polarization, heat_ratio - boundary_kelvin])
    glass_cells = solid_pillar_flags.astype(jnp.float32)[:, :, None]
    fluid_occupied_sites = 1.0 - glass_cells
    rubidium_number_amount = fluid_occupied_sites * jnp.exp(
        rubidium_amount_slope * (rubidium_amount_center - 1.0 / heat_ratio)
    )
    absorber = (
        absorb_scale / total_rows * rubidium_number_amount * (1.0 - rubidium_polarization_old)
    )
    glass_term = glass_depth * glass_cells

    def depth_of(start, size):
        weight = spectral_attenuation_section[start : start + size, None, None, None] / (
            1.0 + earlier_spectral_power[start : start + size].astype(jnp.float32) / saturation
        )
        return absorber[None] * weight + glass_term[None], weight

    def totals_of(start, size, after):
        optical_depth, _ = depth_of(start, size)
        if after is not None:
            optical_depth, _ = lax.optimization_barrier((optical_depth, after))
        return jnp.sum(optical_depth, axis=1)

    def emit(start, size, earlier):
        optical_depth, weight = depth_of(start, size)
        local_column = jnp.pad(
            jnp.cumsum(optical_depth[:, : rows - 1], axis=1), ((0, 0), (1, 0), (0, 0), (0, 0))
        )
        column = earlier[:, None] + local_column
        radiance = entry_spectral_power[start : start + size, None] * jnp.exp(-column)
        return (
            radiance.astype(jnp.bfloat16),
            jnp.sum(weight * radiance, axis=0),
            jnp.sum(radiance * (1.0 - jnp.exp(-optical_depth)), axis=0),
        )

    def tied_faces(faces):
        def exchange(after):
            fields = physical_quantities
            if after is not None:
                fields, _ = lax.optimization_barrier((fields, after))
            return faces(fields)

        return exchange

    lines = earlier_spectral_power.shape[0]
    made, first_faces = pipelined_scan(
        totals_of, emit, lines, "beam", {1: tied_faces(cross_faces), 3: tied_faces(beam_faces)}
    )
    first_bordered = bordered_fields(physical_quantities, first_faces[3], first_faces[1])
    spectral_power = jnp.zeros(earlier_spectral_power.shape, jnp.bfloat16)
    start = 0
    for part, _, _ in made:
        spectral_power = lax.dynamic_update_slice_in_dim(spectral_power, part, start, axis=0)
        start += part.shape[0]
    pumping = made[0][1]
    heating = made[0][2]
    for _, part_pumping, part_heating in made[1:]:
        pumping = pumping + part_pumping
        heating = heating + part_heating
    pumping = pump_scale * pumping
    spin_ratio = pumping / (pumping + spin_decay * (1.0 + rubidium_number_amount))
    rubidium_polarization_new = fluid_occupied_sites * spin_ratio
    drift_speed = flow_scale * flow_rate_forward
    for substep in range(SUBSTEPS):
        bordered = first_bordered if substep == 0 else bordered_fields(physical_quantities)
        physical_quantities = advance(
            bordered, rubidium_number_amount, spin_ratio, heating, drift_speed, fluid_occupied_sites
        )
    return (
        spectral_power,
        physical_quantities[0],
        physical_quantities[1] + boundary_kelvin,
        rubidium_polarization_new,
    )


def solution(mesh):
    in_specs = (
        P("beam", "cross", None),
        P("beam", "cross", None),
        P("beam", "cross", None),
        P(None, "beam", "cross", None),
        P(None, "cross", None),
        P(),
        P("cross", None),
        P("beam", "cross"),
    )
    out_specs = (
        P(None, "beam", "cross", None),
        P("beam", "cross", None),
        P("beam", "cross", None),
        P("beam", "cross", None),
    )
    return jax.shard_map(local, mesh=mesh, in_specs=in_specs, out_specs=out_specs, check_vma=False)
```
